32 devices in a mesh: slab: 16 (over z, x, core), energy: 2 (over y).
Axes of the slice: x: 2, y: 2, z: 4, core: 2. Of those that a mesh axis runs over, the one named last changes fastest.
Arguments:
- mode_floor: float32 [1024], replicated, may hold values from -2.5 to 2.5
- onsite_noise: float32 [256, 1024], P('slab'), may hold values from -0.4 to 0.4
- hopping: float32 [256, 1024], P('slab'), may hold values from 2.3 to 2.7
- lengths: int32 [16], replicated, may hold values from 1 to 16, 128 in all
- energy_index: int32 [8], P('energy'), may hold values from 0 to 4095
- weight_code: int32 [8], P('energy'), may hold values from 1 to 63
- lead_shift: float32 [8, 2, 1024], P('energy'), may hold values from -0.5 to 0.5
- lead_width: float32 [8, 2, 1024], P('energy'), may hold values from 0.2 to 1.2
Outputs:
- density: float32 [256, 1024], P('slab', 'energy')
- bond_density: float32 [256, 1024], P('slab', 'energy')
The draws below stay inside these ranges and needn't reach their ends.
Inputs may be any that keep to these rules, and one draw needn't show every extreme that they name: `lengths`: entry d counts the slabs of index d of slab, which fill its first slots; the entries sum to 128.
All inputs are finite; a program needn't handle non-finite values.
Results may differ from the reference program's by a relative error of at most 0.029.
Values sent between devices are 32-bit elements; how exact they have to be, the bound alone decides.
No kernel may reach another device: no remote copies, remote signals or barrier semaphores. Data moves between devices by JAX's collectives and lax.ppermute only.
A program may use at most 64 MiB of HBM per device.

```python
import math
import jax
import jax.numpy as jnp
import numpy as np
from jax import lax

M = 1024
E_DEV = 4
PMAX = 16
SLABS = 128
SLOTS = 256
NE = 8
N_SLAB = 16
N_ENERGY = 2


def set_ends(result, key, least, top_value):
    shape = result.shape
    spot = [jax.random.randint(jax.random.fold_in(key, axis), (), 0, shape[axis]) for axis in range(len(shape))]
    result = result.at[tuple(spot)].set(least)
    longest = shape.index(max(shape))
    spot[longest] = (spot[longest] + 1) % shape[longest]
    return result.at[tuple(spot)].set(top_value)


def block_levels(key, shape, pieces, low, largest):
    gain, own = 1.0, jax.random.fold_in(key, 6)
    for dim, shards_of in pieces:
        heights = jnp.exp(jax.random.uniform(jax.random.fold_in(own, dim), (shards_of,), jnp.float32, low / len(pieces), largest / len(pieces)))
        gain = gain * jnp.repeat(heights, shape[dim] // shards_of).reshape([-1 if axis == dim else 1 for axis in range(len(shape))])
    return gain


def profile(count, total, reach, slope):
    loads = [(1 << 20) // math.isqrt(grade ** slope) + 1 for grade in range(2, count + 1)]
    rest, given = total - reach - (count - 1), [1] * (count - 1)
    while rest > 0:
        free = [i for i in range(count - 1) if given[i] < reach]
        whole, remaining = sum([loads[i] for i in free]), rest
        for i in free:
            extra = min(reach - given[i], max(1, remaining * loads[i] // whole), rest)
            given[i] = given[i] + extra
            rest = rest - extra
    return np.array([reach] + given)


def uneven(key, count, total, limit, lean):
    if count == 2:
        one = jax.random.randint(key, (), max(1, total - limit), min(limit, total - 1) + 1)
        return jnp.stack([one, total - one])
    tallies = jnp.asarray(profile(count, total, limit, lean), jnp.int32)
    pairs = (count - 1) // 2
    donor, sink = tallies[1:1 + 2 * pairs:2], tallies[2:2 + 2 * pairs:2]
    slack = jnp.minimum(donor - 1, limit - sink)
    passed = jax.random.randint(jax.random.fold_in(key, 1), (pairs,), 0, 1 << 20) % (slack + 1)
    tallies = tallies.at[1:1 + 2 * pairs:2].set(donor - passed).at[2:2 + 2 * pairs:2].set(sink + passed)
    return tallies[jax.random.permutation(jax.random.fold_in(key, 2), count)]


def setup_inputs(seed: int = 0) -> dict:
    keys = jax.random.split(jax.random.key(seed), 9)
    mode_floor = jnp.clip(jax.random.uniform(keys[0], (M,), jnp.float32, -2.5, 2.5), -2.5, 2.5)
    onsite_noise = jnp.clip(jax.random.uniform(keys[1], (SLOTS, M), jnp.float32, -0.4, 0.4) * block_levels(keys[1], (SLOTS, M), ((0, 16),), -0.4, 0.0), -0.4, 0.4)
    hopping = jnp.clip(2.3 + 0.4000001 * jax.random.uniform(keys[2], (SLOTS, M), jnp.float32) ** block_levels(keys[2], (SLOTS, M), ((0, 16),), -0.2, 0.2), 2.3, 2.7)
    lengths = uneven(keys[3], N_SLAB, SLABS, PMAX, 2).astype(jnp.int32)
    energy_index = set_ends(jax.random.randint(keys[4], (NE,), 0, 4096), jax.random.fold_in(keys[4], 1), 0, 4095).astype(jnp.int32)
    weight_code = set_ends(jax.random.randint(keys[5], (NE,), 1, 64), jax.random.fold_in(keys[5], 1), 1, 63).astype(jnp.int32)
    lead_shift = jnp.clip(jax.random.uniform(keys[6], (NE, 2, M), jnp.float32, -0.5, 0.5) * block_levels(keys[6], (NE, 2, M), ((0, 2),), -0.4, 0.0), -0.5, 0.5)
    lead_width = jnp.clip(jnp.exp(math.log(1.2) - 1.7917595 * jax.random.uniform(keys[7], (NE, 2, M), jnp.float32) ** block_levels(keys[7], (NE, 2, M), ((0, 2),), -0.2, 0.2)), 0.2, 1.2)
    return dict(mode_floor=mode_floor, onsite_noise=onsite_noise, hopping=hopping, lengths=lengths, energy_index=energy_index, weight_code=weight_code, lead_shift=lead_shift, lead_width=lead_width)


broaden = 0.002
e_low = -1.5
e_step = 3.0 / 4096.0
inv_pi = 1.0 / 3.141592653589793


def reciprocal(real_part, imag_part):
    norm = real_part * real_part + imag_part * imag_part
    return real_part / norm, -imag_part / norm


def complex_mul(first_re, first_im, second_re, second_im):
    return first_re * second_re - first_im * second_im, first_re * second_im + first_im * second_re


def reference(mode_floor, onsite_noise, hopping, lengths, energy_index, weight_code, lead_shift, lead_width):
    slot = jnp.arange(N_SLAB * PMAX, dtype=jnp.int32)
    owner = slot // PMAX
    place = slot % PMAX
    alive = (place < lengths[owner]).astype(jnp.float32)
    last_slot = (N_SLAB - 1) * PMAX + lengths[N_SLAB - 1] - 1
    first_on = (slot == 0).astype(jnp.float32)[:, None]
    last_on = (slot == last_slot).astype(jnp.float32)[:, None]
    levels = mode_floor[None, :] + onsite_noise
    weights = weight_code.astype(jnp.float32) / (32.0 * E_DEV * N_ENERGY)
    energies = e_low + e_step * energy_index.astype(jnp.float32)
    zero_row = jnp.zeros((M,), jnp.float32)

    def forward_step(carry, slot_data):
        prev_re, prev_im, prev_coupling = carry
        onsite_re, onsite_im, coupling, live = slot_data
        square = prev_coupling * prev_coupling
        g_re, g_im = reciprocal(onsite_re - square * prev_re, onsite_im - square * prev_im)
        keep = live > 0.5
        new_carry = (jnp.where(keep, g_re, prev_re), jnp.where(keep, g_im, prev_im), jnp.where(keep, coupling, prev_coupling))
        return new_carry, (g_re, g_im)

    def backward_step(carry, slot_data):
        next_re, next_im = carry
        onsite_re, onsite_im, coupling, live = slot_data
        square = coupling * coupling
        g_re, g_im = reciprocal(onsite_re - square * next_re, onsite_im - square * next_im)
        keep = live > 0.5
        return (jnp.where(keep, g_re, next_re), jnp.where(keep, g_im, next_im)), (next_re, next_im)

    def one_energy(sums, index):
        onsite_re = energies[index] - levels - first_on * lead_shift[index, 0][None, :] - last_on * lead_shift[index, 1][None, :]
        onsite_im = broaden + first_on * lead_width[index, 0][None, :] + last_on * lead_width[index, 1][None, :]
        onsite_im = onsite_im + jnp.zeros_like(onsite_re)
        xs = (onsite_re, onsite_im, hopping, alive)
        _, (left_re, left_im) = lax.scan(forward_step, (zero_row, zero_row, zero_row), xs)
        _, (next_re, next_im) = lax.scan(backward_step, (zero_row, zero_row), xs, reverse=True)
        square = hopping * hopping
        mix_re, mix_im = complex_mul(left_re, left_im, next_re, next_im)
        inv_re, inv_im = reciprocal(1.0 - square * mix_re, -square * mix_im)
        diag_re, diag_im = complex_mul(left_re, left_im, inv_re, inv_im)
        bond_re, bond_im = complex_mul(diag_re, diag_im, next_re, next_im)
        dens_term = -inv_pi * weights[index] * diag_im * alive[:, None]
        bond_term = -2.0 * inv_pi * weights[index] * hopping * hopping * bond_im * alive[:, None]
        return (sums[0] + dens_term, sums[1] + bond_term), None

    start = (jnp.zeros((N_SLAB * PMAX, M), jnp.float32), jnp.zeros((N_SLAB * PMAX, M), jnp.float32))
    (density, bond_density), _ = lax.scan(one_energy, start, jnp.arange(E_DEV * N_ENERGY, dtype=jnp.int32))
    return density, bond_density
```

```python
import jax
import jax.numpy as jnp
from jax import lax
from jax.sharding import PartitionSpec as P

broaden = 0.002
e_low = -1.5
e_step = 3.0 / 4096.0
inv_pi = 1.0 / 3.141592653589793


def reciprocal(real_part, imag_part):
    norm = real_part * real_part + imag_part * imag_part
    return (real_part / norm, -imag_part / norm)


def complex_mul(first_re, first_im, second_re, second_im):
    return (
        first_re * second_re - first_im * second_im,
        first_re * second_im + first_im * second_re,
    )


def join_segments(left, right):
    square = left[6] * left[6]
    mix_re, mix_im = complex_mul(left[4], left[5], right[0], right[1])
    inv_re, inv_im = reciprocal(1.0 - square * mix_re, -square * mix_im)
    left_sq_re, left_sq_im = complex_mul(left[2], left[3], left[2], left[3])
    head_re, head_im = complex_mul(left_sq_re, left_sq_im, right[0], right[1])
    head_re, head_im = complex_mul(head_re, head_im, inv_re, inv_im)
    right_sq_re, right_sq_im = complex_mul(right[2], right[3], right[2], right[3])
    tail_re, tail_im = complex_mul(right_sq_re, right_sq_im, left[4], left[5])
    tail_re, tail_im = complex_mul(tail_re, tail_im, inv_re, inv_im)
    link_re, link_im = complex_mul(left[2], left[3], right[2], right[3])
    link_re, link_im = complex_mul(link_re, link_im, inv_re, inv_im)
    return (
        left[0] + square * head_re,
        left[1] + square * head_im,
        left[6] * link_re,
        left[6] * link_im,
        right[4] + square * tail_re,
        right[5] + square * tail_im,
        right[6],
    )


def forward_pass(onsite_re, onsite_im, hopping, live, start_re, start_im, start_coupling):
    prev_re, prev_im, prev_coupling = start_re, start_im, start_coupling
    out_re, out_im = [], []
    for slot in range(onsite_re.shape[0]):
        square = prev_coupling * prev_coupling
        g_re, g_im = reciprocal(onsite_re[slot] - square * prev_re, onsite_im[slot] - square * prev_im)
        out_re.append(g_re)
        out_im.append(g_im)
        keep = live[slot]
        prev_re = jnp.where(keep, g_re, prev_re)
        prev_im = jnp.where(keep, g_im, prev_im)
        prev_coupling = jnp.where(keep, hopping[slot], prev_coupling)
    return out_re, out_im


def backward_pass(onsite_re, onsite_im, hopping, live, start_re, start_im):
    next_re, next_im = start_re, start_im
    out_re, out_im = [None] * onsite_re.shape[0], [None] * onsite_re.shape[0]
    for slot in reversed(range(onsite_re.shape[0])):
        out_re[slot], out_im[slot] = next_re, next_im
        square = hopping[slot] * hopping[slot]
        g_re, g_im = reciprocal(onsite_re[slot] - square * next_re, onsite_im[slot] - square * next_im)
        keep = live[slot]
        next_re = jnp.where(keep, g_re, next_re)
        next_im = jnp.where(keep, g_im, next_im)
    return out_re, out_im, next_re, next_im


def shards(
    mode_floor, onsite_noise, hopping, lengths, energy_index, weight_code, lead_shift, lead_width
):
    slots = onsite_noise.shape[0]
    modes = onsite_noise.shape[1]
    points = energy_index.shape[0]
    here = lax.axis_index("slab")
    devices = lax.axis_size("slab")
    count = lengths[here]
    place = jnp.arange(slots, dtype=jnp.int32)
    live = [place[slot] < count for slot in range(slots)]
    alive = (place < count).astype(jnp.float32)
    first_on = ((here == 0) & (place == 0)).astype(jnp.float32)[:, None, None]
    last_on = ((here == devices - 1) & (place == count - 1)).astype(jnp.float32)[:, None, None]
    energies = e_low + e_step * energy_index.astype(jnp.float32)
    weights = weight_code.astype(jnp.float32) / (32.0 * points * lax.axis_size("energy"))
    levels = mode_floor[None, :] + onsite_noise
    onsite_re = (
        energies[None, :, None]
        - levels[:, None, :]
        - first_on * lead_shift[None, :, 0, :]
        - last_on * lead_shift[None, :, 1, :]
    )
    onsite_im = broaden + first_on * lead_width[None, :, 0, :] + last_on * lead_width[None, :, 1, :]
    onsite_im = onsite_im + jnp.zeros_like(onsite_re)
    coupling_rows = hopping[:, None, :]
    zero = jnp.zeros((points, modes), jnp.float32)
    zero_row = jnp.zeros((1, modes), jnp.float32)

    def single(slot):
        g_re, g_im = reciprocal(onsite_re[slot], onsite_im[slot])
        return (g_re, g_im, g_re, g_im, g_re, g_im, coupling_rows[slot])

    summary = single(0)
    for slot in range(1, slots):
        joined = join_segments(summary, single(slot))
        summary = tuple(jnp.where(live[slot], new, old) for new, old in zip(joined, summary))
    first_re, first_im, cross_re, cross_im, final_re, final_im, coupling = summary

    packed = jnp.concatenate(
        [first_re, first_im, cross_re, cross_im, final_re, final_im, coupling], axis=0
    )
    every = lax.all_gather(packed, "slab")

    def part(device, index):
        return every[device, index * points:(index + 1) * points]

    into_re, into_im, into_coupling = zero, zero, zero_row
    run_re, run_im = zero, zero
    for device in range(devices - 1):
        pp = every[device - 1, 6 * points:6 * points + 1] if device > 0 else zero_row
        pp = pp * pp
        c_re, c_im = complex_mul(part(device, 2), part(device, 3), part(device, 2), part(device, 3))
        m_re, m_im = complex_mul(run_re, run_im, part(device, 0), part(device, 1))
        inv_re, inv_im = reciprocal(1.0 - pp * m_re, -pp * m_im)
        t_re, t_im = complex_mul(c_re, c_im, run_re, run_im)
        t_re, t_im = complex_mul(t_re, t_im, inv_re, inv_im)
        run_re = part(device, 4) + pp * t_re
        run_im = part(device, 5) + pp * t_im
        take = device + 1 == here
        into_re = jnp.where(take, run_re, into_re)
        into_im = jnp.where(take, run_im, into_im)
        into_coupling = jnp.where(take, every[device, 6 * points:6 * points + 1], into_coupling)
    from_re, from_im = zero, zero
    run_re, run_im = zero, zero
    for device in range(devices - 1, 0, -1):
        pp = every[device, 6 * points:6 * points + 1]
        pp = pp * pp
        c_re, c_im = complex_mul(part(device, 2), part(device, 3), part(device, 2), part(device, 3))
        m_re, m_im = complex_mul(part(device, 4), part(device, 5), run_re, run_im)
        inv_re, inv_im = reciprocal(1.0 - pp * m_re, -pp * m_im)
        h_re, h_im = complex_mul(c_re, c_im, run_re, run_im)
        h_re, h_im = complex_mul(h_re, h_im, inv_re, inv_im)
        run_re = part(device, 0) + pp * h_re
        run_im = part(device, 1) + pp * h_im
        take = device - 1 == here
        from_re = jnp.where(take, run_re, from_re)
        from_im = jnp.where(take, run_im, from_im)

    left_re, left_im = forward_pass(
        onsite_re, onsite_im, coupling_rows, live, into_re, into_im, into_coupling
    )
    next_re, next_im, _, _ = backward_pass(onsite_re, onsite_im, coupling_rows, live, from_re, from_im)
    left_re, left_im = jnp.stack(left_re), jnp.stack(left_im)
    next_re, next_im = jnp.stack(next_re), jnp.stack(next_im)
    square = coupling_rows * coupling_rows
    mix_re, mix_im = complex_mul(left_re, left_im, next_re, next_im)
    inv_re, inv_im = reciprocal(1.0 - square * mix_re, -square * mix_im)
    diag_re, diag_im = complex_mul(left_re, left_im, inv_re, inv_im)
    bond_re, bond_im = complex_mul(diag_re, diag_im, next_re, next_im)
    live_rows = alive[:, None]
    density_term = -inv_pi * jnp.sum(weights[None, :, None] * diag_im, axis=1) * live_rows
    bond_term = (
        -2.0 * inv_pi * jnp.sum(weights[None, :, None] * square * bond_im, axis=1) * live_rows
    )
    both = lax.psum_scatter(
        jnp.stack([density_term, bond_term]), "energy", scatter_dimension=2, tiled=True
    )
    return (both[0], both[1])


def solution(mesh):
    in_specs = (
        P(),
        P("slab", None),
        P("slab", None),
        P(),
        P("energy"),
        P("energy"),
        P("energy", None, None),
        P("energy", None, None),
    )
    out_specs = (P("slab", "energy"), P("slab", "energy"))
    return jax.shard_map(shards, mesh=mesh, in_specs=in_specs, out_specs=out_specs, check_vma=False)
```

```python
import jax
import jax.numpy as jnp
from jax import lax
from jax.experimental import pallas as pl
from jax.experimental.pallas import tpu as pltpu
from jax.sharding import PartitionSpec as P

broaden = 0.002
e_low = -1.5
e_step = 3.0 / 4096.0
inv_pi = 1.0 / 3.141592653589793


def reciprocal(real_part, imag_part):
    norm = real_part * real_part + imag_part * imag_part
    return (real_part / norm, -imag_part / norm)


def complex_mul(first_re, first_im, second_re, second_im):
    return (
        first_re * second_re - first_im * second_im,
        first_re * second_im + first_im * second_re,
    )


def join_segments(left, right):
    square = left[6] * left[6]
    mix_re, mix_im = complex_mul(left[4], left[5], right[0], right[1])
    inv_re, inv_im = reciprocal(1.0 - square * mix_re, -square * mix_im)
    left_sq_re, left_sq_im = complex_mul(left[2], left[3], left[2], left[3])
    head_re, head_im = complex_mul(left_sq_re, left_sq_im, right[0], right[1])
    head_re, head_im = complex_mul(head_re, head_im, inv_re, inv_im)
    right_sq_re, right_sq_im = complex_mul(right[2], right[3], right[2], right[3])
    tail_re, tail_im = complex_mul(right_sq_re, right_sq_im, left[4], left[5])
    tail_re, tail_im = complex_mul(tail_re, tail_im, inv_re, inv_im)
    link_re, link_im = complex_mul(left[2], left[3], right[2], right[3])
    link_re, link_im = complex_mul(link_re, link_im, inv_re, inv_im)
    return (
        left[0] + square * head_re,
        left[1] + square * head_im,
        left[6] * link_re,
        left[6] * link_im,
        right[4] + square * tail_re,
        right[5] + square * tail_im,
        right[6],
    )


def summary_kernel(count_ref, are_ref, aim_ref, hop_ref, out_ref):
    points = are_ref.shape[1]

    def single(slot):
        g_re, g_im = reciprocal(are_ref[slot], aim_ref[slot])
        return (g_re, g_im, g_re, g_im, g_re, g_im, hop_ref[slot])

    def body(slot, summary):
        return join_segments(summary, single(slot))

    summary = lax.fori_loop(1, count_ref[0], body, single(0))
    for field in range(6):
        out_ref[field * points:(field + 1) * points] = summary[field]
    out_ref[6 * points] = summary[6]


def final_kernel(
    here_ref, count_ref, weight_ref, every_ref, are_ref, aim_ref, hop_ref,
    dens_ref, bond_ref, left_re_ref, left_im_ref,
):
    points = are_ref.shape[1]
    devices = every_ref.shape[0]
    here = here_ref[0]
    count = count_ref[0]

    def field(device, index):
        return every_ref[device, index * points:(index + 1) * points]

    def coupling_of(device):
        return every_ref[device, 6 * points]

    def into_body(device, run):
        run_re, run_im = run
        pp = coupling_of(jnp.maximum(device - 1, 0))
        pp = pp * pp
        c_re, c_im = complex_mul(field(device, 2), field(device, 3), field(device, 2), field(device, 3))
        m_re, m_im = complex_mul(run_re, run_im, field(device, 0), field(device, 1))
        inv_re, inv_im = reciprocal(1.0 - pp * m_re, -pp * m_im)
        t_re, t_im = complex_mul(c_re, c_im, run_re, run_im)
        t_re, t_im = complex_mul(t_re, t_im, inv_re, inv_im)
        return (field(device, 4) + pp * t_re, field(device, 5) + pp * t_im)

    zero = jnp.zeros(are_ref.shape[1:], jnp.float32)
    into_re, into_im = lax.fori_loop(0, here, into_body, (zero, zero))
    into_coupling = coupling_of(jnp.maximum(here - 1, 0))

    def from_body(step, run):
        run_re, run_im = run
        device = devices - 1 - step
        pp = coupling_of(device)
        pp = pp * pp
        c_re, c_im = complex_mul(field(device, 2), field(device, 3), field(device, 2), field(device, 3))
        m_re, m_im = complex_mul(field(device, 4), field(device, 5), run_re, run_im)
        inv_re, inv_im = reciprocal(1.0 - pp * m_re, -pp * m_im)
        h_re, h_im = complex_mul(c_re, c_im, run_re, run_im)
        h_re, h_im = complex_mul(h_re, h_im, inv_re, inv_im)
        return (field(device, 0) + pp * h_re, field(device, 1) + pp * h_im)

    from_re, from_im = lax.fori_loop(0, devices - 1 - here, from_body, (zero, zero))

    def forward_body(slot, carry):
        prev_re, prev_im, prev_coupling = carry
        square = prev_coupling * prev_coupling
        g_re, g_im = reciprocal(are_ref[slot] - square * prev_re, aim_ref[slot] - square * prev_im)
        left_re_ref[slot] = g_re
        left_im_ref[slot] = g_im
        return (g_re, g_im, hop_ref[slot])

    lax.fori_loop(0, count, forward_body, (into_re, into_im, into_coupling))
    dens_ref[...] = jnp.zeros(dens_ref.shape, jnp.float32)
    bond_ref[...] = jnp.zeros(bond_ref.shape, jnp.float32)

    def backward_body(step, carry):
        next_re, next_im = carry
        slot = count - 1 - step
        left_re, left_im = left_re_ref[slot], left_im_ref[slot]
        square = hop_ref[slot] * hop_ref[slot]
        mix_re, mix_im = complex_mul(left_re, left_im, next_re, next_im)
        inv_re, inv_im = reciprocal(1.0 - square * mix_re, -square * mix_im)
        diag_re, diag_im = complex_mul(left_re, left_im, inv_re, inv_im)
        _, bond_im = complex_mul(diag_re, diag_im, next_re, next_im)
        dens = weight_ref[0] * diag_im[0]
        bond = weight_ref[0] * (square * bond_im[0])
        for point in range(1, points):
            dens = dens + weight_ref[point] * diag_im[point]
            bond = bond + weight_ref[point] * (square * bond_im[point])
        dens_ref[slot] = -inv_pi * dens
        bond_ref[slot] = -2.0 * inv_pi * bond
        return reciprocal(are_ref[slot] - square * next_re, aim_ref[slot] - square * next_im)

    lax.fori_loop(0, count, backward_body, (from_re, from_im))


def shards(
    mode_floor, onsite_noise, hopping, lengths, energy_index, weight_code, lead_shift, lead_width
):
    slots = onsite_noise.shape[0]
    modes = onsite_noise.shape[1]
    points = energy_index.shape[0]
    rows = modes // 128
    here = lax.axis_index("slab")
    devices = lax.axis_size("slab")
    count = lengths[here]
    place = jnp.arange(slots, dtype=jnp.int32)
    first_on = ((here == 0) & (place == 0)).astype(jnp.float32)[:, None, None, None]
    last_on = ((here == devices - 1) & (place == count - 1)).astype(jnp.float32)[:, None, None, None]
    energies = e_low + e_step * energy_index.astype(jnp.float32)
    weights = weight_code.astype(jnp.float32) / (32.0 * points * lax.axis_size("energy"))
    levels = (mode_floor[None, :] + onsite_noise).reshape(slots, 1, rows, 128)
    shift = lead_shift.reshape(1, points, 2, rows, 128)
    width = lead_width.reshape(1, points, 2, rows, 128)
    onsite_re = (
        energies[None, :, None, None]
        - levels
        - first_on * shift[:, :, 0]
        - last_on * shift[:, :, 1]
    )
    onsite_im = broaden + first_on * width[:, :, 0] + last_on * width[:, :, 1]
    onsite_im = onsite_im + jnp.zeros_like(onsite_re)
    coupling_rows = hopping.reshape(slots, rows, 128)
    count_arr = count.reshape(1)
    here_arr = here.astype(jnp.int32).reshape(1)
    smem = pl.BlockSpec(memory_space=pltpu.SMEM)
    vmem = pl.BlockSpec(memory_space=pltpu.VMEM)

    packed = pl.pallas_call(
        summary_kernel,
        out_shape=jax.ShapeDtypeStruct((6 * points + 1, rows, 128), jnp.float32),
        in_specs=[smem, vmem, vmem, vmem],
        out_specs=vmem,
    )(count_arr, onsite_re, onsite_im, coupling_rows)
    every = lax.all_gather(packed, "slab")
    density, bond_density = pl.pallas_call(
        final_kernel,
        out_shape=(
            jax.ShapeDtypeStruct((slots, rows, 128), jnp.float32),
            jax.ShapeDtypeStruct((slots, rows, 128), jnp.float32),
        ),
        in_specs=[smem, smem, smem, vmem, vmem, vmem, vmem],
        out_specs=(vmem, vmem),
        scratch_shapes=[
            pltpu.VMEM((slots, points, rows, 128), jnp.float32),
            pltpu.VMEM((slots, points, rows, 128), jnp.float32),
        ],
    )(here_arr, count_arr, weights, every, onsite_re, onsite_im, coupling_rows)
    both = jnp.stack([density.reshape(slots, modes), bond_density.reshape(slots, modes)])
    both = lax.psum_scatter(both, "energy", scatter_dimension=2, tiled=True)
    return (both[0], both[1])


def solution(mesh):
    in_specs = (
        P(),
        P("slab", None),
        P("slab", None),
        P(),
        P("energy"),
        P("energy"),
        P("energy", None, None),
        P("energy", None, None),
    )
    out_specs = (P("slab", "energy"), P("slab", "energy"))
    return jax.shard_map(shards, mesh=mesh, in_specs=in_specs, out_specs=out_specs, check_vma=False)
```

```python
import jax
import jax.numpy as jnp
from jax import lax
from jax.experimental import pallas as pl
from jax.experimental.pallas import tpu as pltpu
from jax.sharding import PartitionSpec as P

broaden = 0.002
e_low = -1.5
e_step = 3.0 / 4096.0
inv_pi = 1.0 / 3.141592653589793


def reciprocal(real_part, imag_part):
    norm = real_part * real_part + imag_part * imag_part
    return (real_part / norm, -imag_part / norm)


def complex_mul(first_re, first_im, second_re, second_im):
    return (
        first_re * second_re - first_im * second_im,
        first_re * second_im + first_im * second_re,
    )


def join_segments(left, right):
    square = left[6] * left[6]
    mix_re, mix_im = complex_mul(left[4], left[5], right[0], right[1])
    inv_re, inv_im = reciprocal(1.0 - square * mix_re, -square * mix_im)
    left_sq_re, left_sq_im = complex_mul(left[2], left[3], left[2], left[3])
    head_re, head_im = complex_mul(left_sq_re, left_sq_im, right[0], right[1])
    head_re, head_im = complex_mul(head_re, head_im, inv_re, inv_im)
    right_sq_re, right_sq_im = complex_mul(right[2], right[3], right[2], right[3])
    tail_re, tail_im = complex_mul(right_sq_re, right_sq_im, left[4], left[5])
    tail_re, tail_im = complex_mul(tail_re, tail_im, inv_re, inv_im)
    link_re, link_im = complex_mul(left[2], left[3], right[2], right[3])
    link_re, link_im = complex_mul(link_re, link_im, inv_re, inv_im)
    return (
        left[0] + square * head_re,
        left[1] + square * head_im,
        left[6] * link_re,
        left[6] * link_im,
        right[4] + square * tail_re,
        right[5] + square * tail_im,
        right[6],
    )


def summary_kernel(count_ref, are_ref, aim_ref, hop_ref, *out_refs):
    per = are_ref.shape[1] // len(out_refs)

    def single(slot):
        g_re, g_im = reciprocal(are_ref[slot], aim_ref[slot])
        return (g_re, g_im, g_re, g_im, g_re, g_im, hop_ref[slot])

    def body(slot, summary):
        return join_segments(summary, single(slot))

    first_re, first_im, cross_re, cross_im, final_re, final_im, coupling = lax.fori_loop(
        1, count_ref[0], body, single(0)
    )
    square = coupling * coupling
    sq_re, sq_im = complex_mul(cross_re, cross_im, cross_re, cross_im)
    fields = (first_re, first_im, square * final_re, square * final_im, square * sq_re, square * sq_im)
    for group, out_ref in enumerate(out_refs):
        for index, value in enumerate(fields):
            out_ref[index * per:(index + 1) * per] = value[group * per:(group + 1) * per]


def final_kernel(here_ref, count_ref, weight_ref, *refs):
    every_refs = refs[:len(refs) - 7]
    are_ref, aim_ref, hop_ref, dens_ref, bond_ref, left_re_ref, left_im_ref = refs[len(refs) - 7:]
    points = are_ref.shape[1]
    per = points // len(every_refs)
    devices = every_refs[0].shape[0]
    here = here_ref[0]
    count = count_ref[0]
    zero = jnp.zeros((per,) + are_ref.shape[2:], jnp.float32)
    into_parts_re, into_parts_im, from_parts_re, from_parts_im = [], [], [], []
    for every_ref in every_refs:

        def field(device, index, every_ref=every_ref):
            return every_ref[device, index * per:(index + 1) * per]

        def into_body(device, run):
            run_re, run_im = run
            m_re, m_im = complex_mul(run_re, run_im, field(device, 0), field(device, 1))
            inv_re, inv_im = reciprocal(1.0 - m_re, -m_im)
            t_re, t_im = complex_mul(field(device, 4), field(device, 5), run_re, run_im)
            t_re, t_im = complex_mul(t_re, t_im, inv_re, inv_im)
            return (field(device, 2) + t_re, field(device, 3) + t_im)

        def from_body(step, run):
            run_re, run_im = run
            device = devices - 1 - step
            m_re, m_im = complex_mul(field(device, 2), field(device, 3), run_re, run_im)
            inv_re, inv_im = reciprocal(1.0 - m_re, -m_im)
            h_re, h_im = complex_mul(field(device, 4), field(device, 5), run_re, run_im)
            h_re, h_im = complex_mul(h_re, h_im, inv_re, inv_im)
            return (field(device, 0) + h_re, field(device, 1) + h_im)

        into_re, into_im = lax.fori_loop(0, here, into_body, (zero, zero))
        from_re, from_im = lax.fori_loop(0, devices - 1 - here, from_body, (zero, zero))
        into_parts_re.append(into_re)
        into_parts_im.append(into_im)
        from_parts_re.append(from_re)
        from_parts_im.append(from_im)
    into_re = jnp.concatenate(into_parts_re, axis=0)
    into_im = jnp.concatenate(into_parts_im, axis=0)
    from_re = jnp.concatenate(from_parts_re, axis=0)
    from_im = jnp.concatenate(from_parts_im, axis=0)

    def forward_body(slot, carry):
        prev_re, prev_im, prev_coupling = carry
        square = prev_coupling * prev_coupling
        g_re, g_im = reciprocal(are_ref[slot] - square * prev_re, aim_ref[slot] - square * prev_im)
        left_re_ref[slot] = g_re
        left_im_ref[slot] = g_im
        return (g_re, g_im, hop_ref[slot])

    ones = jnp.ones(hop_ref.shape[1:], jnp.float32)
    lax.fori_loop(0, count, forward_body, (into_re, into_im, ones))
    dens_ref[...] = jnp.zeros(dens_ref.shape, jnp.float32)
    bond_ref[...] = jnp.zeros(bond_ref.shape, jnp.float32)

    def backward_body(step, carry):
        next_re, next_im = carry
        slot = count - 1 - step
        left_re, left_im = left_re_ref[slot], left_im_ref[slot]
        square = hop_ref[slot] * hop_ref[slot]
        mix_re, mix_im = complex_mul(left_re, left_im, next_re, next_im)
        inv_re, inv_im = reciprocal(1.0 - square * mix_re, -square * mix_im)
        diag_re, diag_im = complex_mul(left_re, left_im, inv_re, inv_im)
        _, bond_im = complex_mul(diag_re, diag_im, next_re, next_im)
        dens = weight_ref[0] * diag_im[0]
        bond = weight_ref[0] * (square * bond_im[0])
        for point in range(1, points):
            dens = dens + weight_ref[point] * diag_im[point]
            bond = bond + weight_ref[point] * (square * bond_im[point])
        dens_ref[slot] = -inv_pi * dens
        bond_ref[slot] = -2.0 * inv_pi * bond
        return reciprocal(are_ref[slot] - square * next_re, aim_ref[slot] - square * next_im)

    lax.fori_loop(0, count, backward_body, (from_re, from_im))


def shards(
    mode_floor, onsite_noise, hopping, lengths, energy_index, weight_code, lead_shift, lead_width
):
    slots = onsite_noise.shape[0]
    modes = onsite_noise.shape[1]
    points = energy_index.shape[0]
    rows = modes // 128
    here = lax.axis_index("slab")
    devices = lax.axis_size("slab")
    count = lengths[here]
    place = jnp.arange(slots, dtype=jnp.int32)
    first_on = ((here == 0) & (place == 0)).astype(jnp.float32)[:, None, None, None]
    last_on = ((here == devices - 1) & (place == count - 1)).astype(jnp.float32)[:, None, None, None]
    energies = e_low + e_step * energy_index.astype(jnp.float32)
    weights = weight_code.astype(jnp.float32) / (32.0 * points * lax.axis_size("energy"))
    levels = (mode_floor[None, :] + onsite_noise).reshape(slots, 1, rows, 128)
    shift = lead_shift.reshape(1, points, 2, rows, 128)
    width = lead_width.reshape(1, points, 2, rows, 128)
    onsite_re = (
        energies[None, :, None, None]
        - levels
        - first_on * shift[:, :, 0]
        - last_on * shift[:, :, 1]
    )
    onsite_im = broaden + first_on * width[:, :, 0] + last_on * width[:, :, 1]
    onsite_im = onsite_im + jnp.zeros_like(onsite_re)
    coupling_rows = hopping.reshape(slots, rows, 128)
    count_arr = count.reshape(1)
    here_arr = here.astype(jnp.int32).reshape(1)
    smem = pl.BlockSpec(memory_space=pltpu.SMEM)
    vmem = pl.BlockSpec(memory_space=pltpu.VMEM)

    groups = 2 if points % 2 == 0 else 1
    per = points // groups
    packed = pl.pallas_call(
        summary_kernel,
        out_shape=tuple(
            jax.ShapeDtypeStruct((6 * per, rows, 128), jnp.float32) for _ in range(groups)
        ),
        in_specs=[smem, vmem, vmem, vmem],
        out_specs=tuple(vmem for _ in range(groups)),
    )(count_arr, onsite_re, onsite_im, coupling_rows)
    every = [lax.all_gather(part, "slab") for part in packed]
    density, bond_density = pl.pallas_call(
        final_kernel,
        out_shape=(
            jax.ShapeDtypeStruct((slots, rows, 128), jnp.float32),
            jax.ShapeDtypeStruct((slots, rows, 128), jnp.float32),
        ),
        in_specs=[smem, smem, smem] + [vmem] * (groups + 3),
        out_specs=(vmem, vmem),
        scratch_shapes=[
            pltpu.VMEM((slots, points, rows, 128), jnp.float32),
            pltpu.VMEM((slots, points, rows, 128), jnp.float32),
        ],
    )(here_arr, count_arr, weights, *every, onsite_re, onsite_im, coupling_rows)
    both = jnp.stack([density.reshape(slots, modes), bond_density.reshape(slots, modes)])
    both = lax.psum_scatter(both, "energy", scatter_dimension=2, tiled=True)
    return (both[0], both[1])


def solution(mesh):
    in_specs = (
        P(),
        P("slab", None),
        P("slab", None),
        P(),
        P("energy"),
        P("energy"),
        P("energy", None, None),
        P("energy", None, None),
    )
    out_specs = (P("slab", "energy"), P("slab", "energy"))
    return jax.shard_map(shards, mesh=mesh, in_specs=in_specs, out_specs=out_specs, check_vma=False)
```

```python
import functools

import jax
import jax.numpy as jnp
from jax import lax
from jax.experimental import pallas as pl
from jax.experimental.pallas import tpu as pltpu
from jax.sharding import PartitionSpec as P

broaden = 0.002
e_low = -1.5
e_step = 3.0 / 4096.0
inv_pi = 1.0 / 3.141592653589793


def reciprocal(real_part, imag_part):
    norm = real_part * real_part + imag_part * imag_part
    return (real_part / norm, -imag_part / norm)


def complex_mul(first_re, first_im, second_re, second_im):
    return (
        first_re * second_re - first_im * second_im,
        first_re * second_im + first_im * second_re,
    )


def join_segments(left, right):
    square = left[6] * left[6]
    mix_re, mix_im = complex_mul(left[4], left[5], right[0], right[1])
    inv_re, inv_im = reciprocal(1.0 - square * mix_re, -square * mix_im)
    left_sq_re, left_sq_im = complex_mul(left[2], left[3], left[2], left[3])
    head_re, head_im = complex_mul(left_sq_re, left_sq_im, right[0], right[1])
    head_re, head_im = complex_mul(head_re, head_im, inv_re, inv_im)
    right_sq_re, right_sq_im = complex_mul(right[2], right[3], right[2], right[3])
    tail_re, tail_im = complex_mul(right_sq_re, right_sq_im, left[4], left[5])
    tail_re, tail_im = complex_mul(tail_re, tail_im, inv_re, inv_im)
    link_re, link_im = complex_mul(left[2], left[3], right[2], right[3])
    link_re, link_im = complex_mul(link_re, link_im, inv_re, inv_im)
    return (
        left[0] + square * head_re,
        left[1] + square * head_im,
        left[6] * link_re,
        left[6] * link_im,
        right[4] + square * tail_re,
        right[5] + square * tail_im,
        right[6],
    )


def summary_kernel(count_ref, are_ref, aim_ref, hop_ref, out_ref):
    points = are_ref.shape[1]

    def single(slot):
        g_re, g_im = reciprocal(are_ref[slot], aim_ref[slot])
        return (g_re, g_im, g_re, g_im, g_re, g_im, hop_ref[slot])

    def body(slot, summary):
        return join_segments(summary, single(slot))

    first_re, first_im, cross_re, cross_im, final_re, final_im, coupling = lax.fori_loop(
        1, count_ref[0], body, single(0)
    )
    square = coupling * coupling
    sq_re, sq_im = complex_mul(cross_re, cross_im, cross_re, cross_im)
    fields = (first_re, first_im, square * final_re, square * final_im, square * sq_re, square * sq_im)
    for index, value in enumerate(fields):
        out_ref[index * points:(index + 1) * points] = value


def final_kernel(here_ref, count_ref, weight_ref, every_ref, are_ref, aim_ref, hop_ref,
                 dens_ref, bond_ref, left_re_ref, left_im_ref, *, mixed):
    points = are_ref.shape[1]
    devices = every_ref.shape[0]
    here = here_ref[0]
    count = count_ref[0]

    def field(device, index):
        block = jnp.bitwise_xor(device, here) if mixed else device
        return every_ref[block, index * points:(index + 1) * points]

    def into_body(device, run):
        run_re, run_im = run
        m_re, m_im = complex_mul(run_re, run_im, field(device, 0), field(device, 1))
        inv_re, inv_im = reciprocal(1.0 - m_re, -m_im)
        t_re, t_im = complex_mul(field(device, 4), field(device, 5), run_re, run_im)
        t_re, t_im = complex_mul(t_re, t_im, inv_re, inv_im)
        return (field(device, 2) + t_re, field(device, 3) + t_im)

    def from_body(step, run):
        run_re, run_im = run
        device = devices - 1 - step
        m_re, m_im = complex_mul(field(device, 2), field(device, 3), run_re, run_im)
        inv_re, inv_im = reciprocal(1.0 - m_re, -m_im)
        h_re, h_im = complex_mul(field(device, 4), field(device, 5), run_re, run_im)
        h_re, h_im = complex_mul(h_re, h_im, inv_re, inv_im)
        return (field(device, 0) + h_re, field(device, 1) + h_im)

    zero = jnp.zeros(are_ref.shape[1:], jnp.float32)
    into_re, into_im = lax.fori_loop(0, here, into_body, (zero, zero))
    from_re, from_im = lax.fori_loop(0, devices - 1 - here, from_body, (zero, zero))

    def forward_body(slot, carry):
        prev_re, prev_im, prev_coupling = carry
        square = prev_coupling * prev_coupling
        g_re, g_im = reciprocal(are_ref[slot] - square * prev_re, aim_ref[slot] - square * prev_im)
        left_re_ref[slot] = g_re
        left_im_ref[slot] = g_im
        return (g_re, g_im, hop_ref[slot])

    ones = jnp.ones(hop_ref.shape[1:], jnp.float32)
    lax.fori_loop(0, count, forward_body, (into_re, into_im, ones))
    dens_ref[...] = jnp.zeros(dens_ref.shape, jnp.float32)
    bond_ref[...] = jnp.zeros(bond_ref.shape, jnp.float32)

    def backward_body(step, carry):
        next_re, next_im = carry
        slot = count - 1 - step
        left_re, left_im = left_re_ref[slot], left_im_ref[slot]
        square = hop_ref[slot] * hop_ref[slot]
        mix_re, mix_im = complex_mul(left_re, left_im, next_re, next_im)
        inv_re, inv_im = reciprocal(1.0 - square * mix_re, -square * mix_im)
        diag_re, diag_im = complex_mul(left_re, left_im, inv_re, inv_im)
        _, bond_im = complex_mul(diag_re, diag_im, next_re, next_im)
        dens = weight_ref[0] * diag_im[0]
        bond = weight_ref[0] * (square * bond_im[0])
        for point in range(1, points):
            dens = dens + weight_ref[point] * diag_im[point]
            bond = bond + weight_ref[point] * (square * bond_im[point])
        dens_ref[slot] = -inv_pi * dens
        bond_ref[slot] = -2.0 * inv_pi * bond
        return reciprocal(are_ref[slot] - square * next_re, aim_ref[slot] - square * next_im)

    lax.fori_loop(0, count, backward_body, (from_re, from_im))


def shards(
    mode_floor, onsite_noise, hopping, lengths, energy_index, weight_code, lead_shift, lead_width
):
    slots = onsite_noise.shape[0]
    modes = onsite_noise.shape[1]
    points = energy_index.shape[0]
    rows = modes // 128
    here = lax.axis_index("slab")
    devices = lax.axis_size("slab")
    count = lengths[here]
    place = jnp.arange(slots, dtype=jnp.int32)
    first_on = ((here == 0) & (place == 0)).astype(jnp.float32)[:, None, None, None]
    last_on = ((here == devices - 1) & (place == count - 1)).astype(jnp.float32)[:, None, None, None]
    energies = e_low + e_step * energy_index.astype(jnp.float32)
    weights = weight_code.astype(jnp.float32) / (32.0 * points * lax.axis_size("energy"))
    levels = (mode_floor[None, :] + onsite_noise).reshape(slots, 1, rows, 128)
    shift = lead_shift.reshape(1, points, 2, rows, 128)
    width = lead_width.reshape(1, points, 2, rows, 128)
    onsite_re = (
        energies[None, :, None, None]
        - levels
        - first_on * shift[:, :, 0]
        - last_on * shift[:, :, 1]
    )
    onsite_im = broaden + first_on * width[:, :, 0] + last_on * width[:, :, 1]
    onsite_im = onsite_im + jnp.zeros_like(onsite_re)
    coupling_rows = hopping.reshape(slots, rows, 128)
    count_arr = count.reshape(1)
    here_arr = here.astype(jnp.int32).reshape(1)
    smem = pl.BlockSpec(memory_space=pltpu.SMEM)
    vmem = pl.BlockSpec(memory_space=pltpu.VMEM)

    packed = pl.pallas_call(
        summary_kernel,
        out_shape=jax.ShapeDtypeStruct((6 * points, rows, 128), jnp.float32),
        in_specs=[smem, vmem, vmem, vmem],
        out_specs=vmem,
    )(count_arr, onsite_re, onsite_im, coupling_rows)
    mixed = devices & (devices - 1) == 0
    if mixed:
        every = packed[None]
        distance = 1
        while distance < devices:
            pairs = [(device, device ^ distance) for device in range(devices)]
            every = jnp.concatenate([every, lax.ppermute(every, "slab", pairs)], axis=0)
            distance *= 2
    else:
        every = lax.all_gather(packed, "slab")
    density, bond_density = pl.pallas_call(
        functools.partial(final_kernel, mixed=mixed),
        out_shape=(
            jax.ShapeDtypeStruct((slots, rows, 128), jnp.float32),
            jax.ShapeDtypeStruct((slots, rows, 128), jnp.float32),
        ),
        in_specs=[smem, smem, smem, vmem, vmem, vmem, vmem],
        out_specs=(vmem, vmem),
        scratch_shapes=[
            pltpu.VMEM((slots, points, rows, 128), jnp.float32),
            pltpu.VMEM((slots, points, rows, 128), jnp.float32),
        ],
    )(here_arr, count_arr, weights, every, onsite_re, onsite_im, coupling_rows)
    both = jnp.stack([density.reshape(slots, modes), bond_density.reshape(slots, modes)])
    if lax.axis_size("energy") == 2:
        halves = both.reshape(2, slots, 2, modes // 2)
        lower = lax.axis_index("energy") == 0
        mine = jnp.where(lower, halves[:, :, 0], halves[:, :, 1])
        theirs = jnp.where(lower, halves[:, :, 1], halves[:, :, 0])
        both = mine + lax.ppermute(theirs, "energy", [(0, 1), (1, 0)])
    else:
        both = lax.psum_scatter(both, "energy", scatter_dimension=2, tiled=True)
    return (both[0], both[1])


def solution(mesh):
    in_specs = (
        P(),
        P("slab", None),
        P("slab", None),
        P(),
        P("energy"),
        P("energy"),
        P("energy", None, None),
        P("energy", None, None),
    )
    out_specs = (P("slab", "energy"), P("slab", "energy"))
    return jax.shard_map(shards, mesh=mesh, in_specs=in_specs, out_specs=out_specs, check_vma=False)
```

```python
import functools

import jax
import jax.numpy as jnp
from jax import lax
from jax.experimental import pallas as pl
from jax.experimental.pallas import tpu as pltpu
from jax.sharding import PartitionSpec as P

broaden = 0.002
e_low = -1.5
e_step = 3.0 / 4096.0
inv_pi = 1.0 / 3.141592653589793


def reciprocal(real_part, imag_part):
    norm = real_part * real_part + imag_part * imag_part
    return (real_part / norm, -imag_part / norm)


def complex_mul(first_re, first_im, second_re, second_im):
    return (
        first_re * second_re - first_im * second_im,
        first_re * second_im + first_im * second_re,
    )


def join_segments(left, right):
    square = left[6] * left[6]
    mix_re, mix_im = complex_mul(left[4], left[5], right[0], right[1])
    inv_re, inv_im = reciprocal(1.0 - square * mix_re, -square * mix_im)
    left_sq_re, left_sq_im = complex_mul(left[2], left[3], left[2], left[3])
    head_re, head_im = complex_mul(left_sq_re, left_sq_im, right[0], right[1])
    head_re, head_im = complex_mul(head_re, head_im, inv_re, inv_im)
    right_sq_re, right_sq_im = complex_mul(right[2], right[3], right[2], right[3])
    tail_re, tail_im = complex_mul(right_sq_re, right_sq_im, left[4], left[5])
    tail_re, tail_im = complex_mul(tail_re, tail_im, inv_re, inv_im)
    link_re, link_im = complex_mul(left[2], left[3], right[2], right[3])
    link_re, link_im = complex_mul(link_re, link_im, inv_re, inv_im)
    return (
        left[0] + square * head_re,
        left[1] + square * head_im,
        left[6] * link_re,
        left[6] * link_im,
        right[4] + square * tail_re,
        right[5] + square * tail_im,
        right[6],
    )


def summary_kernel(count_ref, are_ref, aim_ref, hop_ref, out_ref):
    points = are_ref.shape[1]

    def single(slot):
        g_re, g_im = reciprocal(are_ref[slot], aim_ref[slot])
        return (g_re, g_im, g_re, g_im, g_re, g_im, hop_ref[slot])

    def body(slot, summary):
        return join_segments(summary, single(slot))

    first_re, first_im, cross_re, cross_im, final_re, final_im, coupling = lax.fori_loop(
        1, count_ref[0], body, single(0)
    )
    square = coupling * coupling
    sq_re, sq_im = complex_mul(cross_re, cross_im, cross_re, cross_im)
    fields = (first_re, first_im, square * final_re, square * final_im, square * sq_re, square * sq_im)
    for index, value in enumerate(fields):
        out_ref[index * points:(index + 1) * points] = value


def final_kernel(here_ref, count_ref, weight_ref, every_ref, are_ref, aim_ref, hop_ref,
                 dens_ref, bond_ref, left_re_ref, left_im_ref, *, mixed):
    points = are_ref.shape[1]
    devices = every_ref.shape[0]
    here = here_ref[0]
    count = count_ref[0]

    def field(device, index):
        block = jnp.bitwise_xor(device, here) if mixed else device
        return every_ref[block, index * points:(index + 1) * points]

    def into_body(device, run):
        run_re, run_im = run
        m_re, m_im = complex_mul(run_re, run_im, field(device, 0), field(device, 1))
        inv_re, inv_im = reciprocal(1.0 - m_re, -m_im)
        t_re, t_im = complex_mul(field(device, 4), field(device, 5), run_re, run_im)
        t_re, t_im = complex_mul(t_re, t_im, inv_re, inv_im)
        return (field(device, 2) + t_re, field(device, 3) + t_im)

    def from_body(step, run):
        run_re, run_im = run
        device = devices - 1 - step
        m_re, m_im = complex_mul(field(device, 2), field(device, 3), run_re, run_im)
        inv_re, inv_im = reciprocal(1.0 - m_re, -m_im)
        h_re, h_im = complex_mul(field(device, 4), field(device, 5), run_re, run_im)
        h_re, h_im = complex_mul(h_re, h_im, inv_re, inv_im)
        return (field(device, 0) + h_re, field(device, 1) + h_im)

    zero = jnp.zeros(are_ref.shape[1:], jnp.float32)
    into_re, into_im = lax.fori_loop(0, here, into_body, (zero, zero))
    from_re, from_im = lax.fori_loop(0, devices - 1 - here, from_body, (zero, zero))

    def forward_body(slot, carry):
        prev_re, prev_im, prev_coupling = carry
        square = prev_coupling * prev_coupling
        g_re, g_im = reciprocal(are_ref[slot] - square * prev_re, aim_ref[slot] - square * prev_im)
        left_re_ref[slot] = g_re
        left_im_ref[slot] = g_im
        return (g_re, g_im, hop_ref[slot])

    ones = jnp.ones(hop_ref.shape[1:], jnp.float32)
    lax.fori_loop(0, count, forward_body, (into_re, into_im, ones))
    dens_ref[...] = jnp.zeros(dens_ref.shape, jnp.float32)
    bond_ref[...] = jnp.zeros(bond_ref.shape, jnp.float32)

    def backward_body(step, carry):
        next_re, next_im = carry
        slot = count - 1 - step
        left_re, left_im = left_re_ref[slot], left_im_ref[slot]
        square = hop_ref[slot] * hop_ref[slot]
        mix_re, mix_im = complex_mul(left_re, left_im, next_re, next_im)
        inv_re, inv_im = reciprocal(1.0 - square * mix_re, -square * mix_im)
        diag_re, diag_im = complex_mul(left_re, left_im, inv_re, inv_im)
        _, bond_im = complex_mul(diag_re, diag_im, next_re, next_im)
        dens = weight_ref[0] * diag_im[0]
        bond = weight_ref[0] * (square * bond_im[0])
        for point in range(1, points):
            dens = dens + weight_ref[point] * diag_im[point]
            bond = bond + weight_ref[point] * (square * bond_im[point])
        dens_ref[slot] = -inv_pi * dens
        bond_ref[slot] = -2.0 * inv_pi * bond
        return reciprocal(are_ref[slot] - square * next_re, aim_ref[slot] - square * next_im)

    lax.fori_loop(0, count, backward_body, (from_re, from_im))


def shards(
    mode_floor, onsite_noise, hopping, lengths, energy_index, weight_code, lead_shift, lead_width
):
    slots = onsite_noise.shape[0]
    modes = onsite_noise.shape[1]
    points = energy_index.shape[0]
    rows = modes // 128
    here = lax.axis_index("slab")
    devices = lax.axis_size("slab")
    count = lengths[here]
    place = jnp.arange(slots, dtype=jnp.int32)
    first_on = ((here == 0) & (place == 0)).astype(jnp.float32)[:, None, None, None]
    last_on = ((here == devices - 1) & (place == count - 1)).astype(jnp.float32)[:, None, None, None]
    energies = e_low + e_step * energy_index.astype(jnp.float32)
    weights = weight_code.astype(jnp.float32) / (32.0 * points * lax.axis_size("energy"))
    levels = (mode_floor[None, :] + onsite_noise).reshape(slots, 1, rows, 128)
    shift = lead_shift.reshape(1, points, 2, rows, 128)
    width = lead_width.reshape(1, points, 2, rows, 128)
    onsite_re = (
        energies[None, :, None, None]
        - levels
        - first_on * shift[:, :, 0]
        - last_on * shift[:, :, 1]
    )
    onsite_im = broaden + first_on * width[:, :, 0] + last_on * width[:, :, 1]
    onsite_im = onsite_im + jnp.zeros_like(onsite_re)
    coupling_rows = hopping.reshape(slots, rows, 128)
    count_arr = count.reshape(1)
    here_arr = here.astype(jnp.int32).reshape(1)
    smem = pl.BlockSpec(memory_space=pltpu.SMEM)
    vmem = pl.BlockSpec(memory_space=pltpu.VMEM)

    packed = pl.pallas_call(
        summary_kernel,
        out_shape=jax.ShapeDtypeStruct((6 * points, rows, 128), jnp.float32),
        in_specs=[smem, vmem, vmem, vmem],
        out_specs=vmem,
    )(count_arr, onsite_re, onsite_im, coupling_rows)
    mixed = devices & (devices - 1) == 0
    if mixed:
        every = packed
        distance = devices // 2
        level = 0
        while distance >= 1:
            pairs = [(device, device ^ distance) for device in range(devices)]
            every = jnp.stack([every, lax.ppermute(every, "slab", pairs)], axis=level)
            distance //= 2
            level += 1
        every = every.reshape((devices,) + packed.shape)
    else:
        every = lax.all_gather(packed, "slab")
    density, bond_density = pl.pallas_call(
        functools.partial(final_kernel, mixed=mixed),
        out_shape=(
            jax.ShapeDtypeStruct((slots, rows, 128), jnp.float32),
            jax.ShapeDtypeStruct((slots, rows, 128), jnp.float32),
        ),
        in_specs=[smem, smem, smem, vmem, vmem, vmem, vmem],
        out_specs=(vmem, vmem),
        scratch_shapes=[
            pltpu.VMEM((slots, points, rows, 128), jnp.float32),
            pltpu.VMEM((slots, points, rows, 128), jnp.float32),
        ],
    )(here_arr, count_arr, weights, every, onsite_re, onsite_im, coupling_rows)
    both = jnp.stack([density.reshape(slots, modes), bond_density.reshape(slots, modes)])
    if lax.axis_size("energy") == 2:
        halves = both.reshape(2, slots, 2, modes // 2)
        lower = lax.axis_index("energy") == 0
        mine = jnp.where(lower, halves[:, :, 0], halves[:, :, 1])
        theirs = jnp.where(lower, halves[:, :, 1], halves[:, :, 0])
        both = mine + lax.ppermute(theirs, "energy", [(0, 1), (1, 0)])
    else:
        both = lax.psum_scatter(both, "energy", scatter_dimension=2, tiled=True)
    return (both[0], both[1])


def solution(mesh):
    in_specs = (
        P(),
        P("slab", None),
        P("slab", None),
        P(),
        P("energy"),
        P("energy"),
        P("energy", None, None),
        P("energy", None, None),
    )
    out_specs = (P("slab", "energy"), P("slab", "energy"))
    return jax.shard_map(shards, mesh=mesh, in_specs=in_specs, out_specs=out_specs, check_vma=False)
```

```python
import functools

import jax
import jax.numpy as jnp
from jax import lax
from jax.experimental import pallas as pl
from jax.experimental.pallas import tpu as pltpu
from jax.sharding import PartitionSpec as P

broaden = 0.002
e_low = -1.5
e_step = 3.0 / 4096.0
inv_pi = 1.0 / 3.141592653589793


def reciprocal(real_part, imag_part):
    norm = real_part * real_part + imag_part * imag_part
    return (real_part / norm, -imag_part / norm)


def complex_mul(first_re, first_im, second_re, second_im):
    return (
        first_re * second_re - first_im * second_im,
        first_re * second_im + first_im * second_re,
    )


def join_segments(left, right):
    square = left[6] * left[6]
    mix_re, mix_im = complex_mul(left[4], left[5], right[0], right[1])
    inv_re, inv_im = reciprocal(1.0 - square * mix_re, -square * mix_im)
    left_sq_re, left_sq_im = complex_mul(left[2], left[3], left[2], left[3])
    head_re, head_im = complex_mul(left_sq_re, left_sq_im, right[0], right[1])
    head_re, head_im = complex_mul(head_re, head_im, inv_re, inv_im)
    right_sq_re, right_sq_im = complex_mul(right[2], right[3], right[2], right[3])
    tail_re, tail_im = complex_mul(right_sq_re, right_sq_im, left[4], left[5])
    tail_re, tail_im = complex_mul(tail_re, tail_im, inv_re, inv_im)
    link_re, link_im = complex_mul(left[2], left[3], right[2], right[3])
    link_re, link_im = complex_mul(link_re, link_im, inv_re, inv_im)
    return (
        left[0] + square * head_re,
        left[1] + square * head_im,
        left[6] * link_re,
        left[6] * link_im,
        right[4] + square * tail_re,
        right[5] + square * tail_im,
        right[6],
    )


def onsite_terms(table_ref, energy_ref, here, count, devices, slots, points, slot):
    rows = 2 * slots
    levels = table_ref[slot]
    first_on = jnp.logical_and(here == 0, slot == 0).astype(jnp.float32)
    last_on = jnp.logical_and(here == devices - 1, slot == count - 1).astype(jnp.float32)
    onsite_re, onsite_im = [], []
    for point in range(points):
        energy = e_low + e_step * energy_ref[point].astype(jnp.float32)
        onsite_re.append(
            energy - levels
            - first_on * table_ref[rows + 2 * point]
            - last_on * table_ref[rows + 2 * point + 1]
        )
        onsite_im.append(
            broaden
            + first_on * table_ref[rows + 2 * points + 2 * point]
            + last_on * table_ref[rows + 2 * points + 2 * point + 1]
        )
    return jnp.stack(onsite_re), jnp.stack(onsite_im)


def summary_kernel(here_ref, length_ref, energy_ref, table_ref, out_ref, *, slots, points, devices):
    here = here_ref[0]
    count = length_ref[here]

    def single(slot):
        onsite_re, onsite_im = onsite_terms(
            table_ref, energy_ref, here, count, devices, slots, points, slot
        )
        g_re, g_im = reciprocal(onsite_re, onsite_im)
        return (g_re, g_im, g_re, g_im, g_re, g_im, table_ref[slots + slot])

    def body(slot, summary):
        return join_segments(summary, single(slot))

    first_re, first_im, cross_re, cross_im, final_re, final_im, coupling = lax.fori_loop(
        1, count, body, single(0)
    )
    square = coupling * coupling
    sq_re, sq_im = complex_mul(cross_re, cross_im, cross_re, cross_im)
    fields = (first_re, first_im, square * final_re, square * final_im, square * sq_re, square * sq_im)
    for index, value in enumerate(fields):
        out_ref[index * points:(index + 1) * points] = value


def final_kernel(here_ref, length_ref, energy_ref, code_ref, every_ref, table_ref,
                 low_ref, high_ref, left_re_ref, left_im_ref, dens_ref, bond_ref, *, slots, points, mixed, scale):
    devices = every_ref.shape[0]
    here = here_ref[0]
    count = length_ref[here]
    rows = table_ref.shape[1]

    def field(device, index):
        block = jnp.bitwise_xor(device, here) if mixed else device
        return every_ref[block, index * points:(index + 1) * points]

    def into_body(device, run):
        run_re, run_im = run
        m_re, m_im = complex_mul(run_re, run_im, field(device, 0), field(device, 1))
        inv_re, inv_im = reciprocal(1.0 - m_re, -m_im)
        t_re, t_im = complex_mul(field(device, 4), field(device, 5), run_re, run_im)
        t_re, t_im = complex_mul(t_re, t_im, inv_re, inv_im)
        return (field(device, 2) + t_re, field(device, 3) + t_im)

    def from_body(step, run):
        run_re, run_im = run
        device = devices - 1 - step
        m_re, m_im = complex_mul(field(device, 2), field(device, 3), run_re, run_im)
        inv_re, inv_im = reciprocal(1.0 - m_re, -m_im)
        h_re, h_im = complex_mul(field(device, 4), field(device, 5), run_re, run_im)
        h_re, h_im = complex_mul(h_re, h_im, inv_re, inv_im)
        return (field(device, 0) + h_re, field(device, 1) + h_im)

    zero = jnp.zeros((points,) + table_ref.shape[1:], jnp.float32)
    into_re, into_im = lax.fori_loop(0, here, into_body, (zero, zero))
    from_re, from_im = lax.fori_loop(0, devices - 1 - here, from_body, (zero, zero))

    def onsite(slot):
        return onsite_terms(table_ref, energy_ref, here, count, devices, slots, points, slot)

    def forward_body(slot, carry):
        prev_re, prev_im, prev_coupling = carry
        onsite_re, onsite_im = onsite(slot)
        square = prev_coupling * prev_coupling
        g_re, g_im = reciprocal(onsite_re - square * prev_re, onsite_im - square * prev_im)
        left_re_ref[slot] = g_re
        left_im_ref[slot] = g_im
        return (g_re, g_im, table_ref[slots + slot])

    ones = jnp.ones(table_ref.shape[1:], jnp.float32)
    lax.fori_loop(0, count, forward_body, (into_re, into_im, ones))
    dens_ref[...] = jnp.zeros(dens_ref.shape, jnp.float32)
    bond_ref[...] = jnp.zeros(bond_ref.shape, jnp.float32)
    weights = [code_ref[point].astype(jnp.float32) * scale for point in range(points)]

    def backward_body(step, carry):
        next_re, next_im = carry
        slot = count - 1 - step
        onsite_re, onsite_im = onsite(slot)
        left_re, left_im = left_re_ref[slot], left_im_ref[slot]
        coupling = table_ref[slots + slot]
        square = coupling * coupling
        mix_re, mix_im = complex_mul(left_re, left_im, next_re, next_im)
        inv_re, inv_im = reciprocal(1.0 - square * mix_re, -square * mix_im)
        diag_re, diag_im = complex_mul(left_re, left_im, inv_re, inv_im)
        _, bond_im = complex_mul(diag_re, diag_im, next_re, next_im)
        dens = weights[0] * diag_im[0]
        bond = weights[0] * (square * bond_im[0])
        for point in range(1, points):
            dens = dens + weights[point] * diag_im[point]
            bond = bond + weights[point] * (square * bond_im[point])
        dens_ref[slot] = -inv_pi * dens
        bond_ref[slot] = -2.0 * inv_pi * bond
        return reciprocal(onsite_re - square * next_re, onsite_im - square * next_im)

    lax.fori_loop(0, count, backward_body, (from_re, from_im))
    for slot in range(slots):
        dens = dens_ref[slot]
        bond = bond_ref[slot]
        for row in range(rows):
            target = low_ref if row < rows // 2 else high_ref
            lane = (row % (rows // 2)) * 128
            target[0, slot:slot + 1, lane:lane + 128] = dens[row:row + 1]
            target[1, slot:slot + 1, lane:lane + 128] = bond[row:row + 1]


def shards(
    mode_floor, onsite_noise, hopping, lengths, energy_index, weight_code, lead_shift, lead_width
):
    slots = onsite_noise.shape[0]
    modes = onsite_noise.shape[1]
    points = energy_index.shape[0]
    rows = modes // 128
    here = lax.axis_index("slab")
    devices = lax.axis_size("slab")
    groups = lax.axis_size("energy")
    table = jnp.concatenate(
        [
            mode_floor[None, :] + onsite_noise,
            hopping,
            lead_shift.reshape(2 * points, modes),
            lead_width.reshape(2 * points, modes),
        ],
        axis=0,
    ).reshape(2 * slots + 4 * points, rows, 128)
    here_arr = here.astype(jnp.int32).reshape(1)
    smem = pl.BlockSpec(memory_space=pltpu.SMEM)
    vmem = pl.BlockSpec(memory_space=pltpu.VMEM)

    packed = pl.pallas_call(
        functools.partial(summary_kernel, slots=slots, points=points, devices=devices),
        out_shape=jax.ShapeDtypeStruct((6 * points, rows, 128), jnp.float32),
        in_specs=[smem, smem, smem, vmem],
        out_specs=vmem,
    )(here_arr, lengths, energy_index, table)
    mixed = devices & (devices - 1) == 0
    if mixed:
        every = packed
        distance = devices // 2
        level = 0
        while distance >= 1:
            pairs = [(device, device ^ distance) for device in range(devices)]
            every = jnp.stack([every, lax.ppermute(every, "slab", pairs)], axis=level)
            distance //= 2
            level += 1
        every = every.reshape((devices,) + packed.shape)
    else:
        every = lax.all_gather(packed, "slab")
    half = jax.ShapeDtypeStruct((2, slots, modes // 2), jnp.float32)
    low, high = pl.pallas_call(
        functools.partial(
            final_kernel, slots=slots, points=points, mixed=mixed,
            scale=1.0 / (32.0 * points * groups),
        ),
        out_shape=(half, half),
        in_specs=[smem, smem, smem, smem, vmem, vmem],
        out_specs=(vmem, vmem),
        scratch_shapes=[
            pltpu.VMEM((slots, points, rows, 128), jnp.float32),
            pltpu.VMEM((slots, points, rows, 128), jnp.float32),
            pltpu.VMEM((slots, rows, 128), jnp.float32),
            pltpu.VMEM((slots, rows, 128), jnp.float32),
        ],
    )(here_arr, lengths, energy_index, weight_code, every, table)
    if groups == 2:
        lower = lax.axis_index("energy") == 0
        mine = jnp.where(lower, low, high)
        theirs = jnp.where(lower, high, low)
        both = mine + lax.ppermute(theirs, "energy", [(0, 1), (1, 0)])
    else:
        both = lax.psum_scatter(
            jnp.concatenate([low, high], axis=2), "energy", scatter_dimension=2, tiled=True
        )
    return (both[0], both[1])


def solution(mesh):
    in_specs = (
        P(),
        P("slab", None),
        P("slab", None),
        P(),
        P("energy"),
        P("energy"),
        P("energy", None, None),
        P("energy", None, None),
    )
    out_specs = (P("slab", "energy"), P("slab", "energy"))
    return jax.shard_map(shards, mesh=mesh, in_specs=in_specs, out_specs=out_specs, check_vma=False)
```

```python
import functools

import jax
import jax.numpy as jnp
from jax import lax
from jax.experimental import pallas as pl
from jax.experimental.pallas import tpu as pltpu
from jax.sharding import PartitionSpec as P

broaden = 0.002
e_low = -1.5
e_step = 3.0 / 4096.0
inv_pi = 1.0 / 3.141592653589793


def reciprocal(real_part, imag_part):
    norm = real_part * real_part + imag_part * imag_part
    return (real_part / norm, -imag_part / norm)


def complex_mul(first_re, first_im, second_re, second_im):
    return (
        first_re * second_re - first_im * second_im,
        first_re * second_im + first_im * second_re,
    )


def join_segments(left, right):
    square = left[6] * left[6]
    mix_re, mix_im = complex_mul(left[4], left[5], right[0], right[1])
    inv_re, inv_im = reciprocal(1.0 - square * mix_re, -square * mix_im)
    left_sq_re, left_sq_im = complex_mul(left[2], left[3], left[2], left[3])
    head_re, head_im = complex_mul(left_sq_re, left_sq_im, right[0], right[1])
    head_re, head_im = complex_mul(head_re, head_im, inv_re, inv_im)
    right_sq_re, right_sq_im = complex_mul(right[2], right[3], right[2], right[3])
    tail_re, tail_im = complex_mul(right_sq_re, right_sq_im, left[4], left[5])
    tail_re, tail_im = complex_mul(tail_re, tail_im, inv_re, inv_im)
    link_re, link_im = complex_mul(left[2], left[3], right[2], right[3])
    link_re, link_im = complex_mul(link_re, link_im, inv_re, inv_im)
    return (
        left[0] + square * head_re,
        left[1] + square * head_im,
        left[6] * link_re,
        left[6] * link_im,
        right[4] + square * tail_re,
        right[5] + square * tail_im,
        right[6],
    )


def onsite_terms(table_ref, energy_ref, here, count, devices, slots, points, slot):
    rows = 2 * slots
    levels = table_ref[slot]
    first_on = jnp.logical_and(here == 0, slot == 0).astype(jnp.float32)
    last_on = jnp.logical_and(here == devices - 1, slot == count - 1).astype(jnp.float32)
    onsite_re, onsite_im = [], []
    for point in range(points):
        energy = e_low + e_step * energy_ref[point].astype(jnp.float32)
        onsite_re.append(
            energy - levels
            - first_on * table_ref[rows + 2 * point]
            - last_on * table_ref[rows + 2 * point + 1]
        )
        onsite_im.append(
            broaden
            + first_on * table_ref[rows + 2 * points + 2 * point]
            + last_on * table_ref[rows + 2 * points + 2 * point + 1]
        )
    return jnp.stack(onsite_re), jnp.stack(onsite_im)


def summary_kernel(here_ref, length_ref, energy_ref, table_ref, out_ref, *, slots, points, devices):
    here = here_ref[0]
    count = length_ref[here]

    def single(slot):
        onsite_re, onsite_im = onsite_terms(
            table_ref, energy_ref, here, count, devices, slots, points, slot
        )
        g_re, g_im = reciprocal(onsite_re, onsite_im)
        return (g_re, g_im, g_re, g_im, g_re, g_im, table_ref[slots + slot])

    def body(slot, summary):
        return join_segments(summary, single(slot))

    first_re, first_im, cross_re, cross_im, final_re, final_im, coupling = lax.fori_loop(
        1, count, body, single(0)
    )
    square = coupling * coupling
    sq_re, sq_im = complex_mul(cross_re, cross_im, cross_re, cross_im)
    fields = (first_re, first_im, square * final_re, square * final_im, square * sq_re, square * sq_im)
    for index, value in enumerate(fields):
        out_ref[index * points:(index + 1) * points] = value


def final_kernel(here_ref, group_ref, length_ref, energy_ref, code_ref, every_ref, table_ref,
                 dens_out_ref, bond_out_ref, theirs_ref, left_re_ref, left_im_ref, dens_ref, bond_ref, *, slots, points, mixed, scale):
    devices = every_ref.shape[0]
    here = here_ref[0]
    count = length_ref[here]
    rows = table_ref.shape[1]

    bits = devices.bit_length() - 1

    def field(device, index):
        block = device
        if mixed:
            offset = jnp.bitwise_xor(device, here)
            block = 0
            for bit in range(bits):
                block = block * 2 + jnp.bitwise_and(jnp.right_shift(offset, bit), 1)
        return every_ref[block, index * points:(index + 1) * points]

    def into_body(device, run):
        run_re, run_im = run
        m_re, m_im = complex_mul(run_re, run_im, field(device, 0), field(device, 1))
        inv_re, inv_im = reciprocal(1.0 - m_re, -m_im)
        t_re, t_im = complex_mul(field(device, 4), field(device, 5), run_re, run_im)
        t_re, t_im = complex_mul(t_re, t_im, inv_re, inv_im)
        return (field(device, 2) + t_re, field(device, 3) + t_im)

    def from_body(step, run):
        run_re, run_im = run
        device = devices - 1 - step
        m_re, m_im = complex_mul(field(device, 2), field(device, 3), run_re, run_im)
        inv_re, inv_im = reciprocal(1.0 - m_re, -m_im)
        h_re, h_im = complex_mul(field(device, 4), field(device, 5), run_re, run_im)
        h_re, h_im = complex_mul(h_re, h_im, inv_re, inv_im)
        return (field(device, 0) + h_re, field(device, 1) + h_im)

    zero = jnp.zeros((points,) + table_ref.shape[1:], jnp.float32)
    into_re, into_im = lax.fori_loop(0, here, into_body, (zero, zero))
    from_re, from_im = lax.fori_loop(0, devices - 1 - here, from_body, (zero, zero))

    def onsite(slot):
        return onsite_terms(table_ref, energy_ref, here, count, devices, slots, points, slot)

    def forward_body(slot, carry):
        prev_re, prev_im, prev_coupling = carry
        onsite_re, onsite_im = onsite(slot)
        square = prev_coupling * prev_coupling
        g_re, g_im = reciprocal(onsite_re - square * prev_re, onsite_im - square * prev_im)
        left_re_ref[slot] = g_re
        left_im_ref[slot] = g_im
        return (g_re, g_im, table_ref[slots + slot])

    ones = jnp.ones(table_ref.shape[1:], jnp.float32)
    lax.fori_loop(0, count, forward_body, (into_re, into_im, ones))
    dens_ref[...] = jnp.zeros(dens_ref.shape, jnp.float32)
    bond_ref[...] = jnp.zeros(bond_ref.shape, jnp.float32)
    weights = [code_ref[point].astype(jnp.float32) * scale for point in range(points)]

    def backward_body(step, carry):
        next_re, next_im = carry
        slot = count - 1 - step
        onsite_re, onsite_im = onsite(slot)
        left_re, left_im = left_re_ref[slot], left_im_ref[slot]
        coupling = table_ref[slots + slot]
        square = coupling * coupling
        mix_re, mix_im = complex_mul(left_re, left_im, next_re, next_im)
        inv_re, inv_im = reciprocal(1.0 - square * mix_re, -square * mix_im)
        diag_re, diag_im = complex_mul(left_re, left_im, inv_re, inv_im)
        _, bond_im = complex_mul(diag_re, diag_im, next_re, next_im)
        dens = weights[0] * diag_im[0]
        bond = weights[0] * (square * bond_im[0])
        for point in range(1, points):
            dens = dens + weights[point] * diag_im[point]
            bond = bond + weights[point] * (square * bond_im[point])
        dens_ref[slot] = -inv_pi * dens
        bond_ref[slot] = -2.0 * inv_pi * bond
        return reciprocal(onsite_re - square * next_re, onsite_im - square * next_im)

    lax.fori_loop(0, count, backward_body, (from_re, from_im))
    lower = group_ref[0] == 0
    half = rows // 2
    for slot in range(slots):
        dens = dens_ref[slot]
        bond = bond_ref[slot]
        for row in range(half):
            lane = row * 128
            for kind, value, mine_ref in ((0, dens, dens_out_ref), (1, bond, bond_out_ref)):
                low, high = value[row:row + 1], value[row + half:row + half + 1]
                mine_ref[slot:slot + 1, lane:lane + 128] = jnp.where(lower, low, high)
                theirs_ref[kind, slot:slot + 1, lane:lane + 128] = jnp.where(lower, high, low)


def shards(
    mode_floor, onsite_noise, hopping, lengths, energy_index, weight_code, lead_shift, lead_width
):
    slots = onsite_noise.shape[0]
    modes = onsite_noise.shape[1]
    points = energy_index.shape[0]
    rows = modes // 128
    here = lax.axis_index("slab")
    devices = lax.axis_size("slab")
    groups = lax.axis_size("energy")
    table = jnp.concatenate(
        [
            mode_floor[None, :] + onsite_noise,
            hopping,
            lead_shift.reshape(2 * points, modes),
            lead_width.reshape(2 * points, modes),
        ],
        axis=0,
    ).reshape(2 * slots + 4 * points, rows, 128)
    here_arr = here.astype(jnp.int32).reshape(1)
    smem = pl.BlockSpec(memory_space=pltpu.SMEM)
    vmem = pl.BlockSpec(memory_space=pltpu.VMEM)

    packed = pl.pallas_call(
        functools.partial(summary_kernel, slots=slots, points=points, devices=devices),
        out_shape=jax.ShapeDtypeStruct((6 * points, rows, 128), jnp.float32),
        in_specs=[smem, smem, smem, vmem],
        out_specs=vmem,
    )(here_arr, lengths, energy_index, table)
    mixed = devices & (devices - 1) == 0
    if mixed:
        every = packed[None]
        distance = devices // 2
        while distance >= 1:
            pairs = [(device, device ^ distance) for device in range(devices)]
            every = jnp.concatenate([every, lax.ppermute(every, "slab", pairs)], axis=0)
            distance //= 2
    else:
        every = lax.all_gather(packed, "slab")
    half = jax.ShapeDtypeStruct((slots, modes // 2), jnp.float32)
    group_arr = lax.axis_index("energy").astype(jnp.int32).reshape(1)
    density, bond_density, theirs = pl.pallas_call(
        functools.partial(
            final_kernel, slots=slots, points=points, mixed=mixed,
            scale=1.0 / (32.0 * points * groups),
        ),
        out_shape=(half, half, jax.ShapeDtypeStruct((2, slots, modes // 2), jnp.float32)),
        in_specs=[smem, smem, smem, smem, smem, vmem, vmem],
        out_specs=(vmem, vmem, vmem),
        scratch_shapes=[
            pltpu.VMEM((slots, points, rows, 128), jnp.float32),
            pltpu.VMEM((slots, points, rows, 128), jnp.float32),
            pltpu.VMEM((slots, rows, 128), jnp.float32),
            pltpu.VMEM((slots, rows, 128), jnp.float32),
        ],
    )(here_arr, group_arr, lengths, energy_index, weight_code, every, table)
    if groups == 2:
        theirs = lax.ppermute(theirs, "energy", [(0, 1), (1, 0)])
        return (density + theirs[0], bond_density + theirs[1])
    lower = lax.axis_index("energy") == 0
    both = jnp.stack([
        jnp.where(lower, jnp.concatenate([density, theirs[0]], axis=1), jnp.concatenate([theirs[0], density], axis=1)),
        jnp.where(lower, jnp.concatenate([bond_density, theirs[1]], axis=1), jnp.concatenate([theirs[1], bond_density], axis=1)),
    ])
    both = lax.psum_scatter(both, "energy", scatter_dimension=2, tiled=True)
    return (both[0], both[1])


def solution(mesh):
    in_specs = (
        P(),
        P("slab", None),
        P("slab", None),
        P(),
        P("energy"),
        P("energy"),
        P("energy", None, None),
        P("energy", None, None),
    )
    out_specs = (P("slab", "energy"), P("slab", "energy"))
    return jax.shard_map(shards, mesh=mesh, in_specs=in_specs, out_specs=out_specs, check_vma=False)
```

```python
import functools

import jax
import jax.numpy as jnp
from jax import lax
from jax.experimental import pallas as pl
from jax.experimental.pallas import tpu as pltpu
from jax.sharding import PartitionSpec as P

broaden = 0.002
e_low = -1.5
e_step = 3.0 / 4096.0
inv_pi = 1.0 / 3.141592653589793


def reciprocal(real_part, imag_part):
    norm = real_part * real_part + imag_part * imag_part
    return (real_part / norm, -imag_part / norm)


def complex_mul(first_re, first_im, second_re, second_im):
    return (
        first_re * second_re - first_im * second_im,
        first_re * second_im + first_im * second_re,
    )


def join_segments(left, right):
    square = left[6] * left[6]
    mix_re, mix_im = complex_mul(left[4], left[5], right[0], right[1])
    inv_re, inv_im = reciprocal(1.0 - square * mix_re, -square * mix_im)
    left_sq_re, left_sq_im = complex_mul(left[2], left[3], left[2], left[3])
    head_re, head_im = complex_mul(left_sq_re, left_sq_im, right[0], right[1])
    head_re, head_im = complex_mul(head_re, head_im, inv_re, inv_im)
    right_sq_re, right_sq_im = complex_mul(right[2], right[3], right[2], right[3])
    tail_re, tail_im = complex_mul(right_sq_re, right_sq_im, left[4], left[5])
    tail_re, tail_im = complex_mul(tail_re, tail_im, inv_re, inv_im)
    link_re, link_im = complex_mul(left[2], left[3], right[2], right[3])
    link_re, link_im = complex_mul(link_re, link_im, inv_re, inv_im)
    return (
        left[0] + square * head_re,
        left[1] + square * head_im,
        left[6] * link_re,
        left[6] * link_im,
        right[4] + square * tail_re,
        right[5] + square * tail_im,
        right[6],
    )


def onsite_terms(table_ref, energy_ref, here, count, devices, slots, points, slot):
    rows = 2 * slots
    levels = table_ref[slot]
    first_on = jnp.logical_and(here == 0, slot == 0).astype(jnp.float32)
    last_on = jnp.logical_and(here == devices - 1, slot == count - 1).astype(jnp.float32)
    onsite_re, onsite_im = [], []
    for point in range(points):
        energy = e_low + e_step * energy_ref[point].astype(jnp.float32)
        onsite_re.append(
            energy - levels
            - first_on * table_ref[rows + 2 * point]
            - last_on * table_ref[rows + 2 * point + 1]
        )
        onsite_im.append(
            broaden
            + first_on * table_ref[rows + 2 * points + 2 * point]
            + last_on * table_ref[rows + 2 * points + 2 * point + 1]
        )
    return jnp.stack(onsite_re), jnp.stack(onsite_im)


def summary_kernel(here_ref, length_ref, energy_ref, table_ref, out_ref, *, slots, points, devices):
    here = here_ref[0]
    count = length_ref[here]

    def single(slot):
        onsite_re, onsite_im = onsite_terms(
            table_ref, energy_ref, here, count, devices, slots, points, slot
        )
        g_re, g_im = reciprocal(onsite_re, onsite_im)
        return (g_re, g_im, g_re, g_im, g_re, g_im, table_ref[slots + slot])

    def body(slot, summary):
        return join_segments(summary, single(slot))

    first_re, first_im, cross_re, cross_im, final_re, final_im, coupling = lax.fori_loop(
        1, count, body, single(0)
    )
    square = coupling * coupling
    sq_re, sq_im = complex_mul(cross_re, cross_im, cross_re, cross_im)
    fields = (first_re, first_im, square * final_re, square * final_im, square * sq_re, square * sq_im)
    for index, value in enumerate(fields):
        out_ref[index * points:(index + 1) * points] = value


def join_coupled(left, right):
    d_re, d_im = complex_mul(left[2], left[3], right[0], right[1])
    inv_re, inv_im = reciprocal(1.0 - d_re, -d_im)
    f_re, f_im = complex_mul(left[4], left[5], right[0], right[1])
    f_re, f_im = complex_mul(f_re, f_im, inv_re, inv_im)
    g_re, g_im = complex_mul(right[4], right[5], left[2], left[3])
    g_re, g_im = complex_mul(g_re, g_im, inv_re, inv_im)
    x_re, x_im = complex_mul(left[4], left[5], right[4], right[5])
    x_re, x_im = complex_mul(x_re, x_im, inv_re, inv_im)
    x_re, x_im = complex_mul(x_re, x_im, inv_re, inv_im)
    return (left[0] + f_re, left[1] + f_im, right[2] + g_re, right[3] + g_im, x_re, x_im)


def group_kernel(here_ref, local_ref, out_ref):
    points = local_ref.shape[1] // 6
    size = local_ref.shape[0]
    here = here_ref[0]

    def block(member):
        index = jnp.bitwise_xor(member, jnp.bitwise_and(here, size - 1))
        return tuple(local_ref[index, f * points:(f + 1) * points] for f in range(6))

    def body(member, summary):
        return join_coupled(summary, block(member))

    summary = lax.fori_loop(1, size, body, block(0))
    for index, value in enumerate(summary):
        out_ref[index * points:(index + 1) * points] = value


def final_kernel(here_ref, length_ref, energy_ref, code_ref, local_ref, group_ref, table_ref,
                 low_ref, high_ref, left_re_ref, left_im_ref, dens_ref, bond_ref, *,
                 slots, points, devices, mixed, scale):
    size = local_ref.shape[0]
    groups = group_ref.shape[0]
    here = here_ref[0]
    count = length_ref[here]
    rows = table_ref.shape[1]
    member_here = here % size
    group_here = here // size

    def field(ref, index_of, position, index):
        return ref[index_of(position), index * points:(index + 1) * points]

    def local_index(member):
        return jnp.bitwise_xor(member, member_here) if mixed else member

    def group_index(group):
        return jnp.bitwise_xor(group, group_here) if mixed else group

    def into_step(ref, index_of):
        def body(position, run):
            run_re, run_im = run
            m_re, m_im = complex_mul(run_re, run_im, field(ref, index_of, position, 0), field(ref, index_of, position, 1))
            inv_re, inv_im = reciprocal(1.0 - m_re, -m_im)
            t_re, t_im = complex_mul(field(ref, index_of, position, 4), field(ref, index_of, position, 5), run_re, run_im)
            t_re, t_im = complex_mul(t_re, t_im, inv_re, inv_im)
            return (field(ref, index_of, position, 2) + t_re, field(ref, index_of, position, 3) + t_im)
        return body

    def from_step(ref, index_of, last):
        def body(step, run):
            run_re, run_im = run
            position = last - step
            m_re, m_im = complex_mul(field(ref, index_of, position, 2), field(ref, index_of, position, 3), run_re, run_im)
            inv_re, inv_im = reciprocal(1.0 - m_re, -m_im)
            h_re, h_im = complex_mul(field(ref, index_of, position, 4), field(ref, index_of, position, 5), run_re, run_im)
            h_re, h_im = complex_mul(h_re, h_im, inv_re, inv_im)
            return (field(ref, index_of, position, 0) + h_re, field(ref, index_of, position, 1) + h_im)
        return body

    zero = jnp.zeros((points,) + table_ref.shape[1:], jnp.float32)
    into = lax.fori_loop(0, group_here, into_step(group_ref, group_index), (zero, zero))
    into_re, into_im = lax.fori_loop(0, member_here, into_step(local_ref, local_index), into)
    outof = lax.fori_loop(0, groups - 1 - group_here, from_step(group_ref, group_index, groups - 1), (zero, zero))
    from_re, from_im = lax.fori_loop(
        0, size - 1 - member_here, from_step(local_ref, local_index, size - 1), outof
    )

    def onsite(slot):
        return onsite_terms(table_ref, energy_ref, here, count, devices, slots, points, slot)

    def forward_body(slot, carry):
        prev_re, prev_im, prev_coupling = carry
        onsite_re, onsite_im = onsite(slot)
        square = prev_coupling * prev_coupling
        g_re, g_im = reciprocal(onsite_re - square * prev_re, onsite_im - square * prev_im)
        left_re_ref[slot] = g_re
        left_im_ref[slot] = g_im
        return (g_re, g_im, table_ref[slots + slot])

    ones = jnp.ones(table_ref.shape[1:], jnp.float32)
    lax.fori_loop(0, count, forward_body, (into_re, into_im, ones))
    dens_ref[...] = jnp.zeros(dens_ref.shape, jnp.float32)
    bond_ref[...] = jnp.zeros(bond_ref.shape, jnp.float32)
    weights = [code_ref[point].astype(jnp.float32) * scale for point in range(points)]

    def backward_body(step, carry):
        next_re, next_im = carry
        slot = count - 1 - step
        onsite_re, onsite_im = onsite(slot)
        left_re, left_im = left_re_ref[slot], left_im_ref[slot]
        coupling = table_ref[slots + slot]
        square = coupling * coupling
        mix_re, mix_im = complex_mul(left_re, left_im, next_re, next_im)
        inv_re, inv_im = reciprocal(1.0 - square * mix_re, -square * mix_im)
        diag_re, diag_im = complex_mul(left_re, left_im, inv_re, inv_im)
        _, bond_im = complex_mul(diag_re, diag_im, next_re, next_im)
        dens = weights[0] * diag_im[0]
        bond = weights[0] * (square * bond_im[0])
        for point in range(1, points):
            dens = dens + weights[point] * diag_im[point]
            bond = bond + weights[point] * (square * bond_im[point])
        dens_ref[slot] = -inv_pi * dens
        bond_ref[slot] = -2.0 * inv_pi * bond
        return reciprocal(onsite_re - square * next_re, onsite_im - square * next_im)

    lax.fori_loop(0, count, backward_body, (from_re, from_im))
    for slot in range(slots):
        dens = dens_ref[slot]
        bond = bond_ref[slot]
        for row in range(rows):
            target = low_ref if row < rows // 2 else high_ref
            lane = (row % (rows // 2)) * 128
            target[0, slot:slot + 1, lane:lane + 128] = dens[row:row + 1]
            target[1, slot:slot + 1, lane:lane + 128] = bond[row:row + 1]


def shards(
    mode_floor, onsite_noise, hopping, lengths, energy_index, weight_code, lead_shift, lead_width
):
    slots = onsite_noise.shape[0]
    modes = onsite_noise.shape[1]
    points = energy_index.shape[0]
    rows = modes // 128
    here = lax.axis_index("slab")
    devices = lax.axis_size("slab")
    groups = lax.axis_size("energy")
    table = jnp.concatenate(
        [
            mode_floor[None, :] + onsite_noise,
            hopping,
            lead_shift.reshape(2 * points, modes),
            lead_width.reshape(2 * points, modes),
        ],
        axis=0,
    ).reshape(2 * slots + 4 * points, rows, 128)
    here_arr = here.astype(jnp.int32).reshape(1)
    smem = pl.BlockSpec(memory_space=pltpu.SMEM)
    vmem = pl.BlockSpec(memory_space=pltpu.VMEM)

    packed = pl.pallas_call(
        functools.partial(summary_kernel, slots=slots, points=points, devices=devices),
        out_shape=jax.ShapeDtypeStruct((6 * points, rows, 128), jnp.float32),
        in_specs=[smem, smem, smem, vmem],
        out_specs=vmem,
    )(here_arr, lengths, energy_index, table)
    mixed = devices & (devices - 1) == 0 and devices >= 4
    if mixed:
        size = 4
        local = packed[None]
        for distance in (1, 2):
            pairs = [(device, device ^ distance) for device in range(devices)]
            local = jnp.concatenate([local, lax.ppermute(local, "slab", pairs)], axis=0)
        summary = pl.pallas_call(
            group_kernel,
            out_shape=jax.ShapeDtypeStruct(packed.shape, jnp.float32),
            in_specs=[smem, vmem],
            out_specs=vmem,
        )(here_arr, local)
        every = summary[None]
        distance = size
        while distance < devices:
            pairs = [(device, device ^ distance) for device in range(devices)]
            every = jnp.concatenate([every, lax.ppermute(every, "slab", pairs)], axis=0)
            distance *= 2
    else:
        size = devices
        local = lax.all_gather(packed, "slab")
        every = jnp.zeros((1,) + packed.shape, jnp.float32)
    half = jax.ShapeDtypeStruct((2, slots, modes // 2), jnp.float32)
    low, high = pl.pallas_call(
        functools.partial(
            final_kernel, slots=slots, points=points, devices=devices, mixed=mixed,
            scale=1.0 / (32.0 * points * groups),
        ),
        out_shape=(half, half),
        in_specs=[smem, smem, smem, smem, vmem, vmem, vmem],
        out_specs=(vmem, vmem),
        scratch_shapes=[
            pltpu.VMEM((slots, points, rows, 128), jnp.float32),
            pltpu.VMEM((slots, points, rows, 128), jnp.float32),
            pltpu.VMEM((slots, rows, 128), jnp.float32),
            pltpu.VMEM((slots, rows, 128), jnp.float32),
        ],
    )(here_arr, lengths, energy_index, weight_code, local, every, table)
    if groups == 2:
        lower = lax.axis_index("energy") == 0
        mine = jnp.where(lower, low, high)
        theirs = jnp.where(lower, high, low)
        both = mine + lax.ppermute(theirs, "energy", [(0, 1), (1, 0)])
    else:
        both = lax.psum_scatter(
            jnp.concatenate([low, high], axis=2), "energy", scatter_dimension=2, tiled=True
        )
    return (both[0], both[1])


def solution(mesh):
    in_specs = (
        P(),
        P("slab", None),
        P("slab", None),
        P(),
        P("energy"),
        P("energy"),
        P("energy", None, None),
        P("energy", None, None),
    )
    out_specs = (P("slab", "energy"), P("slab", "energy"))
    return jax.shard_map(shards, mesh=mesh, in_specs=in_specs, out_specs=out_specs, check_vma=False)
```

```python
import functools

import jax
import jax.numpy as jnp
from jax import lax
from jax.experimental import pallas as pl
from jax.experimental.pallas import tpu as pltpu
from jax.sharding import PartitionSpec as P

broaden = 0.002
e_low = -1.5
e_step = 3.0 / 4096.0
inv_pi = 1.0 / 3.141592653589793


def reciprocal(real_part, imag_part):
    norm = real_part * real_part + imag_part * imag_part
    return (real_part / norm, -imag_part / norm)


def complex_mul(first_re, first_im, second_re, second_im):
    return (
        first_re * second_re - first_im * second_im,
        first_re * second_im + first_im * second_re,
    )


def join_segments(left, right):
    square = left[6] * left[6]
    mix_re, mix_im = complex_mul(left[4], left[5], right[0], right[1])
    inv_re, inv_im = reciprocal(1.0 - square * mix_re, -square * mix_im)
    left_sq_re, left_sq_im = complex_mul(left[2], left[3], left[2], left[3])
    head_re, head_im = complex_mul(left_sq_re, left_sq_im, right[0], right[1])
    head_re, head_im = complex_mul(head_re, head_im, inv_re, inv_im)
    right_sq_re, right_sq_im = complex_mul(right[2], right[3], right[2], right[3])
    tail_re, tail_im = complex_mul(right_sq_re, right_sq_im, left[4], left[5])
    tail_re, tail_im = complex_mul(tail_re, tail_im, inv_re, inv_im)
    link_re, link_im = complex_mul(left[2], left[3], right[2], right[3])
    link_re, link_im = complex_mul(link_re, link_im, inv_re, inv_im)
    return (
        left[0] + square * head_re,
        left[1] + square * head_im,
        left[6] * link_re,
        left[6] * link_im,
        right[4] + square * tail_re,
        right[5] + square * tail_im,
        right[6],
    )


def onsite_terms(table_ref, energy_ref, here, count, devices, slots, points, slot):
    rows = 2 * slots
    levels = table_ref[slot]
    first_on = jnp.logical_and(here == 0, slot == 0).astype(jnp.float32)
    last_on = jnp.logical_and(here == devices - 1, slot == count - 1).astype(jnp.float32)
    onsite_re, onsite_im = [], []
    for point in range(points):
        energy = e_low + e_step * energy_ref[point].astype(jnp.float32)
        onsite_re.append(
            energy - levels
            - first_on * table_ref[rows + 2 * point]
            - last_on * table_ref[rows + 2 * point + 1]
        )
        onsite_im.append(
            broaden
            + first_on * table_ref[rows + 2 * points + 2 * point]
            + last_on * table_ref[rows + 2 * points + 2 * point + 1]
        )
    return jnp.stack(onsite_re), jnp.stack(onsite_im)


def summary_kernel(here_ref, length_ref, energy_ref, table_ref, out_ref, *, slots, points, devices):
    here = here_ref[0]
    count = length_ref[here]

    def single(slot):
        onsite_re, onsite_im = onsite_terms(
            table_ref, energy_ref, here, count, devices, slots, points, slot
        )
        g_re, g_im = reciprocal(onsite_re, onsite_im)
        return (g_re, g_im, g_re, g_im, g_re, g_im, table_ref[slots + slot])

    def body(slot, summary):
        return join_segments(summary, single(slot))

    first_re, first_im, cross_re, cross_im, final_re, final_im, coupling = lax.fori_loop(
        1, count, body, single(0)
    )
    square = coupling * coupling
    sq_re, sq_im = complex_mul(cross_re, cross_im, cross_re, cross_im)
    fields = (first_re, first_im, square * final_re, square * final_im, square * sq_re, square * sq_im)
    for index, value in enumerate(fields):
        out_ref[index * points:(index + 1) * points] = value


def join_coupled(left, right):
    d_re, d_im = complex_mul(left[2], left[3], right[0], right[1])
    inv_re, inv_im = reciprocal(1.0 - d_re, -d_im)
    f_re, f_im = complex_mul(left[4], left[5], right[0], right[1])
    f_re, f_im = complex_mul(f_re, f_im, inv_re, inv_im)
    g_re, g_im = complex_mul(right[4], right[5], left[2], left[3])
    g_re, g_im = complex_mul(g_re, g_im, inv_re, inv_im)
    x_re, x_im = complex_mul(left[4], left[5], right[4], right[5])
    x_re, x_im = complex_mul(x_re, x_im, inv_re, inv_im)
    x_re, x_im = complex_mul(x_re, x_im, inv_re, inv_im)
    return (left[0] + f_re, left[1] + f_im, right[2] + g_re, right[3] + g_im, x_re, x_im)


def group_kernel(here_ref, local_ref, out_ref):
    points = local_ref.shape[1] // 6
    size = local_ref.shape[0]
    here = here_ref[0]

    def block(member):
        index = jnp.bitwise_xor(member, jnp.bitwise_and(here, size - 1))
        return tuple(local_ref[index, f * points:(f + 1) * points] for f in range(6))

    def body(member, summary):
        return join_coupled(summary, block(member))

    summary = lax.fori_loop(1, size, body, block(0))
    for index, value in enumerate(summary):
        out_ref[index * points:(index + 1) * points] = value


def final_kernel(here_ref, length_ref, energy_ref, code_ref, local_ref, group_ref, table_ref,
                 low_ref, high_ref, left_re_ref, left_im_ref, dens_ref, bond_ref, *,
                 slots, points, devices, mixed, scale):
    size = local_ref.shape[0]
    groups = group_ref.shape[0]
    here = here_ref[0]
    count = length_ref[here]
    rows = table_ref.shape[1]
    member_here = here % size
    group_here = here // size

    def field(ref, index_of, position, index):
        return ref[index_of(position), index * points:(index + 1) * points]

    def local_index(member):
        return jnp.bitwise_xor(member, member_here) if mixed else member

    def group_index(group):
        return jnp.bitwise_xor(group, group_here) if mixed else group

    def into_step(ref, index_of):
        def body(position, run):
            run_re, run_im = run
            m_re, m_im = complex_mul(run_re, run_im, field(ref, index_of, position, 0), field(ref, index_of, position, 1))
            inv_re, inv_im = reciprocal(1.0 - m_re, -m_im)
            t_re, t_im = complex_mul(field(ref, index_of, position, 4), field(ref, index_of, position, 5), run_re, run_im)
            t_re, t_im = complex_mul(t_re, t_im, inv_re, inv_im)
            return (field(ref, index_of, position, 2) + t_re, field(ref, index_of, position, 3) + t_im)
        return body

    def from_step(ref, index_of, last):
        def body(step, run):
            run_re, run_im = run
            position = last - step
            m_re, m_im = complex_mul(field(ref, index_of, position, 2), field(ref, index_of, position, 3), run_re, run_im)
            inv_re, inv_im = reciprocal(1.0 - m_re, -m_im)
            h_re, h_im = complex_mul(field(ref, index_of, position, 4), field(ref, index_of, position, 5), run_re, run_im)
            h_re, h_im = complex_mul(h_re, h_im, inv_re, inv_im)
            return (field(ref, index_of, position, 0) + h_re, field(ref, index_of, position, 1) + h_im)
        return body

    zero = jnp.zeros((points,) + table_ref.shape[1:], jnp.float32)
    into = lax.fori_loop(0, group_here, into_step(group_ref, group_index), (zero, zero))
    into_re, into_im = lax.fori_loop(0, member_here, into_step(local_ref, local_index), into)
    outof = lax.fori_loop(0, groups - 1 - group_here, from_step(group_ref, group_index, groups - 1), (zero, zero))
    from_re, from_im = lax.fori_loop(
        0, size - 1 - member_here, from_step(local_ref, local_index, size - 1), outof
    )

    def onsite(slot):
        return onsite_terms(table_ref, energy_ref, here, count, devices, slots, points, slot)

    def forward_body(slot, carry):
        prev_re, prev_im, prev_coupling = carry
        onsite_re, onsite_im = onsite(slot)
        square = prev_coupling * prev_coupling
        g_re, g_im = reciprocal(onsite_re - square * prev_re, onsite_im - square * prev_im)
        left_re_ref[slot] = g_re
        left_im_ref[slot] = g_im
        return (g_re, g_im, table_ref[slots + slot])

    ones = jnp.ones(table_ref.shape[1:], jnp.float32)
    lax.fori_loop(0, count, forward_body, (into_re, into_im, ones))
    dens_ref[...] = jnp.zeros(dens_ref.shape, jnp.float32)
    bond_ref[...] = jnp.zeros(bond_ref.shape, jnp.float32)
    weights = [code_ref[point].astype(jnp.float32) * scale for point in range(points)]

    def backward_body(step, carry):
        next_re, next_im = carry
        slot = count - 1 - step
        onsite_re, onsite_im = onsite(slot)
        left_re, left_im = left_re_ref[slot], left_im_ref[slot]
        coupling = table_ref[slots + slot]
        square = coupling * coupling
        mix_re, mix_im = complex_mul(left_re, left_im, next_re, next_im)
        inv_re, inv_im = reciprocal(1.0 - square * mix_re, -square * mix_im)
        diag_re, diag_im = complex_mul(left_re, left_im, inv_re, inv_im)
        _, bond_im = complex_mul(diag_re, diag_im, next_re, next_im)
        dens = weights[0] * diag_im[0]
        bond = weights[0] * (square * bond_im[0])
        for point in range(1, points):
            dens = dens + weights[point] * diag_im[point]
            bond = bond + weights[point] * (square * bond_im[point])
        dens_ref[slot] = -inv_pi * dens
        bond_ref[slot] = -2.0 * inv_pi * bond
        return reciprocal(onsite_re - square * next_re, onsite_im - square * next_im)

    lax.fori_loop(0, count, backward_body, (from_re, from_im))
    for slot in range(slots):
        dens = dens_ref[slot]
        bond = bond_ref[slot]
        for row in range(rows):
            target = low_ref if row < rows // 2 else high_ref
            lane = (row % (rows // 2)) * 128
            target[0, slot:slot + 1, lane:lane + 128] = dens[row:row + 1]
            target[1, slot:slot + 1, lane:lane + 128] = bond[row:row + 1]


def shards(
    mode_floor, onsite_noise, hopping, lengths, energy_index, weight_code, lead_shift, lead_width
):
    slots = onsite_noise.shape[0]
    modes = onsite_noise.shape[1]
    points = energy_index.shape[0]
    rows = modes // 128
    here = lax.axis_index("slab")
    devices = lax.axis_size("slab")
    groups = lax.axis_size("energy")
    table = jnp.concatenate(
        [
            mode_floor[None, :] + onsite_noise,
            hopping,
            lead_shift.reshape(2 * points, modes),
            lead_width.reshape(2 * points, modes),
        ],
        axis=0,
    ).reshape(2 * slots + 4 * points, rows, 128)
    here_arr = here.astype(jnp.int32).reshape(1)
    smem = pl.BlockSpec(memory_space=pltpu.SMEM)
    vmem = pl.BlockSpec(memory_space=pltpu.VMEM)

    packed = pl.pallas_call(
        functools.partial(summary_kernel, slots=slots, points=points, devices=devices),
        out_shape=jax.ShapeDtypeStruct((6 * points, rows, 128), jnp.float32),
        in_specs=[smem, smem, smem, vmem],
        out_specs=vmem,
    )(here_arr, lengths, energy_index, table)
    mixed = devices & (devices - 1) == 0 and devices >= 4
    if mixed:
        size = 4
        local = jnp.stack([packed] + [
            lax.ppermute(packed, "slab", [(device, device ^ offset) for device in range(devices)])
            for offset in range(1, size)
        ])
        summary = pl.pallas_call(
            group_kernel,
            out_shape=jax.ShapeDtypeStruct(packed.shape, jnp.float32),
            in_specs=[smem, vmem],
            out_specs=vmem,
        )(here_arr, local)
        if devices == size * size:
            every = jnp.stack([summary] + [
                lax.ppermute(summary, "slab", [(device, device ^ (offset * size)) for device in range(devices)])
                for offset in range(1, size)
            ])
        else:
            every = summary[None]
            distance = size
            while distance < devices:
                pairs = [(device, device ^ distance) for device in range(devices)]
                every = jnp.concatenate([every, lax.ppermute(every, "slab", pairs)], axis=0)
                distance *= 2
    else:
        size = devices
        local = lax.all_gather(packed, "slab")
        every = jnp.zeros((1,) + packed.shape, jnp.float32)
    half = jax.ShapeDtypeStruct((2, slots, modes // 2), jnp.float32)
    low, high = pl.pallas_call(
        functools.partial(
            final_kernel, slots=slots, points=points, devices=devices, mixed=mixed,
            scale=1.0 / (32.0 * points * groups),
        ),
        out_shape=(half, half),
        in_specs=[smem, smem, smem, smem, vmem, vmem, vmem],
        out_specs=(vmem, vmem),
        scratch_shapes=[
            pltpu.VMEM((slots, points, rows, 128), jnp.float32),
            pltpu.VMEM((slots, points, rows, 128), jnp.float32),
            pltpu.VMEM((slots, rows, 128), jnp.float32),
            pltpu.VMEM((slots, rows, 128), jnp.float32),
        ],
    )(here_arr, lengths, energy_index, weight_code, local, every, table)
    if groups == 2:
        lower = lax.axis_index("energy") == 0
        mine = jnp.where(lower, low, high)
        theirs = jnp.where(lower, high, low)
        both = mine + lax.ppermute(theirs, "energy", [(0, 1), (1, 0)])
    else:
        both = lax.psum_scatter(
            jnp.concatenate([low, high], axis=2), "energy", scatter_dimension=2, tiled=True
        )
    return (both[0], both[1])


def solution(mesh):
    in_specs = (
        P(),
        P("slab", None),
        P("slab", None),
        P(),
        P("energy"),
        P("energy"),
        P("energy", None, None),
        P("energy", None, None),
    )
    out_specs = (P("slab", "energy"), P("slab", "energy"))
    return jax.shard_map(shards, mesh=mesh, in_specs=in_specs, out_specs=out_specs, check_vma=False)
```

```python
import functools

import jax
import jax.numpy as jnp
from jax import lax
from jax.experimental import pallas as pl
from jax.experimental.pallas import tpu as pltpu
from jax.sharding import PartitionSpec as P

broaden = 0.002
e_low = -1.5
e_step = 3.0 / 4096.0
inv_pi = 1.0 / 3.141592653589793


def reciprocal(real_part, imag_part):
    norm = real_part * real_part + imag_part * imag_part
    return (real_part / norm, -imag_part / norm)


def complex_mul(first_re, first_im, second_re, second_im):
    return (
        first_re * second_re - first_im * second_im,
        first_re * second_im + first_im * second_re,
    )


def join_segments(left, right):
    square = left[6] * left[6]
    mix_re, mix_im = complex_mul(left[4], left[5], right[0], right[1])
    inv_re, inv_im = reciprocal(1.0 - square * mix_re, -square * mix_im)
    left_sq_re, left_sq_im = complex_mul(left[2], left[3], left[2], left[3])
    head_re, head_im = complex_mul(left_sq_re, left_sq_im, right[0], right[1])
    head_re, head_im = complex_mul(head_re, head_im, inv_re, inv_im)
    right_sq_re, right_sq_im = complex_mul(right[2], right[3], right[2], right[3])
    tail_re, tail_im = complex_mul(right_sq_re, right_sq_im, left[4], left[5])
    tail_re, tail_im = complex_mul(tail_re, tail_im, inv_re, inv_im)
    link_re, link_im = complex_mul(left[2], left[3], right[2], right[3])
    link_re, link_im = complex_mul(link_re, link_im, inv_re, inv_im)
    return (
        left[0] + square * head_re,
        left[1] + square * head_im,
        left[6] * link_re,
        left[6] * link_im,
        right[4] + square * tail_re,
        right[5] + square * tail_im,
        right[6],
    )


def onsite_terms(table_ref, energy_ref, here, count, devices, slots, points, slot):
    rows = 2 * slots
    levels = table_ref[slot]
    first_on = jnp.logical_and(here == 0, slot == 0).astype(jnp.float32)
    last_on = jnp.logical_and(here == devices - 1, slot == count - 1).astype(jnp.float32)
    onsite_re, onsite_im = [], []
    for point in range(points):
        energy = e_low + e_step * energy_ref[point].astype(jnp.float32)
        onsite_re.append(
            energy - levels
            - first_on * table_ref[rows + 2 * point]
            - last_on * table_ref[rows + 2 * point + 1]
        )
        onsite_im.append(
            broaden
            + first_on * table_ref[rows + 2 * points + 2 * point]
            + last_on * table_ref[rows + 2 * points + 2 * point + 1]
        )
    return jnp.stack(onsite_re), jnp.stack(onsite_im)


def summary_kernel(here_ref, length_ref, energy_ref, table_ref, out_ref, *, slots, points, devices):
    here = here_ref[0]
    count = length_ref[here]

    def single(slot):
        onsite_re, onsite_im = onsite_terms(
            table_ref, energy_ref, here, count, devices, slots, points, slot
        )
        g_re, g_im = reciprocal(onsite_re, onsite_im)
        return (g_re, g_im, g_re, g_im, g_re, g_im, table_ref[slots + slot])

    def body(slot, summary):
        return join_segments(summary, single(slot))

    first_re, first_im, cross_re, cross_im, final_re, final_im, coupling = lax.fori_loop(
        1, count, body, single(0)
    )
    square = coupling * coupling
    sq_re, sq_im = complex_mul(cross_re, cross_im, cross_re, cross_im)
    fields = (first_re, first_im, square * final_re, square * final_im, square * sq_re, square * sq_im)
    for index, value in enumerate(fields):
        out_ref[index * points:(index + 1) * points] = value


def join_coupled(left, right):
    d_re, d_im = complex_mul(left[2], left[3], right[0], right[1])
    inv_re, inv_im = reciprocal(1.0 - d_re, -d_im)
    f_re, f_im = complex_mul(left[4], left[5], right[0], right[1])
    f_re, f_im = complex_mul(f_re, f_im, inv_re, inv_im)
    g_re, g_im = complex_mul(right[4], right[5], left[2], left[3])
    g_re, g_im = complex_mul(g_re, g_im, inv_re, inv_im)
    x_re, x_im = complex_mul(left[4], left[5], right[4], right[5])
    x_re, x_im = complex_mul(x_re, x_im, inv_re, inv_im)
    x_re, x_im = complex_mul(x_re, x_im, inv_re, inv_im)
    return (left[0] + f_re, left[1] + f_im, right[2] + g_re, right[3] + g_im, x_re, x_im)


def in_order(refs, own, mixed):
    loaded = [ref[...] for ref in refs]
    if not mixed:
        return loaded
    ordered = []
    for position in range(len(refs)):
        offset = jnp.bitwise_xor(own, position)
        value = loaded[0]
        for index in range(1, len(refs)):
            value = jnp.where(offset == index, loaded[index], value)
        ordered.append(value)
    return ordered


def split_fields(value, points):
    return tuple(value[f * points:(f + 1) * points] for f in range(6))


def group_kernel(here_ref, *refs):
    local_refs, out_ref = refs[:-1], refs[-1]
    points = out_ref.shape[0] // 6
    size = len(local_refs)
    here = here_ref[0]
    blocks = in_order(local_refs, jnp.bitwise_and(here, size - 1), True)
    summary = split_fields(blocks[0], points)
    for member in range(1, size):
        summary = join_coupled(summary, split_fields(blocks[member], points))
    for index, value in enumerate(summary):
        out_ref[index * points:(index + 1) * points] = value


def final_kernel(here_ref, length_ref, energy_ref, code_ref, *refs,
                 slots, points, devices, mixed, size, groups, scale):
    local_refs = refs[:size]
    group_refs = refs[size:size + groups]
    table_ref, low_ref, high_ref, left_re_ref, left_im_ref, dens_ref, bond_ref = refs[size + groups:]
    here = here_ref[0]
    count = length_ref[here]
    rows = table_ref.shape[1]
    member_here = here % size
    group_here = here // size

    def into_step(block, run):
        run_re, run_im = run
        m_re, m_im = complex_mul(run_re, run_im, block[0], block[1])
        inv_re, inv_im = reciprocal(1.0 - m_re, -m_im)
        t_re, t_im = complex_mul(block[4], block[5], run_re, run_im)
        t_re, t_im = complex_mul(t_re, t_im, inv_re, inv_im)
        return (block[2] + t_re, block[3] + t_im)

    def from_step(block, run):
        run_re, run_im = run
        m_re, m_im = complex_mul(block[2], block[3], run_re, run_im)
        inv_re, inv_im = reciprocal(1.0 - m_re, -m_im)
        h_re, h_im = complex_mul(block[4], block[5], run_re, run_im)
        h_re, h_im = complex_mul(h_re, h_im, inv_re, inv_im)
        return (block[0] + h_re, block[1] + h_im)

    def masked(keep, new, old):
        return tuple(jnp.where(keep, n, o) for n, o in zip(new, old))

    zero = jnp.zeros((points,) + table_ref.shape[1:], jnp.float32)
    group_blocks = [split_fields(v, points) for v in in_order(group_refs, group_here, mixed)]
    local_blocks = [split_fields(v, points) for v in in_order(local_refs, member_here, mixed)]
    into = (zero, zero)
    for group in range(groups):
        into = masked(group < group_here, into_step(group_blocks[group], into), into)
    for member in range(size):
        into = masked(member < member_here, into_step(local_blocks[member], into), into)
    outof = (zero, zero)
    for group in reversed(range(groups)):
        outof = masked(group > group_here, from_step(group_blocks[group], outof), outof)
    for member in reversed(range(size)):
        outof = masked(member > member_here, from_step(local_blocks[member], outof), outof)
    into_re, into_im = into
    from_re, from_im = outof

    def onsite(slot):
        return onsite_terms(table_ref, energy_ref, here, count, devices, slots, points, slot)

    def forward_body(slot, carry):
        prev_re, prev_im, prev_coupling = carry
        onsite_re, onsite_im = onsite(slot)
        square = prev_coupling * prev_coupling
        g_re, g_im = reciprocal(onsite_re - square * prev_re, onsite_im - square * prev_im)
        left_re_ref[slot] = g_re
        left_im_ref[slot] = g_im
        return (g_re, g_im, table_ref[slots + slot])

    ones = jnp.ones(table_ref.shape[1:], jnp.float32)
    lax.fori_loop(0, count, forward_body, (into_re, into_im, ones))
    dens_ref[...] = jnp.zeros(dens_ref.shape, jnp.float32)
    bond_ref[...] = jnp.zeros(bond_ref.shape, jnp.float32)
    weights = [code_ref[point].astype(jnp.float32) * scale for point in range(points)]

    def backward_body(step, carry):
        next_re, next_im = carry
        slot = count - 1 - step
        onsite_re, onsite_im = onsite(slot)
        left_re, left_im = left_re_ref[slot], left_im_ref[slot]
        coupling = table_ref[slots + slot]
        square = coupling * coupling
        mix_re, mix_im = complex_mul(left_re, left_im, next_re, next_im)
        inv_re, inv_im = reciprocal(1.0 - square * mix_re, -square * mix_im)
        diag_re, diag_im = complex_mul(left_re, left_im, inv_re, inv_im)
        _, bond_im = complex_mul(diag_re, diag_im, next_re, next_im)
        dens = weights[0] * diag_im[0]
        bond = weights[0] * (square * bond_im[0])
        for point in range(1, points):
            dens = dens + weights[point] * diag_im[point]
            bond = bond + weights[point] * (square * bond_im[point])
        dens_ref[slot] = -inv_pi * dens
        bond_ref[slot] = -2.0 * inv_pi * bond
        return reciprocal(onsite_re - square * next_re, onsite_im - square * next_im)

    lax.fori_loop(0, count, backward_body, (from_re, from_im))
    for slot in range(slots):
        dens = dens_ref[slot]
        bond = bond_ref[slot]
        for row in range(rows):
            target = low_ref if row < rows // 2 else high_ref
            lane = (row % (rows // 2)) * 128
            target[0, slot:slot + 1, lane:lane + 128] = dens[row:row + 1]
            target[1, slot:slot + 1, lane:lane + 128] = bond[row:row + 1]


def shards(
    mode_floor, onsite_noise, hopping, lengths, energy_index, weight_code, lead_shift, lead_width
):
    slots = onsite_noise.shape[0]
    modes = onsite_noise.shape[1]
    points = energy_index.shape[0]
    rows = modes // 128
    here = lax.axis_index("slab")
    devices = lax.axis_size("slab")
    groups = lax.axis_size("energy")
    table = jnp.concatenate(
        [
            mode_floor[None, :] + onsite_noise,
            hopping,
            lead_shift.reshape(2 * points, modes),
            lead_width.reshape(2 * points, modes),
        ],
        axis=0,
    ).reshape(2 * slots + 4 * points, rows, 128)
    here_arr = here.astype(jnp.int32).reshape(1)
    smem = pl.BlockSpec(memory_space=pltpu.SMEM)
    vmem = pl.BlockSpec(memory_space=pltpu.VMEM)

    packed = pl.pallas_call(
        functools.partial(summary_kernel, slots=slots, points=points, devices=devices),
        out_shape=jax.ShapeDtypeStruct((6 * points, rows, 128), jnp.float32),
        in_specs=[smem, smem, smem, vmem],
        out_specs=vmem,
    )(here_arr, lengths, energy_index, table)
    mixed = devices & (devices - 1) == 0 and devices >= 4
    if mixed:
        size = 4
        local = [packed] + [
            lax.ppermute(packed, "slab", [(device, device ^ offset) for device in range(devices)])
            for offset in range(1, size)
        ]
        summary = pl.pallas_call(
            group_kernel,
            out_shape=jax.ShapeDtypeStruct(packed.shape, jnp.float32),
            in_specs=[smem] + [vmem] * size,
            out_specs=vmem,
        )(here_arr, *local)
        if devices == size * size:
            every = [summary] + [
                lax.ppermute(summary, "slab", [(device, device ^ (offset * size)) for device in range(devices)])
                for offset in range(1, size)
            ]
        else:
            stacked = summary[None]
            distance = size
            while distance < devices:
                pairs = [(device, device ^ distance) for device in range(devices)]
                stacked = jnp.concatenate([stacked, lax.ppermute(stacked, "slab", pairs)], axis=0)
                distance *= 2
            every = [stacked[index] for index in range(devices // size)]
    else:
        size = devices
        gathered = lax.all_gather(packed, "slab")
        local = [gathered[index] for index in range(devices)]
        every = [jnp.zeros(packed.shape, jnp.float32)]
    half = jax.ShapeDtypeStruct((2, slots, modes // 2), jnp.float32)
    low, high = pl.pallas_call(
        functools.partial(
            final_kernel, slots=slots, points=points, devices=devices, mixed=mixed,
            size=len(local), groups=len(every), scale=1.0 / (32.0 * points * groups),
        ),
        out_shape=(half, half),
        in_specs=[smem] * 4 + [vmem] * (len(local) + len(every) + 1),
        out_specs=(vmem, vmem),
        scratch_shapes=[
            pltpu.VMEM((slots, points, rows, 128), jnp.float32),
            pltpu.VMEM((slots, points, rows, 128), jnp.float32),
            pltpu.VMEM((slots, rows, 128), jnp.float32),
            pltpu.VMEM((slots, rows, 128), jnp.float32),
        ],
    )(here_arr, lengths, energy_index, weight_code, *local, *every, table)
    if groups == 2:
        lower = lax.axis_index("energy") == 0
        mine = jnp.where(lower, low, high)
        theirs = jnp.where(lower, high, low)
        both = mine + lax.ppermute(theirs, "energy", [(0, 1), (1, 0)])
    else:
        both = lax.psum_scatter(
            jnp.concatenate([low, high], axis=2), "energy", scatter_dimension=2, tiled=True
        )
    return (both[0], both[1])


def solution(mesh):
    in_specs = (
        P(),
        P("slab", None),
        P("slab", None),
        P(),
        P("energy"),
        P("energy"),
        P("energy", None, None),
        P("energy", None, None),
    )
    out_specs = (P("slab", "energy"), P("slab", "energy"))
    return jax.shard_map(shards, mesh=mesh, in_specs=in_specs, out_specs=out_specs, check_vma=False)
```

```python
import functools

import jax
import jax.numpy as jnp
from jax import lax
from jax.experimental import pallas as pl
from jax.experimental.pallas import tpu as pltpu
from jax.sharding import PartitionSpec as P

broaden = 0.002
e_low = -1.5
e_step = 3.0 / 4096.0
inv_pi = 1.0 / 3.141592653589793


def reciprocal(real_part, imag_part):
    norm = real_part * real_part + imag_part * imag_part
    return (real_part / norm, -imag_part / norm)


def complex_mul(first_re, first_im, second_re, second_im):
    return (
        first_re * second_re - first_im * second_im,
        first_re * second_im + first_im * second_re,
    )


def join_segments(left, right):
    square = left[6] * left[6]
    mix_re, mix_im = complex_mul(left[4], left[5], right[0], right[1])
    inv_re, inv_im = reciprocal(1.0 - square * mix_re, -square * mix_im)
    left_sq_re, left_sq_im = complex_mul(left[2], left[3], left[2], left[3])
    head_re, head_im = complex_mul(left_sq_re, left_sq_im, right[0], right[1])
    head_re, head_im = complex_mul(head_re, head_im, inv_re, inv_im)
    right_sq_re, right_sq_im = complex_mul(right[2], right[3], right[2], right[3])
    tail_re, tail_im = complex_mul(right_sq_re, right_sq_im, left[4], left[5])
    tail_re, tail_im = complex_mul(tail_re, tail_im, inv_re, inv_im)
    link_re, link_im = complex_mul(left[2], left[3], right[2], right[3])
    link_re, link_im = complex_mul(link_re, link_im, inv_re, inv_im)
    return (
        left[0] + square * head_re,
        left[1] + square * head_im,
        left[6] * link_re,
        left[6] * link_im,
        right[4] + square * tail_re,
        right[5] + square * tail_im,
        right[6],
    )


def onsite_terms(table_ref, energy_ref, here, count, devices, slots, points, slot):
    rows = 2 * slots
    levels = table_ref[slot]
    first_on = jnp.logical_and(here == 0, slot == 0).astype(jnp.float32)
    last_on = jnp.logical_and(here == devices - 1, slot == count - 1).astype(jnp.float32)
    onsite_re, onsite_im = [], []
    for point in range(points):
        energy = e_low + e_step * energy_ref[point].astype(jnp.float32)
        onsite_re.append(
            energy - levels
            - first_on * table_ref[rows + 2 * point]
            - last_on * table_ref[rows + 2 * point + 1]
        )
        onsite_im.append(
            broaden
            + first_on * table_ref[rows + 2 * points + 2 * point]
            + last_on * table_ref[rows + 2 * points + 2 * point + 1]
        )
    return jnp.stack(onsite_re), jnp.stack(onsite_im)


def summary_kernel(here_ref, length_ref, energy_ref, table_ref, out_ref, *, slots, points, devices):
    here = here_ref[0]
    count = length_ref[here]

    def single(slot):
        onsite_re, onsite_im = onsite_terms(
            table_ref, energy_ref, here, count, devices, slots, points, slot
        )
        g_re, g_im = reciprocal(onsite_re, onsite_im)
        return (g_re, g_im, g_re, g_im, g_re, g_im, table_ref[slots + slot])

    def body(slot, summary):
        return join_segments(summary, single(slot))

    first_re, first_im, cross_re, cross_im, final_re, final_im, coupling = lax.fori_loop(
        1, count, body, single(0)
    )
    square = coupling * coupling
    sq_re, sq_im = complex_mul(cross_re, cross_im, cross_re, cross_im)
    fields = (first_re, first_im, square * final_re, square * final_im, square * sq_re, square * sq_im)
    for index, value in enumerate(fields):
        out_ref[index * points:(index + 1) * points] = value


def join_coupled(left, right):
    d_re, d_im = complex_mul(left[2], left[3], right[0], right[1])
    inv_re, inv_im = reciprocal(1.0 - d_re, -d_im)
    f_re, f_im = complex_mul(left[4], left[5], right[0], right[1])
    f_re, f_im = complex_mul(f_re, f_im, inv_re, inv_im)
    g_re, g_im = complex_mul(right[4], right[5], left[2], left[3])
    g_re, g_im = complex_mul(g_re, g_im, inv_re, inv_im)
    x_re, x_im = complex_mul(left[4], left[5], right[4], right[5])
    x_re, x_im = complex_mul(x_re, x_im, inv_re, inv_im)
    x_re, x_im = complex_mul(x_re, x_im, inv_re, inv_im)
    return (left[0] + f_re, left[1] + f_im, right[2] + g_re, right[3] + g_im, x_re, x_im)


def in_order(refs, own, mixed):
    loaded = [ref[...] for ref in refs]
    if not mixed:
        return loaded
    ordered = []
    for position in range(len(refs)):
        offset = jnp.bitwise_xor(own, position)
        value = loaded[0]
        for index in range(1, len(refs)):
            value = jnp.where(offset == index, loaded[index], value)
        ordered.append(value)
    return ordered


def split_fields(value, points):
    return tuple(value[f * points:(f + 1) * points] for f in range(6))


def group_kernel(here_ref, *refs):
    local_refs, out_ref = refs[:-1], refs[-1]
    points = out_ref.shape[0] // 6
    size = len(local_refs)
    here = here_ref[0]
    blocks = in_order(local_refs, jnp.bitwise_and(here, size - 1), True)
    summary = split_fields(blocks[0], points)
    for member in range(1, size):
        summary = join_coupled(summary, split_fields(blocks[member], points))
    for index, value in enumerate(summary):
        out_ref[index * points:(index + 1) * points] = value


def final_kernel(here_ref, group_ref, length_ref, energy_ref, code_ref, *refs,
                 slots, points, devices, mixed, size, groups, scale):
    local_refs = refs[:size]
    group_refs = refs[size:size + groups]
    table_ref, dens_out_ref, bond_out_ref, theirs_ref, left_re_ref, left_im_ref, dens_ref, bond_ref = refs[size + groups:]
    here = here_ref[0]
    count = length_ref[here]
    rows = table_ref.shape[1]
    member_here = here % size
    group_here = here // size

    def into_step(block, run):
        run_re, run_im = run
        m_re, m_im = complex_mul(run_re, run_im, block[0], block[1])
        inv_re, inv_im = reciprocal(1.0 - m_re, -m_im)
        t_re, t_im = complex_mul(block[4], block[5], run_re, run_im)
        t_re, t_im = complex_mul(t_re, t_im, inv_re, inv_im)
        return (block[2] + t_re, block[3] + t_im)

    def from_step(block, run):
        run_re, run_im = run
        m_re, m_im = complex_mul(block[2], block[3], run_re, run_im)
        inv_re, inv_im = reciprocal(1.0 - m_re, -m_im)
        h_re, h_im = complex_mul(block[4], block[5], run_re, run_im)
        h_re, h_im = complex_mul(h_re, h_im, inv_re, inv_im)
        return (block[0] + h_re, block[1] + h_im)

    def masked(keep, new, old):
        return tuple(jnp.where(keep, n, o) for n, o in zip(new, old))

    zero = jnp.zeros((points,) + table_ref.shape[1:], jnp.float32)
    group_blocks = [split_fields(v, points) for v in in_order(group_refs, group_here, mixed)]
    local_blocks = [split_fields(v, points) for v in in_order(local_refs, member_here, mixed)]
    into = (zero, zero)
    for group in range(groups):
        into = masked(group < group_here, into_step(group_blocks[group], into), into)
    for member in range(size):
        into = masked(member < member_here, into_step(local_blocks[member], into), into)
    outof = (zero, zero)
    for group in reversed(range(groups)):
        outof = masked(group > group_here, from_step(group_blocks[group], outof), outof)
    for member in reversed(range(size)):
        outof = masked(member > member_here, from_step(local_blocks[member], outof), outof)
    into_re, into_im = into
    from_re, from_im = outof

    def onsite(slot):
        return onsite_terms(table_ref, energy_ref, here, count, devices, slots, points, slot)

    def forward_body(slot, carry):
        prev_re, prev_im, prev_coupling = carry
        onsite_re, onsite_im = onsite(slot)
        square = prev_coupling * prev_coupling
        g_re, g_im = reciprocal(onsite_re - square * prev_re, onsite_im - square * prev_im)
        left_re_ref[slot] = g_re
        left_im_ref[slot] = g_im
        return (g_re, g_im, table_ref[slots + slot])

    ones = jnp.ones(table_ref.shape[1:], jnp.float32)
    lax.fori_loop(0, count, forward_body, (into_re, into_im, ones))
    dens_ref[...] = jnp.zeros(dens_ref.shape, jnp.float32)
    bond_ref[...] = jnp.zeros(bond_ref.shape, jnp.float32)
    weights = [code_ref[point].astype(jnp.float32) * scale for point in range(points)]

    def backward_body(step, carry):
        next_re, next_im = carry
        slot = count - 1 - step
        onsite_re, onsite_im = onsite(slot)
        left_re, left_im = left_re_ref[slot], left_im_ref[slot]
        coupling = table_ref[slots + slot]
        square = coupling * coupling
        mix_re, mix_im = complex_mul(left_re, left_im, next_re, next_im)
        inv_re, inv_im = reciprocal(1.0 - square * mix_re, -square * mix_im)
        diag_re, diag_im = complex_mul(left_re, left_im, inv_re, inv_im)
        _, bond_im = complex_mul(diag_re, diag_im, next_re, next_im)
        dens = weights[0] * diag_im[0]
        bond = weights[0] * (square * bond_im[0])
        for point in range(1, points):
            dens = dens + weights[point] * diag_im[point]
            bond = bond + weights[point] * (square * bond_im[point])
        dens_ref[slot] = -inv_pi * dens
        bond_ref[slot] = -2.0 * inv_pi * bond
        return reciprocal(onsite_re - square * next_re, onsite_im - square * next_im)

    lax.fori_loop(0, count, backward_body, (from_re, from_im))
    lower = group_ref[0] == 0
    half = rows // 2
    for slot in range(slots):
        dens = dens_ref[slot]
        bond = bond_ref[slot]
        for row in range(half):
            lane = row * 128
            for kind, value, mine_ref in ((0, dens, dens_out_ref), (1, bond, bond_out_ref)):
                low, high = value[row:row + 1], value[row + half:row + half + 1]
                mine_ref[slot:slot + 1, lane:lane + 128] = jnp.where(lower, low, high)
                theirs_ref[kind, slot:slot + 1, lane:lane + 128] = jnp.where(lower, high, low)


def shards(
    mode_floor, onsite_noise, hopping, lengths, energy_index, weight_code, lead_shift, lead_width
):
    slots = onsite_noise.shape[0]
    modes = onsite_noise.shape[1]
    points = energy_index.shape[0]
    rows = modes // 128
    here = lax.axis_index("slab")
    devices = lax.axis_size("slab")
    groups = lax.axis_size("energy")
    table = jnp.concatenate(
        [
            mode_floor[None, :] + onsite_noise,
            hopping,
            lead_shift.reshape(2 * points, modes),
            lead_width.reshape(2 * points, modes),
        ],
        axis=0,
    ).reshape(2 * slots + 4 * points, rows, 128)
    here_arr = here.astype(jnp.int32).reshape(1)
    smem = pl.BlockSpec(memory_space=pltpu.SMEM)
    vmem = pl.BlockSpec(memory_space=pltpu.VMEM)

    packed = pl.pallas_call(
        functools.partial(summary_kernel, slots=slots, points=points, devices=devices),
        out_shape=jax.ShapeDtypeStruct((6 * points, rows, 128), jnp.float32),
        in_specs=[smem, smem, smem, vmem],
        out_specs=vmem,
    )(here_arr, lengths, energy_index, table)
    mixed = devices & (devices - 1) == 0 and devices >= 4
    if mixed:
        size = 4
        local = [packed] + [
            lax.ppermute(packed, "slab", [(device, device ^ offset) for device in range(devices)])
            for offset in range(1, size)
        ]
        summary = pl.pallas_call(
            group_kernel,
            out_shape=jax.ShapeDtypeStruct(packed.shape, jnp.float32),
            in_specs=[smem] + [vmem] * size,
            out_specs=vmem,
        )(here_arr, *local)
        if devices == size * size:
            every = [summary] + [
                lax.ppermute(summary, "slab", [(device, device ^ (offset * size)) for device in range(devices)])
                for offset in range(1, size)
            ]
        else:
            stacked = summary[None]
            distance = size
            while distance < devices:
                pairs = [(device, device ^ distance) for device in range(devices)]
                stacked = jnp.concatenate([stacked, lax.ppermute(stacked, "slab", pairs)], axis=0)
                distance *= 2
            every = [stacked[index] for index in range(devices // size)]
    else:
        size = devices
        gathered = lax.all_gather(packed, "slab")
        local = [gathered[index] for index in range(devices)]
        every = [jnp.zeros(packed.shape, jnp.float32)]
    half = jax.ShapeDtypeStruct((slots, modes // 2), jnp.float32)
    group_arr = lax.axis_index("energy").astype(jnp.int32).reshape(1)
    density, bond_density, theirs = pl.pallas_call(
        functools.partial(
            final_kernel, slots=slots, points=points, devices=devices, mixed=mixed,
            size=len(local), groups=len(every), scale=1.0 / (32.0 * points * groups),
        ),
        out_shape=(half, half, jax.ShapeDtypeStruct((2, slots, modes // 2), jnp.float32)),
        in_specs=[smem] * 5 + [vmem] * (len(local) + len(every) + 1),
        out_specs=(vmem, vmem, vmem),
        scratch_shapes=[
            pltpu.VMEM((slots, points, rows, 128), jnp.float32),
            pltpu.VMEM((slots, points, rows, 128), jnp.float32),
            pltpu.VMEM((slots, rows, 128), jnp.float32),
            pltpu.VMEM((slots, rows, 128), jnp.float32),
        ],
    )(here_arr, group_arr, lengths, energy_index, weight_code, *local, *every, table)
    if groups == 2:
        theirs = lax.ppermute(theirs, "energy", [(0, 1), (1, 0)])
        return (density + theirs[0], bond_density + theirs[1])
    lower = lax.axis_index("energy") == 0
    both = jnp.stack([
        jnp.where(lower, jnp.concatenate([density, theirs[0]], axis=1), jnp.concatenate([theirs[0], density], axis=1)),
        jnp.where(lower, jnp.concatenate([bond_density, theirs[1]], axis=1), jnp.concatenate([theirs[1], bond_density], axis=1)),
    ])
    both = lax.psum_scatter(both, "energy", scatter_dimension=2, tiled=True)
    return (both[0], both[1])


def solution(mesh):
    in_specs = (
        P(),
        P("slab", None),
        P("slab", None),
        P(),
        P("energy"),
        P("energy"),
        P("energy", None, None),
        P("energy", None, None),
    )
    out_specs = (P("slab", "energy"), P("slab", "energy"))
    return jax.shard_map(shards, mesh=mesh, in_specs=in_specs, out_specs=out_specs, check_vma=False)
```

```python
import functools

import jax
import jax.numpy as jnp
from jax import lax
from jax.experimental import pallas as pl
from jax.experimental.pallas import tpu as pltpu
from jax.sharding import PartitionSpec as P

broaden = 0.002
e_low = -1.5
e_step = 3.0 / 4096.0
inv_pi = 1.0 / 3.141592653589793


def reciprocal(real_part, imag_part):
    norm = real_part * real_part + imag_part * imag_part
    return (real_part / norm, -imag_part / norm)


def complex_mul(first_re, first_im, second_re, second_im):
    return (
        first_re * second_re - first_im * second_im,
        first_re * second_im + first_im * second_re,
    )


def join_segments(left, right):
    square = left[6] * left[6]
    mix_re, mix_im = complex_mul(left[4], left[5], right[0], right[1])
    inv_re, inv_im = reciprocal(1.0 - square * mix_re, -square * mix_im)
    left_sq_re, left_sq_im = complex_mul(left[2], left[3], left[2], left[3])
    head_re, head_im = complex_mul(left_sq_re, left_sq_im, right[0], right[1])
    head_re, head_im = complex_mul(head_re, head_im, inv_re, inv_im)
    right_sq_re, right_sq_im = complex_mul(right[2], right[3], right[2], right[3])
    tail_re, tail_im = complex_mul(right_sq_re, right_sq_im, left[4], left[5])
    tail_re, tail_im = complex_mul(tail_re, tail_im, inv_re, inv_im)
    link_re, link_im = complex_mul(left[2], left[3], right[2], right[3])
    link_re, link_im = complex_mul(link_re, link_im, inv_re, inv_im)
    return (
        left[0] + square * head_re,
        left[1] + square * head_im,
        left[6] * link_re,
        left[6] * link_im,
        right[4] + square * tail_re,
        right[5] + square * tail_im,
        right[6],
    )


def onsite_terms(table_ref, energy_ref, here, count, devices, slots, points, slot):
    rows = 2 * slots
    levels = table_ref[slot]
    first_on = jnp.logical_and(here == 0, slot == 0).astype(jnp.float32)
    last_on = jnp.logical_and(here == devices - 1, slot == count - 1).astype(jnp.float32)
    onsite_re, onsite_im = [], []
    for point in range(points):
        energy = e_low + e_step * energy_ref[point].astype(jnp.float32)
        onsite_re.append(
            energy - levels
            - first_on * table_ref[rows + 2 * point]
            - last_on * table_ref[rows + 2 * point + 1]
        )
        onsite_im.append(
            broaden
            + first_on * table_ref[rows + 2 * points + 2 * point]
            + last_on * table_ref[rows + 2 * points + 2 * point + 1]
        )
    return jnp.stack(onsite_re), jnp.stack(onsite_im)


def summary_kernel(here_ref, length_ref, energy_ref, table_ref, out_ref, *, slots, points, devices):
    here = here_ref[0]
    count = length_ref[here]
    zero = jnp.zeros((points,) + table_ref.shape[1:], jnp.float32)
    identity = (zero, zero, zero, zero, zero + 1.0, zero)
    blocks = []
    for slot in range(slots):
        onsite_re, onsite_im = onsite_terms(
            table_ref, energy_ref, here, count, devices, slots, points, slot
        )
        g_re, g_im = reciprocal(onsite_re, onsite_im)
        coupling = table_ref[slots + slot]
        square = coupling * coupling
        sq_re, sq_im = complex_mul(g_re, g_im, g_re, g_im)
        block = (g_re, g_im, square * g_re, square * g_im, square * sq_re, square * sq_im)
        live = slot < count
        blocks.append(tuple(jnp.where(live, new, old) for new, old in zip(block, identity)))
    while len(blocks) > 1:
        paired = [join_coupled(blocks[i], blocks[i + 1]) for i in range(0, len(blocks) - 1, 2)]
        if len(blocks) % 2:
            paired.append(blocks[-1])
        blocks = paired
    for index, value in enumerate(blocks[0]):
        out_ref[index * points:(index + 1) * points] = value


def join_coupled(left, right):
    d_re, d_im = complex_mul(left[2], left[3], right[0], right[1])
    inv_re, inv_im = reciprocal(1.0 - d_re, -d_im)
    f_re, f_im = complex_mul(left[4], left[5], right[0], right[1])
    f_re, f_im = complex_mul(f_re, f_im, inv_re, inv_im)
    g_re, g_im = complex_mul(right[4], right[5], left[2], left[3])
    g_re, g_im = complex_mul(g_re, g_im, inv_re, inv_im)
    x_re, x_im = complex_mul(left[4], left[5], right[4], right[5])
    x_re, x_im = complex_mul(x_re, x_im, inv_re, inv_im)
    x_re, x_im = complex_mul(x_re, x_im, inv_re, inv_im)
    return (left[0] + f_re, left[1] + f_im, right[2] + g_re, right[3] + g_im, x_re, x_im)


def in_order(refs, own, mixed):
    loaded = [ref[...] for ref in refs]
    if not mixed:
        return loaded
    ordered = []
    for position in range(len(refs)):
        offset = jnp.bitwise_xor(own, position)
        value = loaded[0]
        for index in range(1, len(refs)):
            value = jnp.where(offset == index, loaded[index], value)
        ordered.append(value)
    return ordered


def split_fields(value, points):
    return tuple(value[f * points:(f + 1) * points] for f in range(6))


def group_kernel(here_ref, *refs):
    local_refs, out_ref = refs[:-1], refs[-1]
    points = out_ref.shape[0] // 6
    size = len(local_refs)
    here = here_ref[0]
    blocks = in_order(local_refs, jnp.bitwise_and(here, size - 1), True)
    summary = split_fields(blocks[0], points)
    for member in range(1, size):
        summary = join_coupled(summary, split_fields(blocks[member], points))
    for index, value in enumerate(summary):
        out_ref[index * points:(index + 1) * points] = value


def final_kernel(here_ref, group_ref, length_ref, energy_ref, code_ref, *refs,
                 slots, points, devices, mixed, size, groups, scale):
    local_refs = refs[:size]
    group_refs = refs[size:size + groups]
    table_ref, dens_out_ref, bond_out_ref, theirs_ref, left_re_ref, left_im_ref, dens_ref, bond_ref = refs[size + groups:]
    here = here_ref[0]
    count = length_ref[here]
    rows = table_ref.shape[1]
    member_here = here % size
    group_here = here // size

    def into_step(block, run):
        run_re, run_im = run
        m_re, m_im = complex_mul(run_re, run_im, block[0], block[1])
        inv_re, inv_im = reciprocal(1.0 - m_re, -m_im)
        t_re, t_im = complex_mul(block[4], block[5], run_re, run_im)
        t_re, t_im = complex_mul(t_re, t_im, inv_re, inv_im)
        return (block[2] + t_re, block[3] + t_im)

    def from_step(block, run):
        run_re, run_im = run
        m_re, m_im = complex_mul(block[2], block[3], run_re, run_im)
        inv_re, inv_im = reciprocal(1.0 - m_re, -m_im)
        h_re, h_im = complex_mul(block[4], block[5], run_re, run_im)
        h_re, h_im = complex_mul(h_re, h_im, inv_re, inv_im)
        return (block[0] + h_re, block[1] + h_im)

    def masked(keep, new, old):
        return tuple(jnp.where(keep, n, o) for n, o in zip(new, old))

    zero = jnp.zeros((points,) + table_ref.shape[1:], jnp.float32)
    group_blocks = [split_fields(v, points) for v in in_order(group_refs, group_here, mixed)]
    local_blocks = [split_fields(v, points) for v in in_order(local_refs, member_here, mixed)]
    into = (zero, zero)
    for group in range(groups):
        into = masked(group < group_here, into_step(group_blocks[group], into), into)
    for member in range(size):
        into = masked(member < member_here, into_step(local_blocks[member], into), into)
    outof = (zero, zero)
    for group in reversed(range(groups)):
        outof = masked(group > group_here, from_step(group_blocks[group], outof), outof)
    for member in reversed(range(size)):
        outof = masked(member > member_here, from_step(local_blocks[member], outof), outof)
    into_re, into_im = into
    from_re, from_im = outof

    def onsite(slot):
        return onsite_terms(table_ref, energy_ref, here, count, devices, slots, points, slot)

    def forward_body(slot, carry):
        prev_re, prev_im, prev_coupling = carry
        onsite_re, onsite_im = onsite(slot)
        square = prev_coupling * prev_coupling
        g_re, g_im = reciprocal(onsite_re - square * prev_re, onsite_im - square * prev_im)
        left_re_ref[slot] = g_re
        left_im_ref[slot] = g_im
        return (g_re, g_im, table_ref[slots + slot])

    ones = jnp.ones(table_ref.shape[1:], jnp.float32)
    lax.fori_loop(0, count, forward_body, (into_re, into_im, ones))
    dens_ref[...] = jnp.zeros(dens_ref.shape, jnp.float32)
    bond_ref[...] = jnp.zeros(bond_ref.shape, jnp.float32)
    weights = [code_ref[point].astype(jnp.float32) * scale for point in range(points)]

    def backward_body(step, carry):
        next_re, next_im = carry
        slot = count - 1 - step
        onsite_re, onsite_im = onsite(slot)
        left_re, left_im = left_re_ref[slot], left_im_ref[slot]
        coupling = table_ref[slots + slot]
        square = coupling * coupling
        mix_re, mix_im = complex_mul(left_re, left_im, next_re, next_im)
        inv_re, inv_im = reciprocal(1.0 - square * mix_re, -square * mix_im)
        diag_re, diag_im = complex_mul(left_re, left_im, inv_re, inv_im)
        _, bond_im = complex_mul(diag_re, diag_im, next_re, next_im)
        dens = weights[0] * diag_im[0]
        bond = weights[0] * (square * bond_im[0])
        for point in range(1, points):
            dens = dens + weights[point] * diag_im[point]
            bond = bond + weights[point] * (square * bond_im[point])
        dens_ref[slot] = -inv_pi * dens
        bond_ref[slot] = -2.0 * inv_pi * bond
        return reciprocal(onsite_re - square * next_re, onsite_im - square * next_im)

    lax.fori_loop(0, count, backward_body, (from_re, from_im))
    lower = group_ref[0] == 0
    half = rows // 2
    for slot in range(slots):
        dens = dens_ref[slot]
        bond = bond_ref[slot]
        for row in range(half):
            lane = row * 128
            for kind, value, mine_ref in ((0, dens, dens_out_ref), (1, bond, bond_out_ref)):
                low, high = value[row:row + 1], value[row + half:row + half + 1]
                mine_ref[slot:slot + 1, lane:lane + 128] = jnp.where(lower, low, high)
                theirs_ref[kind, slot:slot + 1, lane:lane + 128] = jnp.where(lower, high, low)


def shards(
    mode_floor, onsite_noise, hopping, lengths, energy_index, weight_code, lead_shift, lead_width
):
    slots = onsite_noise.shape[0]
    modes = onsite_noise.shape[1]
    points = energy_index.shape[0]
    rows = modes // 128
    here = lax.axis_index("slab")
    devices = lax.axis_size("slab")
    groups = lax.axis_size("energy")
    table = jnp.concatenate(
        [
            mode_floor[None, :] + onsite_noise,
            hopping,
            lead_shift.reshape(2 * points, modes),
            lead_width.reshape(2 * points, modes),
        ],
        axis=0,
    ).reshape(2 * slots + 4 * points, rows, 128)
    here_arr = here.astype(jnp.int32).reshape(1)
    smem = pl.BlockSpec(memory_space=pltpu.SMEM)
    vmem = pl.BlockSpec(memory_space=pltpu.VMEM)

    packed = pl.pallas_call(
        functools.partial(summary_kernel, slots=slots, points=points, devices=devices),
        out_shape=jax.ShapeDtypeStruct((6 * points, rows, 128), jnp.float32),
        in_specs=[smem, smem, smem, vmem],
        out_specs=vmem,
    )(here_arr, lengths, energy_index, table)
    mixed = devices & (devices - 1) == 0 and devices >= 4
    if mixed:
        size = 4
        local = [packed] + [
            lax.ppermute(packed, "slab", [(device, device ^ offset) for device in range(devices)])
            for offset in range(1, size)
        ]
        summary = pl.pallas_call(
            group_kernel,
            out_shape=jax.ShapeDtypeStruct(packed.shape, jnp.float32),
            in_specs=[smem] + [vmem] * size,
            out_specs=vmem,
        )(here_arr, *local)
        if devices == size * size:
            every = [summary] + [
                lax.ppermute(summary, "slab", [(device, device ^ (offset * size)) for device in range(devices)])
                for offset in range(1, size)
            ]
        else:
            stacked = summary[None]
            distance = size
            while distance < devices:
                pairs = [(device, device ^ distance) for device in range(devices)]
                stacked = jnp.concatenate([stacked, lax.ppermute(stacked, "slab", pairs)], axis=0)
                distance *= 2
            every = [stacked[index] for index in range(devices // size)]
    else:
        size = devices
        gathered = lax.all_gather(packed, "slab")
        local = [gathered[index] for index in range(devices)]
        every = [jnp.zeros(packed.shape, jnp.float32)]
    half = jax.ShapeDtypeStruct((slots, modes // 2), jnp.float32)
    group_arr = lax.axis_index("energy").astype(jnp.int32).reshape(1)
    density, bond_density, theirs = pl.pallas_call(
        functools.partial(
            final_kernel, slots=slots, points=points, devices=devices, mixed=mixed,
            size=len(local), groups=len(every), scale=1.0 / (32.0 * points * groups),
        ),
        out_shape=(half, half, jax.ShapeDtypeStruct((2, slots, modes // 2), jnp.float32)),
        in_specs=[smem] * 5 + [vmem] * (len(local) + len(every) + 1),
        out_specs=(vmem, vmem, vmem),
        scratch_shapes=[
            pltpu.VMEM((slots, points, rows, 128), jnp.float32),
            pltpu.VMEM((slots, points, rows, 128), jnp.float32),
            pltpu.VMEM((slots, rows, 128), jnp.float32),
            pltpu.VMEM((slots, rows, 128), jnp.float32),
        ],
    )(here_arr, group_arr, lengths, energy_index, weight_code, *local, *every, table)
    if groups == 2:
        theirs = lax.ppermute(theirs, "energy", [(0, 1), (1, 0)])
        return (density + theirs[0], bond_density + theirs[1])
    lower = lax.axis_index("energy") == 0
    both = jnp.stack([
        jnp.where(lower, jnp.concatenate([density, theirs[0]], axis=1), jnp.concatenate([theirs[0], density], axis=1)),
        jnp.where(lower, jnp.concatenate([bond_density, theirs[1]], axis=1), jnp.concatenate([theirs[1], bond_density], axis=1)),
    ])
    both = lax.psum_scatter(both, "energy", scatter_dimension=2, tiled=True)
    return (both[0], both[1])


def solution(mesh):
    in_specs = (
        P(),
        P("slab", None),
        P("slab", None),
        P(),
        P("energy"),
        P("energy"),
        P("energy", None, None),
        P("energy", None, None),
    )
    out_specs = (P("slab", "energy"), P("slab", "energy"))
    return jax.shard_map(shards, mesh=mesh, in_specs=in_specs, out_specs=out_specs, check_vma=False)
```

```python
import functools

import jax
import jax.numpy as jnp
from jax import lax
from jax.experimental import pallas as pl
from jax.experimental.pallas import tpu as pltpu
from jax.sharding import PartitionSpec as P

broaden = 0.002
e_low = -1.5
e_step = 3.0 / 4096.0
inv_pi = 1.0 / 3.141592653589793


def reciprocal(real_part, imag_part):
    scale = 1.0 / (real_part * real_part + imag_part * imag_part)
    return (real_part * scale, -imag_part * scale)


def complex_mul(first_re, first_im, second_re, second_im):
    return (
        first_re * second_re - first_im * second_im,
        first_re * second_im + first_im * second_re,
    )


def join_segments(left, right):
    square = left[6] * left[6]
    mix_re, mix_im = complex_mul(left[4], left[5], right[0], right[1])
    inv_re, inv_im = reciprocal(1.0 - square * mix_re, -square * mix_im)
    left_sq_re, left_sq_im = complex_mul(left[2], left[3], left[2], left[3])
    head_re, head_im = complex_mul(left_sq_re, left_sq_im, right[0], right[1])
    head_re, head_im = complex_mul(head_re, head_im, inv_re, inv_im)
    right_sq_re, right_sq_im = complex_mul(right[2], right[3], right[2], right[3])
    tail_re, tail_im = complex_mul(right_sq_re, right_sq_im, left[4], left[5])
    tail_re, tail_im = complex_mul(tail_re, tail_im, inv_re, inv_im)
    link_re, link_im = complex_mul(left[2], left[3], right[2], right[3])
    link_re, link_im = complex_mul(link_re, link_im, inv_re, inv_im)
    return (
        left[0] + square * head_re,
        left[1] + square * head_im,
        left[6] * link_re,
        left[6] * link_im,
        right[4] + square * tail_re,
        right[5] + square * tail_im,
        right[6],
    )


def onsite_terms(table_ref, energy_ref, here, count, devices, slots, points, slot):
    rows = 2 * slots
    levels = table_ref[slot]
    first_on = jnp.logical_and(here == 0, slot == 0).astype(jnp.float32)
    last_on = jnp.logical_and(here == devices - 1, slot == count - 1).astype(jnp.float32)
    onsite_re, onsite_im = [], []
    for point in range(points):
        energy = e_low + e_step * energy_ref[point].astype(jnp.float32)
        onsite_re.append(
            energy - levels
            - first_on * table_ref[rows + 2 * point]
            - last_on * table_ref[rows + 2 * point + 1]
        )
        onsite_im.append(
            broaden
            + first_on * table_ref[rows + 2 * points + 2 * point]
            + last_on * table_ref[rows + 2 * points + 2 * point + 1]
        )
    return jnp.stack(onsite_re), jnp.stack(onsite_im)


def summary_kernel(here_ref, length_ref, energy_ref, table_ref, out_ref, *, slots, points, devices):
    here = here_ref[0]
    count = length_ref[here]

    def single(slot):
        onsite_re, onsite_im = onsite_terms(
            table_ref, energy_ref, here, count, devices, slots, points, slot
        )
        g_re, g_im = reciprocal(onsite_re, onsite_im)
        return (g_re, g_im, g_re, g_im, g_re, g_im, table_ref[slots + slot])

    def body(slot, summary):
        return join_segments(summary, single(slot))

    first_re, first_im, cross_re, cross_im, final_re, final_im, coupling = lax.fori_loop(
        1, count, body, single(0)
    )
    square = coupling * coupling
    sq_re, sq_im = complex_mul(cross_re, cross_im, cross_re, cross_im)
    fields = (first_re, first_im, square * final_re, square * final_im, square * sq_re, square * sq_im)
    for index, value in enumerate(fields):
        out_ref[index * points:(index + 1) * points] = value


def join_coupled(left, right):
    d_re, d_im = complex_mul(left[2], left[3], right[0], right[1])
    inv_re, inv_im = reciprocal(1.0 - d_re, -d_im)
    f_re, f_im = complex_mul(left[4], left[5], right[0], right[1])
    f_re, f_im = complex_mul(f_re, f_im, inv_re, inv_im)
    g_re, g_im = complex_mul(right[4], right[5], left[2], left[3])
    g_re, g_im = complex_mul(g_re, g_im, inv_re, inv_im)
    x_re, x_im = complex_mul(left[4], left[5], right[4], right[5])
    x_re, x_im = complex_mul(x_re, x_im, inv_re, inv_im)
    x_re, x_im = complex_mul(x_re, x_im, inv_re, inv_im)
    return (left[0] + f_re, left[1] + f_im, right[2] + g_re, right[3] + g_im, x_re, x_im)


def in_order(refs, own, mixed):
    loaded = [ref[...] for ref in refs]
    if not mixed:
        return loaded
    ordered = []
    for position in range(len(refs)):
        offset = jnp.bitwise_xor(own, position)
        value = loaded[0]
        for index in range(1, len(refs)):
            value = jnp.where(offset == index, loaded[index], value)
        ordered.append(value)
    return ordered


def split_fields(value, points):
    return tuple(value[f * points:(f + 1) * points] for f in range(6))


def group_kernel(here_ref, *refs):
    local_refs, out_ref = refs[:-1], refs[-1]
    points = out_ref.shape[0] // 6
    size = len(local_refs)
    here = here_ref[0]
    blocks = in_order(local_refs, jnp.bitwise_and(here, size - 1), True)
    summary = split_fields(blocks[0], points)
    for member in range(1, size):
        summary = join_coupled(summary, split_fields(blocks[member], points))
    for index, value in enumerate(summary):
        out_ref[index * points:(index + 1) * points] = value


def final_kernel(here_ref, group_ref, length_ref, energy_ref, code_ref, *refs,
                 slots, points, devices, mixed, size, groups, scale):
    local_refs = refs[:size]
    group_refs = refs[size:size + groups]
    table_ref, dens_out_ref, bond_out_ref, theirs_ref, left_re_ref, left_im_ref, dens_ref, bond_ref = refs[size + groups:]
    here = here_ref[0]
    count = length_ref[here]
    rows = table_ref.shape[1]
    member_here = here % size
    group_here = here // size

    def into_step(block, run):
        run_re, run_im = run
        m_re, m_im = complex_mul(run_re, run_im, block[0], block[1])
        inv_re, inv_im = reciprocal(1.0 - m_re, -m_im)
        t_re, t_im = complex_mul(block[4], block[5], run_re, run_im)
        t_re, t_im = complex_mul(t_re, t_im, inv_re, inv_im)
        return (block[2] + t_re, block[3] + t_im)

    def from_step(block, run):
        run_re, run_im = run
        m_re, m_im = complex_mul(block[2], block[3], run_re, run_im)
        inv_re, inv_im = reciprocal(1.0 - m_re, -m_im)
        h_re, h_im = complex_mul(block[4], block[5], run_re, run_im)
        h_re, h_im = complex_mul(h_re, h_im, inv_re, inv_im)
        return (block[0] + h_re, block[1] + h_im)

    def masked(keep, new, old):
        return tuple(jnp.where(keep, n, o) for n, o in zip(new, old))

    zero = jnp.zeros((points,) + table_ref.shape[1:], jnp.float32)
    group_blocks = [split_fields(v, points) for v in in_order(group_refs, group_here, mixed)]
    local_blocks = [split_fields(v, points) for v in in_order(local_refs, member_here, mixed)]
    into = (zero, zero)
    for group in range(groups):
        into = masked(group < group_here, into_step(group_blocks[group], into), into)
    for member in range(size):
        into = masked(member < member_here, into_step(local_blocks[member], into), into)
    outof = (zero, zero)
    for group in reversed(range(groups)):
        outof = masked(group > group_here, from_step(group_blocks[group], outof), outof)
    for member in reversed(range(size)):
        outof = masked(member > member_here, from_step(local_blocks[member], outof), outof)
    into_re, into_im = into
    from_re, from_im = outof

    def onsite(slot):
        return onsite_terms(table_ref, energy_ref, here, count, devices, slots, points, slot)

    def forward_body(slot, carry):
        prev_re, prev_im, prev_coupling = carry
        onsite_re, onsite_im = onsite(slot)
        square = prev_coupling * prev_coupling
        g_re, g_im = reciprocal(onsite_re - square * prev_re, onsite_im - square * prev_im)
        left_re_ref[slot] = g_re
        left_im_ref[slot] = g_im
        return (g_re, g_im, table_ref[slots + slot])

    ones = jnp.ones(table_ref.shape[1:], jnp.float32)
    lax.fori_loop(0, count, forward_body, (into_re, into_im, ones))
    dens_ref[...] = jnp.zeros(dens_ref.shape, jnp.float32)
    bond_ref[...] = jnp.zeros(bond_ref.shape, jnp.float32)
    weights = [code_ref[point].astype(jnp.float32) * scale for point in range(points)]

    def backward_body(step, carry):
        next_re, next_im = carry
        slot = count - 1 - step
        onsite_re, onsite_im = onsite(slot)
        left_re, left_im = left_re_ref[slot], left_im_ref[slot]
        coupling = table_ref[slots + slot]
        square = coupling * coupling
        mix_re, mix_im = complex_mul(left_re, left_im, next_re, next_im)
        inv_re, inv_im = reciprocal(1.0 - square * mix_re, -square * mix_im)
        diag_re, diag_im = complex_mul(left_re, left_im, inv_re, inv_im)
        _, bond_im = complex_mul(diag_re, diag_im, next_re, next_im)
        dens = weights[0] * diag_im[0]
        bond = weights[0] * (square * bond_im[0])
        for point in range(1, points):
            dens = dens + weights[point] * diag_im[point]
            bond = bond + weights[point] * (square * bond_im[point])
        dens_ref[slot] = -inv_pi * dens
        bond_ref[slot] = -2.0 * inv_pi * bond
        return reciprocal(onsite_re - square * next_re, onsite_im - square * next_im)

    lax.fori_loop(0, count, backward_body, (from_re, from_im))
    lower = group_ref[0] == 0
    half = rows // 2
    for slot in range(slots):
        dens = dens_ref[slot]
        bond = bond_ref[slot]
        for row in range(half):
            lane = row * 128
            for kind, value, mine_ref in ((0, dens, dens_out_ref), (1, bond, bond_out_ref)):
                low, high = value[row:row + 1], value[row + half:row + half + 1]
                mine_ref[slot:slot + 1, lane:lane + 128] = jnp.where(lower, low, high)
                theirs_ref[kind, slot:slot + 1, lane:lane + 128] = jnp.where(lower, high, low)


def shards(
    mode_floor, onsite_noise, hopping, lengths, energy_index, weight_code, lead_shift, lead_width
):
    slots = onsite_noise.shape[0]
    modes = onsite_noise.shape[1]
    points = energy_index.shape[0]
    rows = modes // 128
    here = lax.axis_index("slab")
    devices = lax.axis_size("slab")
    groups = lax.axis_size("energy")
    table = jnp.concatenate(
        [
            mode_floor[None, :] + onsite_noise,
            hopping,
            lead_shift.reshape(2 * points, modes),
            lead_width.reshape(2 * points, modes),
        ],
        axis=0,
    ).reshape(2 * slots + 4 * points, rows, 128)
    here_arr = here.astype(jnp.int32).reshape(1)
    smem = pl.BlockSpec(memory_space=pltpu.SMEM)
    vmem = pl.BlockSpec(memory_space=pltpu.VMEM)

    packed = pl.pallas_call(
        functools.partial(summary_kernel, slots=slots, points=points, devices=devices),
        out_shape=jax.ShapeDtypeStruct((6 * points, rows, 128), jnp.float32),
        in_specs=[smem, smem, smem, vmem],
        out_specs=vmem,
    )(here_arr, lengths, energy_index, table)
    mixed = devices & (devices - 1) == 0 and devices >= 4
    if mixed:
        size = 4
        local = [packed] + [
            lax.ppermute(packed, "slab", [(device, device ^ offset) for device in range(devices)])
            for offset in range(1, size)
        ]
        summary = pl.pallas_call(
            group_kernel,
            out_shape=jax.ShapeDtypeStruct(packed.shape, jnp.float32),
            in_specs=[smem] + [vmem] * size,
            out_specs=vmem,
        )(here_arr, *local)
        if devices == size * size:
            every = [summary] + [
                lax.ppermute(summary, "slab", [(device, device ^ (offset * size)) for device in range(devices)])
                for offset in range(1, size)
            ]
        else:
            stacked = summary[None]
            distance = size
            while distance < devices:
                pairs = [(device, device ^ distance) for device in range(devices)]
                stacked = jnp.concatenate([stacked, lax.ppermute(stacked, "slab", pairs)], axis=0)
                distance *= 2
            every = [stacked[index] for index in range(devices // size)]
    else:
        size = devices
        gathered = lax.all_gather(packed, "slab")
        local = [gathered[index] for index in range(devices)]
        every = [jnp.zeros(packed.shape, jnp.float32)]
    half = jax.ShapeDtypeStruct((slots, modes // 2), jnp.float32)
    group_arr = lax.axis_index("energy").astype(jnp.int32).reshape(1)
    density, bond_density, theirs = pl.pallas_call(
        functools.partial(
            final_kernel, slots=slots, points=points, devices=devices, mixed=mixed,
            size=len(local), groups=len(every), scale=1.0 / (32.0 * points * groups),
        ),
        out_shape=(half, half, jax.ShapeDtypeStruct((2, slots, modes // 2), jnp.float32)),
        in_specs=[smem] * 5 + [vmem] * (len(local) + len(every) + 1),
        out_specs=(vmem, vmem, vmem),
        scratch_shapes=[
            pltpu.VMEM((slots, points, rows, 128), jnp.float32),
            pltpu.VMEM((slots, points, rows, 128), jnp.float32),
            pltpu.VMEM((slots, rows, 128), jnp.float32),
            pltpu.VMEM((slots, rows, 128), jnp.float32),
        ],
    )(here_arr, group_arr, lengths, energy_index, weight_code, *local, *every, table)
    if groups == 2:
        theirs = lax.ppermute(theirs, "energy", [(0, 1), (1, 0)])
        return (density + theirs[0], bond_density + theirs[1])
    lower = lax.axis_index("energy") == 0
    both = jnp.stack([
        jnp.where(lower, jnp.concatenate([density, theirs[0]], axis=1), jnp.concatenate([theirs[0], density], axis=1)),
        jnp.where(lower, jnp.concatenate([bond_density, theirs[1]], axis=1), jnp.concatenate([theirs[1], bond_density], axis=1)),
    ])
    both = lax.psum_scatter(both, "energy", scatter_dimension=2, tiled=True)
    return (both[0], both[1])


def solution(mesh):
    in_specs = (
        P(),
        P("slab", None),
        P("slab", None),
        P(),
        P("energy"),
        P("energy"),
        P("energy", None, None),
        P("energy", None, None),
    )
    out_specs = (P("slab", "energy"), P("slab", "energy"))
    return jax.shard_map(shards, mesh=mesh, in_specs=in_specs, out_specs=out_specs, check_vma=False)
```

```python
import functools

import jax
import jax.numpy as jnp
from jax import lax
from jax.experimental import pallas as pl
from jax.experimental.pallas import tpu as pltpu
from jax.sharding import PartitionSpec as P

broaden = 0.002
e_low = -1.5
e_step = 3.0 / 4096.0
inv_pi = 1.0 / 3.141592653589793


def reciprocal(real_part, imag_part):
    scale = 1.0 / (real_part * real_part + imag_part * imag_part)
    return (real_part * scale, -imag_part * scale)


def complex_mul(first_re, first_im, second_re, second_im):
    return (
        first_re * second_re - first_im * second_im,
        first_re * second_im + first_im * second_re,
    )


def join_segments(left, right):
    square = left[6] * left[6]
    mix_re, mix_im = complex_mul(left[4], left[5], right[0], right[1])
    inv_re, inv_im = reciprocal(1.0 - square * mix_re, -square * mix_im)
    left_sq_re, left_sq_im = complex_mul(left[2], left[3], left[2], left[3])
    head_re, head_im = complex_mul(left_sq_re, left_sq_im, right[0], right[1])
    head_re, head_im = complex_mul(head_re, head_im, inv_re, inv_im)
    right_sq_re, right_sq_im = complex_mul(right[2], right[3], right[2], right[3])
    tail_re, tail_im = complex_mul(right_sq_re, right_sq_im, left[4], left[5])
    tail_re, tail_im = complex_mul(tail_re, tail_im, inv_re, inv_im)
    link_re, link_im = complex_mul(left[2], left[3], right[2], right[3])
    link_re, link_im = complex_mul(link_re, link_im, inv_re, inv_im)
    return (
        left[0] + square * head_re,
        left[1] + square * head_im,
        left[6] * link_re,
        left[6] * link_im,
        right[4] + square * tail_re,
        right[5] + square * tail_im,
        right[6],
    )


def onsite_terms(table_ref, energy_ref, here, count, devices, slots, points, slot):
    rows = 2 * slots
    levels = table_ref[slot]
    first_on = jnp.logical_and(here == 0, slot == 0).astype(jnp.float32)
    last_on = jnp.logical_and(here == devices - 1, slot == count - 1).astype(jnp.float32)
    onsite_re, onsite_im = [], []
    for point in range(points):
        energy = e_low + e_step * energy_ref[point].astype(jnp.float32)
        onsite_re.append(
            energy - levels
            - first_on * table_ref[rows + 2 * point]
            - last_on * table_ref[rows + 2 * point + 1]
        )
        onsite_im.append(
            broaden
            + first_on * table_ref[rows + 2 * points + 2 * point]
            + last_on * table_ref[rows + 2 * points + 2 * point + 1]
        )
    return jnp.stack(onsite_re), jnp.stack(onsite_im)


def summary_kernel(here_ref, length_ref, energy_ref, table_ref, out_ref, *, slots, points, devices):
    here = here_ref[0]
    count = length_ref[here]

    def single(slot):
        onsite_re, onsite_im = onsite_terms(
            table_ref, energy_ref, here, count, devices, slots, points, slot
        )
        g_re, g_im = reciprocal(onsite_re, onsite_im)
        coupling = table_ref[slots + slot]
        square = coupling * coupling
        sq_re, sq_im = complex_mul(g_re, g_im, g_re, g_im)
        return (g_re, g_im, square * g_re, square * g_im, square * sq_re, square * sq_im)

    def body(slot, summary):
        return join_coupled(summary, single(slot))

    summary = lax.fori_loop(1, count, body, single(0))
    for index, value in enumerate(summary):
        out_ref[index * points:(index + 1) * points] = value


def join_coupled(left, right):
    d_re, d_im = complex_mul(left[2], left[3], right[0], right[1])
    inv_re, inv_im = reciprocal(1.0 - d_re, -d_im)
    f_re, f_im = complex_mul(left[4], left[5], right[0], right[1])
    f_re, f_im = complex_mul(f_re, f_im, inv_re, inv_im)
    g_re, g_im = complex_mul(right[4], right[5], left[2], left[3])
    g_re, g_im = complex_mul(g_re, g_im, inv_re, inv_im)
    x_re, x_im = complex_mul(left[4], left[5], right[4], right[5])
    x_re, x_im = complex_mul(x_re, x_im, inv_re, inv_im)
    x_re, x_im = complex_mul(x_re, x_im, inv_re, inv_im)
    return (left[0] + f_re, left[1] + f_im, right[2] + g_re, right[3] + g_im, x_re, x_im)


def in_order(refs, own, mixed):
    loaded = [ref[...] for ref in refs]
    if not mixed:
        return loaded
    ordered = []
    for position in range(len(refs)):
        offset = jnp.bitwise_xor(own, position)
        value = loaded[0]
        for index in range(1, len(refs)):
            value = jnp.where(offset == index, loaded[index], value)
        ordered.append(value)
    return ordered


def split_fields(value, points):
    return tuple(value[f * points:(f + 1) * points] for f in range(6))


def group_kernel(here_ref, *refs):
    local_refs, out_ref = refs[:-1], refs[-1]
    points = out_ref.shape[0] // 6
    size = len(local_refs)
    here = here_ref[0]
    blocks = in_order(local_refs, jnp.bitwise_and(here, size - 1), True)
    summary = split_fields(blocks[0], points)
    for member in range(1, size):
        summary = join_coupled(summary, split_fields(blocks[member], points))
    for index, value in enumerate(summary):
        out_ref[index * points:(index + 1) * points] = value


def final_kernel(here_ref, group_ref, length_ref, energy_ref, code_ref, *refs,
                 slots, points, devices, mixed, size, groups, scale):
    local_refs = refs[:size]
    group_refs = refs[size:size + groups]
    table_ref, dens_out_ref, bond_out_ref, theirs_ref, left_re_ref, left_im_ref, dens_ref, bond_ref = refs[size + groups:]
    here = here_ref[0]
    count = length_ref[here]
    rows = table_ref.shape[1]
    member_here = here % size
    group_here = here // size

    def into_step(block, run):
        run_re, run_im = run
        m_re, m_im = complex_mul(run_re, run_im, block[0], block[1])
        inv_re, inv_im = reciprocal(1.0 - m_re, -m_im)
        t_re, t_im = complex_mul(block[4], block[5], run_re, run_im)
        t_re, t_im = complex_mul(t_re, t_im, inv_re, inv_im)
        return (block[2] + t_re, block[3] + t_im)

    def from_step(block, run):
        run_re, run_im = run
        m_re, m_im = complex_mul(block[2], block[3], run_re, run_im)
        inv_re, inv_im = reciprocal(1.0 - m_re, -m_im)
        h_re, h_im = complex_mul(block[4], block[5], run_re, run_im)
        h_re, h_im = complex_mul(h_re, h_im, inv_re, inv_im)
        return (block[0] + h_re, block[1] + h_im)

    def masked(keep, new, old):
        return tuple(jnp.where(keep, n, o) for n, o in zip(new, old))

    zero = jnp.zeros((points,) + table_ref.shape[1:], jnp.float32)
    group_blocks = [split_fields(v, points) for v in in_order(group_refs, group_here, mixed)]
    local_blocks = [split_fields(v, points) for v in in_order(local_refs, member_here, mixed)]
    into = (zero, zero)
    for group in range(groups):
        into = masked(group < group_here, into_step(group_blocks[group], into), into)
    for member in range(size):
        into = masked(member < member_here, into_step(local_blocks[member], into), into)
    outof = (zero, zero)
    for group in reversed(range(groups)):
        outof = masked(group > group_here, from_step(group_blocks[group], outof), outof)
    for member in reversed(range(size)):
        outof = masked(member > member_here, from_step(local_blocks[member], outof), outof)
    into_re, into_im = into
    from_re, from_im = outof

    def onsite(slot):
        return onsite_terms(table_ref, energy_ref, here, count, devices, slots, points, slot)

    def forward_body(slot, carry):
        prev_re, prev_im, prev_coupling = carry
        onsite_re, onsite_im = onsite(slot)
        square = prev_coupling * prev_coupling
        g_re, g_im = reciprocal(onsite_re - square * prev_re, onsite_im - square * prev_im)
        left_re_ref[slot] = g_re
        left_im_ref[slot] = g_im
        return (g_re, g_im, table_ref[slots + slot])

    ones = jnp.ones(table_ref.shape[1:], jnp.float32)
    lax.fori_loop(0, count, forward_body, (into_re, into_im, ones))
    dens_ref[...] = jnp.zeros(dens_ref.shape, jnp.float32)
    bond_ref[...] = jnp.zeros(bond_ref.shape, jnp.float32)
    weights = [code_ref[point].astype(jnp.float32) * scale for point in range(points)]

    def backward_body(step, carry):
        next_re, next_im = carry
        slot = count - 1 - step
        onsite_re, onsite_im = onsite(slot)
        left_re, left_im = left_re_ref[slot], left_im_ref[slot]
        coupling = table_ref[slots + slot]
        square = coupling * coupling
        mix_re, mix_im = complex_mul(left_re, left_im, next_re, next_im)
        inv_re, inv_im = reciprocal(1.0 - square * mix_re, -square * mix_im)
        diag_re, diag_im = complex_mul(left_re, left_im, inv_re, inv_im)
        _, bond_im = complex_mul(diag_re, diag_im, next_re, next_im)
        dens = weights[0] * diag_im[0]
        bond = weights[0] * (square * bond_im[0])
        for point in range(1, points):
            dens = dens + weights[point] * diag_im[point]
            bond = bond + weights[point] * (square * bond_im[point])
        dens_ref[slot] = -inv_pi * dens
        bond_ref[slot] = -2.0 * inv_pi * bond
        return reciprocal(onsite_re - square * next_re, onsite_im - square * next_im)

    lax.fori_loop(0, count, backward_body, (from_re, from_im))
    lower = group_ref[0] == 0
    half = rows // 2
    for slot in range(slots):
        dens = dens_ref[slot]
        bond = bond_ref[slot]
        for row in range(half):
            lane = row * 128
            for kind, value, mine_ref in ((0, dens, dens_out_ref), (1, bond, bond_out_ref)):
                low, high = value[row:row + 1], value[row + half:row + half + 1]
                mine_ref[slot:slot + 1, lane:lane + 128] = jnp.where(lower, low, high)
                theirs_ref[kind, slot:slot + 1, lane:lane + 128] = jnp.where(lower, high, low)


def shards(
    mode_floor, onsite_noise, hopping, lengths, energy_index, weight_code, lead_shift, lead_width
):
    slots = onsite_noise.shape[0]
    modes = onsite_noise.shape[1]
    points = energy_index.shape[0]
    rows = modes // 128
    here = lax.axis_index("slab")
    devices = lax.axis_size("slab")
    groups = lax.axis_size("energy")
    table = jnp.concatenate(
        [
            mode_floor[None, :] + onsite_noise,
            hopping,
            lead_shift.reshape(2 * points, modes),
            lead_width.reshape(2 * points, modes),
        ],
        axis=0,
    ).reshape(2 * slots + 4 * points, rows, 128)
    here_arr = here.astype(jnp.int32).reshape(1)
    smem = pl.BlockSpec(memory_space=pltpu.SMEM)
    vmem = pl.BlockSpec(memory_space=pltpu.VMEM)

    packed = pl.pallas_call(
        functools.partial(summary_kernel, slots=slots, points=points, devices=devices),
        out_shape=jax.ShapeDtypeStruct((6 * points, rows, 128), jnp.float32),
        in_specs=[smem, smem, smem, vmem],
        out_specs=vmem,
    )(here_arr, lengths, energy_index, table)
    mixed = devices & (devices - 1) == 0 and devices >= 4
    if mixed:
        size = 4
        local = [packed] + [
            lax.ppermute(packed, "slab", [(device, device ^ offset) for device in range(devices)])
            for offset in range(1, size)
        ]
        summary = pl.pallas_call(
            group_kernel,
            out_shape=jax.ShapeDtypeStruct(packed.shape, jnp.float32),
            in_specs=[smem] + [vmem] * size,
            out_specs=vmem,
        )(here_arr, *local)
        if devices == size * size:
            every = [summary] + [
                lax.ppermute(summary, "slab", [(device, device ^ (offset * size)) for device in range(devices)])
                for offset in range(1, size)
            ]
        else:
            stacked = summary[None]
            distance = size
            while distance < devices:
                pairs = [(device, device ^ distance) for device in range(devices)]
                stacked = jnp.concatenate([stacked, lax.ppermute(stacked, "slab", pairs)], axis=0)
                distance *= 2
            every = [stacked[index] for index in range(devices // size)]
    else:
        size = devices
        gathered = lax.all_gather(packed, "slab")
        local = [gathered[index] for index in range(devices)]
        every = [jnp.zeros(packed.shape, jnp.float32)]
    half = jax.ShapeDtypeStruct((slots, modes // 2), jnp.float32)
    group_arr = lax.axis_index("energy").astype(jnp.int32).reshape(1)
    density, bond_density, theirs = pl.pallas_call(
        functools.partial(
            final_kernel, slots=slots, points=points, devices=devices, mixed=mixed,
            size=len(local), groups=len(every), scale=1.0 / (32.0 * points * groups),
        ),
        out_shape=(half, half, jax.ShapeDtypeStruct((2, slots, modes // 2), jnp.float32)),
        in_specs=[smem] * 5 + [vmem] * (len(local) + len(every) + 1),
        out_specs=(vmem, vmem, vmem),
        scratch_shapes=[
            pltpu.VMEM((slots, points, rows, 128), jnp.float32),
            pltpu.VMEM((slots, points, rows, 128), jnp.float32),
            pltpu.VMEM((slots, rows, 128), jnp.float32),
            pltpu.VMEM((slots, rows, 128), jnp.float32),
        ],
    )(here_arr, group_arr, lengths, energy_index, weight_code, *local, *every, table)
    if groups == 2:
        theirs = lax.ppermute(theirs, "energy", [(0, 1), (1, 0)])
        return (density + theirs[0], bond_density + theirs[1])
    lower = lax.axis_index("energy") == 0
    both = jnp.stack([
        jnp.where(lower, jnp.concatenate([density, theirs[0]], axis=1), jnp.concatenate([theirs[0], density], axis=1)),
        jnp.where(lower, jnp.concatenate([bond_density, theirs[1]], axis=1), jnp.concatenate([theirs[1], bond_density], axis=1)),
    ])
    both = lax.psum_scatter(both, "energy", scatter_dimension=2, tiled=True)
    return (both[0], both[1])


def solution(mesh):
    in_specs = (
        P(),
        P("slab", None),
        P("slab", None),
        P(),
        P("energy"),
        P("energy"),
        P("energy", None, None),
        P("energy", None, None),
    )
    out_specs = (P("slab", "energy"), P("slab", "energy"))
    return jax.shard_map(shards, mesh=mesh, in_specs=in_specs, out_specs=out_specs, check_vma=False)
```

```python
import functools

import jax
import jax.numpy as jnp
from jax import lax
from jax.experimental import pallas as pl
from jax.experimental.pallas import tpu as pltpu
from jax.sharding import PartitionSpec as P

broaden = 0.002
e_low = -1.5
e_step = 3.0 / 4096.0
inv_pi = 1.0 / 3.141592653589793


def reciprocal(real_part, imag_part):
    scale = 1.0 / (real_part * real_part + imag_part * imag_part)
    return (real_part * scale, -imag_part * scale)


def complex_mul(first_re, first_im, second_re, second_im):
    return (
        first_re * second_re - first_im * second_im,
        first_re * second_im + first_im * second_re,
    )


def join_segments(left, right):
    square = left[6] * left[6]
    mix_re, mix_im = complex_mul(left[4], left[5], right[0], right[1])
    inv_re, inv_im = reciprocal(1.0 - square * mix_re, -square * mix_im)
    left_sq_re, left_sq_im = complex_mul(left[2], left[3], left[2], left[3])
    head_re, head_im = complex_mul(left_sq_re, left_sq_im, right[0], right[1])
    head_re, head_im = complex_mul(head_re, head_im, inv_re, inv_im)
    right_sq_re, right_sq_im = complex_mul(right[2], right[3], right[2], right[3])
    tail_re, tail_im = complex_mul(right_sq_re, right_sq_im, left[4], left[5])
    tail_re, tail_im = complex_mul(tail_re, tail_im, inv_re, inv_im)
    link_re, link_im = complex_mul(left[2], left[3], right[2], right[3])
    link_re, link_im = complex_mul(link_re, link_im, inv_re, inv_im)
    return (
        left[0] + square * head_re,
        left[1] + square * head_im,
        left[6] * link_re,
        left[6] * link_im,
        right[4] + square * tail_re,
        right[5] + square * tail_im,
        right[6],
    )


def onsite_terms(table_ref, energy_ref, here, count, devices, slots, points, slot):
    rows = 2 * slots
    levels = table_ref[slot]
    first_on = jnp.logical_and(here == 0, slot == 0).astype(jnp.float32)
    last_on = jnp.logical_and(here == devices - 1, slot == count - 1).astype(jnp.float32)
    onsite_re, onsite_im = [], []
    for point in range(points):
        energy = e_low + e_step * energy_ref[point].astype(jnp.float32)
        onsite_re.append(
            energy - levels
            - first_on * table_ref[rows + 2 * point]
            - last_on * table_ref[rows + 2 * point + 1]
        )
        onsite_im.append(
            broaden
            + first_on * table_ref[rows + 2 * points + 2 * point]
            + last_on * table_ref[rows + 2 * points + 2 * point + 1]
        )
    return jnp.stack(onsite_re), jnp.stack(onsite_im)


def summary_kernel(here_ref, length_ref, energy_ref, table_ref, out_ref, *, slots, points, devices):
    here = here_ref[0]
    count = length_ref[here]

    def single(slot):
        onsite_re, onsite_im = onsite_terms(
            table_ref, energy_ref, here, count, devices, slots, points, slot
        )
        g_re, g_im = reciprocal(onsite_re, onsite_im)
        coupling = table_ref[slots + slot]
        square = coupling * coupling
        sq_re, sq_im = complex_mul(g_re, g_im, g_re, g_im)
        return (g_re, g_im, square * g_re, square * g_im, square * sq_re, square * sq_im)

    def body(slot, summary):
        return join_coupled(summary, single(slot))

    summary = lax.fori_loop(1, count, body, single(0))
    for index, value in enumerate(summary):
        out_ref[index * points:(index + 1) * points] = value


def join_coupled(left, right):
    d_re, d_im = complex_mul(left[2], left[3], right[0], right[1])
    inv_re, inv_im = reciprocal(1.0 - d_re, -d_im)
    f_re, f_im = complex_mul(left[4], left[5], right[0], right[1])
    f_re, f_im = complex_mul(f_re, f_im, inv_re, inv_im)
    g_re, g_im = complex_mul(right[4], right[5], left[2], left[3])
    g_re, g_im = complex_mul(g_re, g_im, inv_re, inv_im)
    x_re, x_im = complex_mul(left[4], left[5], right[4], right[5])
    x_re, x_im = complex_mul(x_re, x_im, inv_re, inv_im)
    x_re, x_im = complex_mul(x_re, x_im, inv_re, inv_im)
    return (left[0] + f_re, left[1] + f_im, right[2] + g_re, right[3] + g_im, x_re, x_im)


def in_order(refs, own, mixed):
    loaded = [ref[...] for ref in refs]
    if not mixed:
        return loaded
    ordered = []
    for position in range(len(refs)):
        offset = jnp.bitwise_xor(own, position)
        value = loaded[0]
        for index in range(1, len(refs)):
            value = jnp.where(offset == index, loaded[index], value)
        ordered.append(value)
    return ordered


def split_fields(value, points):
    return tuple(value[f * points:(f + 1) * points] for f in range(6))


def group_kernel(here_ref, *refs):
    local_refs, out_ref = refs[:-1], refs[-1]
    points = out_ref.shape[0] // 6
    size = len(local_refs)
    here = here_ref[0]
    blocks = in_order(local_refs, jnp.bitwise_and(here, size - 1), True)
    summary = split_fields(blocks[0], points)
    for member in range(1, size):
        summary = join_coupled(summary, split_fields(blocks[member], points))
    for index, value in enumerate(summary):
        out_ref[index * points:(index + 1) * points] = value


def final_kernel(here_ref, group_ref, length_ref, energy_ref, code_ref, *refs,
                 slots, points, devices, mixed, size, groups, scale):
    local_refs = refs[:size]
    group_refs = refs[size:size + groups]
    table_ref, dens_out_ref, bond_out_ref, theirs_ref, left_re_ref, left_im_ref, dens_ref, bond_ref = refs[size + groups:]
    here = here_ref[0]
    count = length_ref[here]
    rows = table_ref.shape[1]
    member_here = here % size
    group_here = here // size

    def into_step(block, run):
        run_re, run_im = run
        m_re, m_im = complex_mul(run_re, run_im, block[0], block[1])
        inv_re, inv_im = reciprocal(1.0 - m_re, -m_im)
        t_re, t_im = complex_mul(block[4], block[5], run_re, run_im)
        t_re, t_im = complex_mul(t_re, t_im, inv_re, inv_im)
        return (block[2] + t_re, block[3] + t_im)

    def from_step(block, run):
        run_re, run_im = run
        m_re, m_im = complex_mul(block[2], block[3], run_re, run_im)
        inv_re, inv_im = reciprocal(1.0 - m_re, -m_im)
        h_re, h_im = complex_mul(block[4], block[5], run_re, run_im)
        h_re, h_im = complex_mul(h_re, h_im, inv_re, inv_im)
        return (block[0] + h_re, block[1] + h_im)

    def masked(keep, new, old):
        return tuple(jnp.where(keep, n, o) for n, o in zip(new, old))

    zero = jnp.zeros((points,) + table_ref.shape[1:], jnp.float32)
    group_blocks = [split_fields(v, points) for v in in_order(group_refs, group_here, mixed)]
    local_blocks = [split_fields(v, points) for v in in_order(local_refs, member_here, mixed)]
    into = (zero, zero)
    for group in range(groups):
        into = masked(group < group_here, into_step(group_blocks[group], into), into)
    for member in range(size):
        into = masked(member < member_here, into_step(local_blocks[member], into), into)
    outof = (zero, zero)
    for group in reversed(range(groups)):
        outof = masked(group > group_here, from_step(group_blocks[group], outof), outof)
    for member in reversed(range(size)):
        outof = masked(member > member_here, from_step(local_blocks[member], outof), outof)
    into_re, into_im = into
    from_re, from_im = outof

    def onsite(slot):
        return onsite_terms(table_ref, energy_ref, here, count, devices, slots, points, slot)

    def forward_body(slot, carry):
        prev_re, prev_im, prev_coupling = carry
        onsite_re, onsite_im = onsite(slot)
        square = prev_coupling * prev_coupling
        denom_re, denom_im = onsite_re - square * prev_re, onsite_im - square * prev_im
        g_re, g_im = reciprocal(denom_re, denom_im)
        left_re_ref[slot] = denom_re
        left_im_ref[slot] = denom_im
        return (g_re, g_im, table_ref[slots + slot])

    ones = jnp.ones(table_ref.shape[1:], jnp.float32)
    lax.fori_loop(0, count, forward_body, (into_re, into_im, ones))
    dens_ref[...] = jnp.zeros(dens_ref.shape, jnp.float32)
    bond_ref[...] = jnp.zeros(bond_ref.shape, jnp.float32)
    weights = [code_ref[point].astype(jnp.float32) * scale for point in range(points)]

    def backward_body(step, carry):
        next_re, next_im = carry
        slot = count - 1 - step
        onsite_re, onsite_im = onsite(slot)
        denom_re, denom_im = left_re_ref[slot], left_im_ref[slot]
        coupling = table_ref[slots + slot]
        square = coupling * coupling
        diag_re, diag_im = reciprocal(denom_re - square * next_re, denom_im - square * next_im)
        _, bond_im = complex_mul(diag_re, diag_im, next_re, next_im)
        dens = weights[0] * diag_im[0]
        bond = weights[0] * (square * bond_im[0])
        for point in range(1, points):
            dens = dens + weights[point] * diag_im[point]
            bond = bond + weights[point] * (square * bond_im[point])
        dens_ref[slot] = -inv_pi * dens
        bond_ref[slot] = -2.0 * inv_pi * bond
        return reciprocal(onsite_re - square * next_re, onsite_im - square * next_im)

    lax.fori_loop(0, count, backward_body, (from_re, from_im))
    lower = group_ref[0] == 0
    half = rows // 2
    for slot in range(slots):
        dens = dens_ref[slot]
        bond = bond_ref[slot]
        for row in range(half):
            lane = row * 128
            for kind, value, mine_ref in ((0, dens, dens_out_ref), (1, bond, bond_out_ref)):
                low, high = value[row:row + 1], value[row + half:row + half + 1]
                mine_ref[slot:slot + 1, lane:lane + 128] = jnp.where(lower, low, high)
                theirs_ref[kind, slot:slot + 1, lane:lane + 128] = jnp.where(lower, high, low)


def shards(
    mode_floor, onsite_noise, hopping, lengths, energy_index, weight_code, lead_shift, lead_width
):
    slots = onsite_noise.shape[0]
    modes = onsite_noise.shape[1]
    points = energy_index.shape[0]
    rows = modes // 128
    here = lax.axis_index("slab")
    devices = lax.axis_size("slab")
    groups = lax.axis_size("energy")
    table = jnp.concatenate(
        [
            mode_floor[None, :] + onsite_noise,
            hopping,
            lead_shift.reshape(2 * points, modes),
            lead_width.reshape(2 * points, modes),
        ],
        axis=0,
    ).reshape(2 * slots + 4 * points, rows, 128)
    here_arr = here.astype(jnp.int32).reshape(1)
    smem = pl.BlockSpec(memory_space=pltpu.SMEM)
    vmem = pl.BlockSpec(memory_space=pltpu.VMEM)

    packed = pl.pallas_call(
        functools.partial(summary_kernel, slots=slots, points=points, devices=devices),
        out_shape=jax.ShapeDtypeStruct((6 * points, rows, 128), jnp.float32),
        in_specs=[smem, smem, smem, vmem],
        out_specs=vmem,
    )(here_arr, lengths, energy_index, table)
    mixed = devices & (devices - 1) == 0 and devices >= 4
    if mixed:
        size = 4
        local = [packed] + [
            lax.ppermute(packed, "slab", [(device, device ^ offset) for device in range(devices)])
            for offset in range(1, size)
        ]
        summary = pl.pallas_call(
            group_kernel,
            out_shape=jax.ShapeDtypeStruct(packed.shape, jnp.float32),
            in_specs=[smem] + [vmem] * size,
            out_specs=vmem,
        )(here_arr, *local)
        if devices == size * size:
            every = [summary] + [
                lax.ppermute(summary, "slab", [(device, device ^ (offset * size)) for device in range(devices)])
                for offset in range(1, size)
            ]
        else:
            stacked = summary[None]
            distance = size
            while distance < devices:
                pairs = [(device, device ^ distance) for device in range(devices)]
                stacked = jnp.concatenate([stacked, lax.ppermute(stacked, "slab", pairs)], axis=0)
                distance *= 2
            every = [stacked[index] for index in range(devices // size)]
    else:
        size = devices
        gathered = lax.all_gather(packed, "slab")
        local = [gathered[index] for index in range(devices)]
        every = [jnp.zeros(packed.shape, jnp.float32)]
    half = jax.ShapeDtypeStruct((slots, modes // 2), jnp.float32)
    group_arr = lax.axis_index("energy").astype(jnp.int32).reshape(1)
    density, bond_density, theirs = pl.pallas_call(
        functools.partial(
            final_kernel, slots=slots, points=points, devices=devices, mixed=mixed,
            size=len(local), groups=len(every), scale=1.0 / (32.0 * points * groups),
        ),
        out_shape=(half, half, jax.ShapeDtypeStruct((2, slots, modes // 2), jnp.float32)),
        in_specs=[smem] * 5 + [vmem] * (len(local) + len(every) + 1),
        out_specs=(vmem, vmem, vmem),
        scratch_shapes=[
            pltpu.VMEM((slots, points, rows, 128), jnp.float32),
            pltpu.VMEM((slots, points, rows, 128), jnp.float32),
            pltpu.VMEM((slots, rows, 128), jnp.float32),
            pltpu.VMEM((slots, rows, 128), jnp.float32),
        ],
    )(here_arr, group_arr, lengths, energy_index, weight_code, *local, *every, table)
    if groups == 2:
        theirs = lax.ppermute(theirs, "energy", [(0, 1), (1, 0)])
        return (density + theirs[0], bond_density + theirs[1])
    lower = lax.axis_index("energy") == 0
    both = jnp.stack([
        jnp.where(lower, jnp.concatenate([density, theirs[0]], axis=1), jnp.concatenate([theirs[0], density], axis=1)),
        jnp.where(lower, jnp.concatenate([bond_density, theirs[1]], axis=1), jnp.concatenate([theirs[1], bond_density], axis=1)),
    ])
    both = lax.psum_scatter(both, "energy", scatter_dimension=2, tiled=True)
    return (both[0], both[1])


def solution(mesh):
    in_specs = (
        P(),
        P("slab", None),
        P("slab", None),
        P(),
        P("energy"),
        P("energy"),
        P("energy", None, None),
        P("energy", None, None),
    )
    out_specs = (P("slab", "energy"), P("slab", "energy"))
    return jax.shard_map(shards, mesh=mesh, in_specs=in_specs, out_specs=out_specs, check_vma=False)
```

```python
import functools

import jax
import jax.numpy as jnp
from jax import lax
from jax.experimental import pallas as pl
from jax.experimental.pallas import tpu as pltpu
from jax.sharding import PartitionSpec as P

broaden = 0.002
e_low = -1.5
e_step = 3.0 / 4096.0
inv_pi = 1.0 / 3.141592653589793


def reciprocal(real_part, imag_part):
    scale = 1.0 / (real_part * real_part + imag_part * imag_part)
    return (real_part * scale, -imag_part * scale)


def complex_mul(first_re, first_im, second_re, second_im):
    return (
        first_re * second_re - first_im * second_im,
        first_re * second_im + first_im * second_re,
    )


def join_segments(left, right):
    square = left[6] * left[6]
    mix_re, mix_im = complex_mul(left[4], left[5], right[0], right[1])
    inv_re, inv_im = reciprocal(1.0 - square * mix_re, -square * mix_im)
    left_sq_re, left_sq_im = complex_mul(left[2], left[3], left[2], left[3])
    head_re, head_im = complex_mul(left_sq_re, left_sq_im, right[0], right[1])
    head_re, head_im = complex_mul(head_re, head_im, inv_re, inv_im)
    right_sq_re, right_sq_im = complex_mul(right[2], right[3], right[2], right[3])
    tail_re, tail_im = complex_mul(right_sq_re, right_sq_im, left[4], left[5])
    tail_re, tail_im = complex_mul(tail_re, tail_im, inv_re, inv_im)
    link_re, link_im = complex_mul(left[2], left[3], right[2], right[3])
    link_re, link_im = complex_mul(link_re, link_im, inv_re, inv_im)
    return (
        left[0] + square * head_re,
        left[1] + square * head_im,
        left[6] * link_re,
        left[6] * link_im,
        right[4] + square * tail_re,
        right[5] + square * tail_im,
        right[6],
    )


def onsite_terms(table_ref, energy_ref, here, count, devices, slots, points, slot):
    rows = 2 * slots
    levels = table_ref[slot]
    first_on = jnp.logical_and(here == 0, slot == 0).astype(jnp.float32)
    last_on = jnp.logical_and(here == devices - 1, slot == count - 1).astype(jnp.float32)
    onsite_re, onsite_im = [], []
    for point in range(points):
        energy = e_low + e_step * energy_ref[point].astype(jnp.float32)
        onsite_re.append(
            energy - levels
            - first_on * table_ref[rows + 2 * point]
            - last_on * table_ref[rows + 2 * point + 1]
        )
        onsite_im.append(
            broaden
            + first_on * table_ref[rows + 2 * points + 2 * point]
            + last_on * table_ref[rows + 2 * points + 2 * point + 1]
        )
    return jnp.stack(onsite_re), jnp.stack(onsite_im)


def build_table(floor_ref, noise_ref, hop_ref, shift_ref, width_ref, table_ref):
    slots = noise_ref.shape[0]
    points = shift_ref.shape[0]
    for row in range(table_ref.shape[1]):
        lanes = slice(row * 128, (row + 1) * 128)
        floor = floor_ref[0:1, lanes]
        for slot in range(slots):
            table_ref[slot, row:row + 1, :] = floor + noise_ref[slot:slot + 1, lanes]
            table_ref[slots + slot, row:row + 1, :] = hop_ref[slot:slot + 1, lanes]
        for point in range(points):
            for side in range(2):
                index = 2 * slots + 2 * point + side
                table_ref[index, row:row + 1, :] = shift_ref[point, side:side + 1, lanes]
                table_ref[index + 2 * points, row:row + 1, :] = width_ref[point, side:side + 1, lanes]


def summary_kernel(here_ref, length_ref, energy_ref, floor_ref, noise_ref, hop_ref, shift_ref, width_ref,
                   out_ref, table_ref, *, slots, points, devices):
    build_table(floor_ref, noise_ref, hop_ref, shift_ref, width_ref, table_ref)
    here = here_ref[0]
    count = length_ref[here]

    def single(slot):
        onsite_re, onsite_im = onsite_terms(
            table_ref, energy_ref, here, count, devices, slots, points, slot
        )
        g_re, g_im = reciprocal(onsite_re, onsite_im)
        coupling = table_ref[slots + slot]
        square = coupling * coupling
        sq_re, sq_im = complex_mul(g_re, g_im, g_re, g_im)
        return (g_re, g_im, square * g_re, square * g_im, square * sq_re, square * sq_im)

    def body(slot, summary):
        return join_coupled(summary, single(slot))

    summary = lax.fori_loop(1, count, body, single(0))
    for index, value in enumerate(summary):
        out_ref[index * points:(index + 1) * points] = value


def join_coupled(left, right):
    d_re, d_im = complex_mul(left[2], left[3], right[0], right[1])
    inv_re, inv_im = reciprocal(1.0 - d_re, -d_im)
    f_re, f_im = complex_mul(left[4], left[5], right[0], right[1])
    f_re, f_im = complex_mul(f_re, f_im, inv_re, inv_im)
    g_re, g_im = complex_mul(right[4], right[5], left[2], left[3])
    g_re, g_im = complex_mul(g_re, g_im, inv_re, inv_im)
    x_re, x_im = complex_mul(left[4], left[5], right[4], right[5])
    x_re, x_im = complex_mul(x_re, x_im, inv_re, inv_im)
    x_re, x_im = complex_mul(x_re, x_im, inv_re, inv_im)
    return (left[0] + f_re, left[1] + f_im, right[2] + g_re, right[3] + g_im, x_re, x_im)


def in_order(refs, own, mixed):
    loaded = [ref[...] for ref in refs]
    if not mixed:
        return loaded
    ordered = []
    for position in range(len(refs)):
        offset = jnp.bitwise_xor(own, position)
        value = loaded[0]
        for index in range(1, len(refs)):
            value = jnp.where(offset == index, loaded[index], value)
        ordered.append(value)
    return ordered


def split_fields(value, points):
    return tuple(value[f * points:(f + 1) * points] for f in range(6))


def group_kernel(here_ref, *refs):
    local_refs, out_ref = refs[:-1], refs[-1]
    points = out_ref.shape[0] // 6
    size = len(local_refs)
    here = here_ref[0]
    blocks = in_order(local_refs, jnp.bitwise_and(here, size - 1), True)
    summary = split_fields(blocks[0], points)
    for member in range(1, size):
        summary = join_coupled(summary, split_fields(blocks[member], points))
    for index, value in enumerate(summary):
        out_ref[index * points:(index + 1) * points] = value


def final_kernel(here_ref, group_ref, length_ref, energy_ref, code_ref, *refs,
                 slots, points, devices, mixed, size, groups, scale):
    local_refs = refs[:size]
    group_refs = refs[size:size + groups]
    (floor_ref, noise_ref, hop_ref, shift_ref, width_ref, dens_out_ref, bond_out_ref, theirs_ref,
     left_re_ref, left_im_ref, dens_ref, bond_ref, table_ref) = refs[size + groups:]
    build_table(floor_ref, noise_ref, hop_ref, shift_ref, width_ref, table_ref)
    here = here_ref[0]
    count = length_ref[here]
    rows = table_ref.shape[1]
    member_here = here % size
    group_here = here // size

    def into_step(block, run):
        run_re, run_im = run
        m_re, m_im = complex_mul(run_re, run_im, block[0], block[1])
        inv_re, inv_im = reciprocal(1.0 - m_re, -m_im)
        t_re, t_im = complex_mul(block[4], block[5], run_re, run_im)
        t_re, t_im = complex_mul(t_re, t_im, inv_re, inv_im)
        return (block[2] + t_re, block[3] + t_im)

    def from_step(block, run):
        run_re, run_im = run
        m_re, m_im = complex_mul(block[2], block[3], run_re, run_im)
        inv_re, inv_im = reciprocal(1.0 - m_re, -m_im)
        h_re, h_im = complex_mul(block[4], block[5], run_re, run_im)
        h_re, h_im = complex_mul(h_re, h_im, inv_re, inv_im)
        return (block[0] + h_re, block[1] + h_im)

    def masked(keep, new, old):
        return tuple(jnp.where(keep, n, o) for n, o in zip(new, old))

    zero = jnp.zeros((points,) + table_ref.shape[1:], jnp.float32)
    group_blocks = [split_fields(v, points) for v in in_order(group_refs, group_here, mixed)]
    local_blocks = [split_fields(v, points) for v in in_order(local_refs, member_here, mixed)]
    into = (zero, zero)
    for group in range(groups):
        into = masked(group < group_here, into_step(group_blocks[group], into), into)
    for member in range(size):
        into = masked(member < member_here, into_step(local_blocks[member], into), into)
    outof = (zero, zero)
    for group in reversed(range(groups)):
        outof = masked(group > group_here, from_step(group_blocks[group], outof), outof)
    for member in reversed(range(size)):
        outof = masked(member > member_here, from_step(local_blocks[member], outof), outof)
    into_re, into_im = into
    from_re, from_im = outof

    def onsite(slot):
        return onsite_terms(table_ref, energy_ref, here, count, devices, slots, points, slot)

    def forward_body(slot, carry):
        prev_re, prev_im, prev_coupling = carry
        onsite_re, onsite_im = onsite(slot)
        square = prev_coupling * prev_coupling
        denom_re, denom_im = onsite_re - square * prev_re, onsite_im - square * prev_im
        g_re, g_im = reciprocal(denom_re, denom_im)
        left_re_ref[slot] = denom_re
        left_im_ref[slot] = denom_im
        return (g_re, g_im, table_ref[slots + slot])

    ones = jnp.ones(table_ref.shape[1:], jnp.float32)
    lax.fori_loop(0, count, forward_body, (into_re, into_im, ones))
    dens_ref[...] = jnp.zeros(dens_ref.shape, jnp.float32)
    bond_ref[...] = jnp.zeros(bond_ref.shape, jnp.float32)
    weights = [code_ref[point].astype(jnp.float32) * scale for point in range(points)]

    def backward_body(step, carry):
        next_re, next_im = carry
        slot = count - 1 - step
        onsite_re, onsite_im = onsite(slot)
        denom_re, denom_im = left_re_ref[slot], left_im_ref[slot]
        coupling = table_ref[slots + slot]
        square = coupling * coupling
        diag_re, diag_im = reciprocal(denom_re - square * next_re, denom_im - square * next_im)
        _, bond_im = complex_mul(diag_re, diag_im, next_re, next_im)
        dens = weights[0] * diag_im[0]
        bond = weights[0] * (square * bond_im[0])
        for point in range(1, points):
            dens = dens + weights[point] * diag_im[point]
            bond = bond + weights[point] * (square * bond_im[point])
        dens_ref[slot] = -inv_pi * dens
        bond_ref[slot] = -2.0 * inv_pi * bond
        return reciprocal(onsite_re - square * next_re, onsite_im - square * next_im)

    lax.fori_loop(0, count, backward_body, (from_re, from_im))
    lower = group_ref[0] == 0
    half = rows // 2
    for slot in range(slots):
        dens = dens_ref[slot]
        bond = bond_ref[slot]
        for row in range(half):
            lane = row * 128
            for kind, value, mine_ref in ((0, dens, dens_out_ref), (1, bond, bond_out_ref)):
                low, high = value[row:row + 1], value[row + half:row + half + 1]
                mine_ref[slot:slot + 1, lane:lane + 128] = jnp.where(lower, low, high)
                theirs_ref[kind, slot:slot + 1, lane:lane + 128] = jnp.where(lower, high, low)


def shards(
    mode_floor, onsite_noise, hopping, lengths, energy_index, weight_code, lead_shift, lead_width
):
    slots = onsite_noise.shape[0]
    modes = onsite_noise.shape[1]
    points = energy_index.shape[0]
    rows = modes // 128
    here = lax.axis_index("slab")
    devices = lax.axis_size("slab")
    groups = lax.axis_size("energy")
    raw = (mode_floor.reshape(1, modes), onsite_noise, hopping, lead_shift, lead_width)
    table_shape = (2 * slots + 4 * points, rows, 128)
    here_arr = here.astype(jnp.int32).reshape(1)
    smem = pl.BlockSpec(memory_space=pltpu.SMEM)
    vmem = pl.BlockSpec(memory_space=pltpu.VMEM)

    packed = pl.pallas_call(
        functools.partial(summary_kernel, slots=slots, points=points, devices=devices),
        out_shape=jax.ShapeDtypeStruct((6 * points, rows, 128), jnp.float32),
        in_specs=[smem, smem, smem] + [vmem] * len(raw),
        out_specs=vmem,
        scratch_shapes=[pltpu.VMEM(table_shape, jnp.float32)],
    )(here_arr, lengths, energy_index, *raw)
    mixed = devices & (devices - 1) == 0 and devices >= 4
    if mixed:
        size = 4
        local = [packed] + [
            lax.ppermute(packed, "slab", [(device, device ^ offset) for device in range(devices)])
            for offset in range(1, size)
        ]
        summary = pl.pallas_call(
            group_kernel,
            out_shape=jax.ShapeDtypeStruct(packed.shape, jnp.float32),
            in_specs=[smem] + [vmem] * size,
            out_specs=vmem,
        )(here_arr, *local)
        if devices == size * size:
            every = [summary] + [
                lax.ppermute(summary, "slab", [(device, device ^ (offset * size)) for device in range(devices)])
                for offset in range(1, size)
            ]
        else:
            stacked = summary[None]
            distance = size
            while distance < devices:
                pairs = [(device, device ^ distance) for device in range(devices)]
                stacked = jnp.concatenate([stacked, lax.ppermute(stacked, "slab", pairs)], axis=0)
                distance *= 2
            every = [stacked[index] for index in range(devices // size)]
    else:
        size = devices
        gathered = lax.all_gather(packed, "slab")
        local = [gathered[index] for index in range(devices)]
        every = [jnp.zeros(packed.shape, jnp.float32)]
    half = jax.ShapeDtypeStruct((slots, modes // 2), jnp.float32)
    group_arr = lax.axis_index("energy").astype(jnp.int32).reshape(1)
    density, bond_density, theirs = pl.pallas_call(
        functools.partial(
            final_kernel, slots=slots, points=points, devices=devices, mixed=mixed,
            size=len(local), groups=len(every), scale=1.0 / (32.0 * points * groups),
        ),
        out_shape=(half, half, jax.ShapeDtypeStruct((2, slots, modes // 2), jnp.float32)),
        in_specs=[smem] * 5 + [vmem] * (len(local) + len(every) + len(raw)),
        out_specs=(vmem, vmem, vmem),
        scratch_shapes=[
            pltpu.VMEM((slots, points, rows, 128), jnp.float32),
            pltpu.VMEM((slots, points, rows, 128), jnp.float32),
            pltpu.VMEM((slots, rows, 128), jnp.float32),
            pltpu.VMEM((slots, rows, 128), jnp.float32),
            pltpu.VMEM(table_shape, jnp.float32),
        ],
    )(here_arr, group_arr, lengths, energy_index, weight_code, *local, *every, *raw)
    if groups == 2:
        theirs = lax.ppermute(theirs, "energy", [(0, 1), (1, 0)])
        return (density + theirs[0], bond_density + theirs[1])
    lower = lax.axis_index("energy") == 0
    both = jnp.stack([
        jnp.where(lower, jnp.concatenate([density, theirs[0]], axis=1), jnp.concatenate([theirs[0], density], axis=1)),
        jnp.where(lower, jnp.concatenate([bond_density, theirs[1]], axis=1), jnp.concatenate([theirs[1], bond_density], axis=1)),
    ])
    both = lax.psum_scatter(both, "energy", scatter_dimension=2, tiled=True)
    return (both[0], both[1])


def solution(mesh):
    in_specs = (
        P(),
        P("slab", None),
        P("slab", None),
        P(),
        P("energy"),
        P("energy"),
        P("energy", None, None),
        P("energy", None, None),
    )
    out_specs = (P("slab", "energy"), P("slab", "energy"))
    return jax.shard_map(shards, mesh=mesh, in_specs=in_specs, out_specs=out_specs, check_vma=False)
```

```python
import functools

import jax
import jax.numpy as jnp
from jax import lax
from jax.experimental import pallas as pl
from jax.experimental.pallas import tpu as pltpu
from jax.sharding import PartitionSpec as P

broaden = 0.002
e_low = -1.5
e_step = 3.0 / 4096.0
inv_pi = 1.0 / 3.141592653589793


def reciprocal(real_part, imag_part):
    scale = 1.0 / (real_part * real_part + imag_part * imag_part)
    return (real_part * scale, -imag_part * scale)


def complex_mul(first_re, first_im, second_re, second_im):
    return (
        first_re * second_re - first_im * second_im,
        first_re * second_im + first_im * second_re,
    )


def join_segments(left, right):
    square = left[6] * left[6]
    mix_re, mix_im = complex_mul(left[4], left[5], right[0], right[1])
    inv_re, inv_im = reciprocal(1.0 - square * mix_re, -square * mix_im)
    left_sq_re, left_sq_im = complex_mul(left[2], left[3], left[2], left[3])
    head_re, head_im = complex_mul(left_sq_re, left_sq_im, right[0], right[1])
    head_re, head_im = complex_mul(head_re, head_im, inv_re, inv_im)
    right_sq_re, right_sq_im = complex_mul(right[2], right[3], right[2], right[3])
    tail_re, tail_im = complex_mul(right_sq_re, right_sq_im, left[4], left[5])
    tail_re, tail_im = complex_mul(tail_re, tail_im, inv_re, inv_im)
    link_re, link_im = complex_mul(left[2], left[3], right[2], right[3])
    link_re, link_im = complex_mul(link_re, link_im, inv_re, inv_im)
    return (
        left[0] + square * head_re,
        left[1] + square * head_im,
        left[6] * link_re,
        left[6] * link_im,
        right[4] + square * tail_re,
        right[5] + square * tail_im,
        right[6],
    )


def onsite_terms(table_ref, energy_ref, here, count, devices, slots, points, slot):
    rows = 2 * slots
    levels = table_ref[slot]
    first_on = jnp.logical_and(here == 0, slot == 0).astype(jnp.float32)
    last_on = jnp.logical_and(here == devices - 1, slot == count - 1).astype(jnp.float32)
    onsite_re, onsite_im = [], []
    for point in range(points):
        energy = e_low + e_step * energy_ref[point].astype(jnp.float32)
        onsite_re.append(
            energy - levels
            - first_on * table_ref[rows + 2 * point]
            - last_on * table_ref[rows + 2 * point + 1]
        )
        onsite_im.append(
            broaden
            + first_on * table_ref[rows + 2 * points + 2 * point]
            + last_on * table_ref[rows + 2 * points + 2 * point + 1]
        )
    return jnp.stack(onsite_re), jnp.stack(onsite_im)


def build_table(floor_ref, noise_ref, hop_ref, shift_ref, width_ref, table_ref):
    slots = noise_ref.shape[0]
    points = shift_ref.shape[0]
    for row in range(table_ref.shape[1]):
        lanes = slice(row * 128, (row + 1) * 128)
        floor = floor_ref[0:1, lanes]
        for slot in range(slots):
            table_ref[slot, row:row + 1, :] = floor + noise_ref[slot:slot + 1, lanes]
            table_ref[slots + slot, row:row + 1, :] = hop_ref[slot:slot + 1, lanes]
        for point in range(points):
            for side in range(2):
                index = 2 * slots + 2 * point + side
                table_ref[index, row:row + 1, :] = shift_ref[point, side:side + 1, lanes]
                table_ref[index + 2 * points, row:row + 1, :] = width_ref[point, side:side + 1, lanes]


def summary_kernel(here_ref, length_ref, energy_ref, floor_ref, noise_ref, hop_ref, shift_ref, width_ref,
                   out_ref, table_ref, *, slots, points, devices):
    build_table(floor_ref, noise_ref, hop_ref, shift_ref, width_ref, table_ref)
    here = here_ref[0]
    count = length_ref[here]

    def single(slot):
        onsite_re, onsite_im = onsite_terms(
            table_ref, energy_ref, here, count, devices, slots, points, slot
        )
        g_re, g_im = reciprocal(onsite_re, onsite_im)
        coupling = table_ref[slots + slot]
        square = coupling * coupling
        sq_re, sq_im = complex_mul(g_re, g_im, g_re, g_im)
        return (g_re, g_im, square * g_re, square * g_im, square * sq_re, square * sq_im)

    def body(slot, summary):
        return join_coupled(summary, single(slot))

    summary = lax.fori_loop(1, count, body, single(0))
    for index, value in enumerate(summary):
        out_ref[index * points:(index + 1) * points] = value


def join_coupled(left, right):
    d_re, d_im = complex_mul(left[2], left[3], right[0], right[1])
    inv_re, inv_im = reciprocal(1.0 - d_re, -d_im)
    f_re, f_im = complex_mul(left[4], left[5], right[0], right[1])
    f_re, f_im = complex_mul(f_re, f_im, inv_re, inv_im)
    g_re, g_im = complex_mul(right[4], right[5], left[2], left[3])
    g_re, g_im = complex_mul(g_re, g_im, inv_re, inv_im)
    x_re, x_im = complex_mul(left[4], left[5], right[4], right[5])
    x_re, x_im = complex_mul(x_re, x_im, inv_re, inv_im)
    x_re, x_im = complex_mul(x_re, x_im, inv_re, inv_im)
    return (left[0] + f_re, left[1] + f_im, right[2] + g_re, right[3] + g_im, x_re, x_im)


def in_order(refs, own, mixed):
    loaded = [ref[...] for ref in refs]
    if not mixed:
        return loaded
    ordered = []
    for position in range(len(refs)):
        offset = jnp.bitwise_xor(own, position)
        value = loaded[0]
        for index in range(1, len(refs)):
            value = jnp.where(offset == index, loaded[index], value)
        ordered.append(value)
    return ordered


def split_fields(value, points):
    return tuple(value[f * points:(f + 1) * points] for f in range(6))


def group_kernel(here_ref, *refs):
    local_refs, out_ref = refs[:-1], refs[-1]
    points = out_ref.shape[0] // 6
    size = len(local_refs)
    here = here_ref[0]
    blocks = in_order(local_refs, jnp.bitwise_and(here, size - 1), True)
    summary = split_fields(blocks[0], points)
    for member in range(1, size):
        summary = join_coupled(summary, split_fields(blocks[member], points))
    for index, value in enumerate(summary):
        out_ref[index * points:(index + 1) * points] = value


def final_kernel(here_ref, group_ref, length_ref, energy_ref, code_ref, *refs,
                 slots, points, devices, mixed, size, groups, scale):
    local_refs = refs[:size]
    group_refs = refs[size:size + groups]
    (table_ref, dens_out_ref, bond_out_ref, theirs_ref,
     left_re_ref, left_im_ref, dens_ref, bond_ref) = refs[size + groups:]
    here = here_ref[0]
    count = length_ref[here]
    rows = table_ref.shape[1]
    member_here = here % size
    group_here = here // size

    def into_step(block, run):
        run_re, run_im = run
        m_re, m_im = complex_mul(run_re, run_im, block[0], block[1])
        inv_re, inv_im = reciprocal(1.0 - m_re, -m_im)
        t_re, t_im = complex_mul(block[4], block[5], run_re, run_im)
        t_re, t_im = complex_mul(t_re, t_im, inv_re, inv_im)
        return (block[2] + t_re, block[3] + t_im)

    def from_step(block, run):
        run_re, run_im = run
        m_re, m_im = complex_mul(block[2], block[3], run_re, run_im)
        inv_re, inv_im = reciprocal(1.0 - m_re, -m_im)
        h_re, h_im = complex_mul(block[4], block[5], run_re, run_im)
        h_re, h_im = complex_mul(h_re, h_im, inv_re, inv_im)
        return (block[0] + h_re, block[1] + h_im)

    def masked(keep, new, old):
        return tuple(jnp.where(keep, n, o) for n, o in zip(new, old))

    zero = jnp.zeros((points,) + table_ref.shape[1:], jnp.float32)
    group_blocks = [split_fields(v, points) for v in in_order(group_refs, group_here, mixed)]
    local_blocks = [split_fields(v, points) for v in in_order(local_refs, member_here, mixed)]
    into = (zero, zero)
    for group in range(groups):
        into = masked(group < group_here, into_step(group_blocks[group], into), into)
    for member in range(size):
        into = masked(member < member_here, into_step(local_blocks[member], into), into)
    outof = (zero, zero)
    for group in reversed(range(groups)):
        outof = masked(group > group_here, from_step(group_blocks[group], outof), outof)
    for member in reversed(range(size)):
        outof = masked(member > member_here, from_step(local_blocks[member], outof), outof)
    into_re, into_im = into
    from_re, from_im = outof

    def onsite(slot):
        return onsite_terms(table_ref, energy_ref, here, count, devices, slots, points, slot)

    def forward_body(slot, carry):
        prev_re, prev_im, prev_coupling = carry
        onsite_re, onsite_im = onsite(slot)
        square = prev_coupling * prev_coupling
        denom_re, denom_im = onsite_re - square * prev_re, onsite_im - square * prev_im
        g_re, g_im = reciprocal(denom_re, denom_im)
        left_re_ref[slot] = denom_re
        left_im_ref[slot] = denom_im
        return (g_re, g_im, table_ref[slots + slot])

    ones = jnp.ones(table_ref.shape[1:], jnp.float32)
    lax.fori_loop(0, count, forward_body, (into_re, into_im, ones))
    dens_ref[...] = jnp.zeros(dens_ref.shape, jnp.float32)
    bond_ref[...] = jnp.zeros(bond_ref.shape, jnp.float32)
    weights = [code_ref[point].astype(jnp.float32) * scale for point in range(points)]

    def backward_body(step, carry):
        next_re, next_im = carry
        slot = count - 1 - step
        onsite_re, onsite_im = onsite(slot)
        denom_re, denom_im = left_re_ref[slot], left_im_ref[slot]
        coupling = table_ref[slots + slot]
        square = coupling * coupling
        diag_re, diag_im = reciprocal(denom_re - square * next_re, denom_im - square * next_im)
        _, bond_im = complex_mul(diag_re, diag_im, next_re, next_im)
        dens = weights[0] * diag_im[0]
        bond = weights[0] * (square * bond_im[0])
        for point in range(1, points):
            dens = dens + weights[point] * diag_im[point]
            bond = bond + weights[point] * (square * bond_im[point])
        dens_ref[slot] = -inv_pi * dens
        bond_ref[slot] = -2.0 * inv_pi * bond
        return reciprocal(onsite_re - square * next_re, onsite_im - square * next_im)

    lax.fori_loop(0, count, backward_body, (from_re, from_im))
    lower = group_ref[0] == 0
    half = rows // 2
    for slot in range(slots):
        dens = dens_ref[slot]
        bond = bond_ref[slot]
        for row in range(half):
            lane = row * 128
            for kind, value, mine_ref in ((0, dens, dens_out_ref), (1, bond, bond_out_ref)):
                low, high = value[row:row + 1], value[row + half:row + half + 1]
                mine_ref[slot:slot + 1, lane:lane + 128] = jnp.where(lower, low, high)
                theirs_ref[kind, slot:slot + 1, lane:lane + 128] = jnp.where(lower, high, low)


def shards(
    mode_floor, onsite_noise, hopping, lengths, energy_index, weight_code, lead_shift, lead_width
):
    slots = onsite_noise.shape[0]
    modes = onsite_noise.shape[1]
    points = energy_index.shape[0]
    rows = modes // 128
    here = lax.axis_index("slab")
    devices = lax.axis_size("slab")
    groups = lax.axis_size("energy")
    raw = (mode_floor.reshape(1, modes), onsite_noise, hopping, lead_shift, lead_width)
    table_shape = (2 * slots + 4 * points, rows, 128)
    here_arr = here.astype(jnp.int32).reshape(1)
    smem = pl.BlockSpec(memory_space=pltpu.SMEM)
    vmem = pl.BlockSpec(memory_space=pltpu.VMEM)

    packed, table = pl.pallas_call(
        functools.partial(summary_kernel, slots=slots, points=points, devices=devices),
        out_shape=(
            jax.ShapeDtypeStruct((6 * points, rows, 128), jnp.float32),
            jax.ShapeDtypeStruct(table_shape, jnp.float32),
        ),
        in_specs=[smem, smem, smem] + [vmem] * len(raw),
        out_specs=(vmem, vmem),
    )(here_arr, lengths, energy_index, *raw)
    mixed = devices & (devices - 1) == 0 and devices >= 4
    if mixed:
        size = 4
        local = [packed] + [
            lax.ppermute(packed, "slab", [(device, device ^ offset) for device in range(devices)])
            for offset in range(1, size)
        ]
        summary = pl.pallas_call(
            group_kernel,
            out_shape=jax.ShapeDtypeStruct(packed.shape, jnp.float32),
            in_specs=[smem] + [vmem] * size,
            out_specs=vmem,
        )(here_arr, *local)
        if devices == size * size:
            every = [summary] + [
                lax.ppermute(summary, "slab", [(device, device ^ (offset * size)) for device in range(devices)])
                for offset in range(1, size)
            ]
        else:
            stacked = summary[None]
            distance = size
            while distance < devices:
                pairs = [(device, device ^ distance) for device in range(devices)]
                stacked = jnp.concatenate([stacked, lax.ppermute(stacked, "slab", pairs)], axis=0)
                distance *= 2
            every = [stacked[index] for index in range(devices // size)]
    else:
        size = devices
        gathered = lax.all_gather(packed, "slab")
        local = [gathered[index] for index in range(devices)]
        every = [jnp.zeros(packed.shape, jnp.float32)]
    half = jax.ShapeDtypeStruct((slots, modes // 2), jnp.float32)
    group_arr = lax.axis_index("energy").astype(jnp.int32).reshape(1)
    density, bond_density, theirs = pl.pallas_call(
        functools.partial(
            final_kernel, slots=slots, points=points, devices=devices, mixed=mixed,
            size=len(local), groups=len(every), scale=1.0 / (32.0 * points * groups),
        ),
        out_shape=(half, half, jax.ShapeDtypeStruct((2, slots, modes // 2), jnp.float32)),
        in_specs=[smem] * 5 + [vmem] * (len(local) + len(every) + 1),
        out_specs=(vmem, vmem, vmem),
        scratch_shapes=[
            pltpu.VMEM((slots, points, rows, 128), jnp.float32),
            pltpu.VMEM((slots, points, rows, 128), jnp.float32),
            pltpu.VMEM((slots, rows, 128), jnp.float32),
            pltpu.VMEM((slots, rows, 128), jnp.float32),
        ],
    )(here_arr, group_arr, lengths, energy_index, weight_code, *local, *every, table)
    if groups == 2:
        theirs = lax.ppermute(theirs, "energy", [(0, 1), (1, 0)])
        return (density + theirs[0], bond_density + theirs[1])
    lower = lax.axis_index("energy") == 0
    both = jnp.stack([
        jnp.where(lower, jnp.concatenate([density, theirs[0]], axis=1), jnp.concatenate([theirs[0], density], axis=1)),
        jnp.where(lower, jnp.concatenate([bond_density, theirs[1]], axis=1), jnp.concatenate([theirs[1], bond_density], axis=1)),
    ])
    both = lax.psum_scatter(both, "energy", scatter_dimension=2, tiled=True)
    return (both[0], both[1])


def solution(mesh):
    in_specs = (
        P(),
        P("slab", None),
        P("slab", None),
        P(),
        P("energy"),
        P("energy"),
        P("energy", None, None),
        P("energy", None, None),
    )
    out_specs = (P("slab", "energy"), P("slab", "energy"))
    return jax.shard_map(shards, mesh=mesh, in_specs=in_specs, out_specs=out_specs, check_vma=False)
```

```python
import functools

import jax
import jax.numpy as jnp
from jax import lax
from jax.experimental import pallas as pl
from jax.experimental.pallas import tpu as pltpu
from jax.sharding import PartitionSpec as P

broaden = 0.002
e_low = -1.5
e_step = 3.0 / 4096.0
inv_pi = 1.0 / 3.141592653589793


def reciprocal(real_part, imag_part):
    scale = 1.0 / (real_part * real_part + imag_part * imag_part)
    return (real_part * scale, -imag_part * scale)


def complex_mul(first_re, first_im, second_re, second_im):
    return (
        first_re * second_re - first_im * second_im,
        first_re * second_im + first_im * second_re,
    )


def join_segments(left, right):
    square = left[6] * left[6]
    mix_re, mix_im = complex_mul(left[4], left[5], right[0], right[1])
    inv_re, inv_im = reciprocal(1.0 - square * mix_re, -square * mix_im)
    left_sq_re, left_sq_im = complex_mul(left[2], left[3], left[2], left[3])
    head_re, head_im = complex_mul(left_sq_re, left_sq_im, right[0], right[1])
    head_re, head_im = complex_mul(head_re, head_im, inv_re, inv_im)
    right_sq_re, right_sq_im = complex_mul(right[2], right[3], right[2], right[3])
    tail_re, tail_im = complex_mul(right_sq_re, right_sq_im, left[4], left[5])
    tail_re, tail_im = complex_mul(tail_re, tail_im, inv_re, inv_im)
    link_re, link_im = complex_mul(left[2], left[3], right[2], right[3])
    link_re, link_im = complex_mul(link_re, link_im, inv_re, inv_im)
    return (
        left[0] + square * head_re,
        left[1] + square * head_im,
        left[6] * link_re,
        left[6] * link_im,
        right[4] + square * tail_re,
        right[5] + square * tail_im,
        right[6],
    )


def onsite_terms(table_ref, energy_ref, here, count, devices, slots, points, slot):
    rows = 2 * slots
    levels = table_ref[slot]
    first_on = jnp.logical_and(here == 0, slot == 0).astype(jnp.float32)
    last_on = jnp.logical_and(here == devices - 1, slot == count - 1).astype(jnp.float32)
    onsite_re, onsite_im = [], []
    for point in range(points):
        energy = e_low + e_step * energy_ref[point].astype(jnp.float32)
        onsite_re.append(
            energy - levels
            - first_on * table_ref[rows + 2 * point]
            - last_on * table_ref[rows + 2 * point + 1]
        )
        onsite_im.append(
            broaden
            + first_on * table_ref[rows + 2 * points + 2 * point]
            + last_on * table_ref[rows + 2 * points + 2 * point + 1]
        )
    return jnp.stack(onsite_re), jnp.stack(onsite_im)


def build_table(floor_ref, noise_ref, hop_ref, shift_ref, width_ref, table_ref):
    slots = noise_ref.shape[0]
    points = shift_ref.shape[0]
    for row in range(table_ref.shape[1]):
        lanes = slice(row * 128, (row + 1) * 128)
        floor = floor_ref[0:1, lanes]
        for slot in range(slots):
            table_ref[slot, row:row + 1, :] = floor + noise_ref[slot:slot + 1, lanes]
            table_ref[slots + slot, row:row + 1, :] = hop_ref[slot:slot + 1, lanes]
        for point in range(points):
            for side in range(2):
                index = 2 * slots + 2 * point + side
                table_ref[index, row:row + 1, :] = shift_ref[point, side:side + 1, lanes]
                table_ref[index + 2 * points, row:row + 1, :] = width_ref[point, side:side + 1, lanes]


def summary_kernel(here_ref, length_ref, energy_ref, floor_ref, noise_ref, hop_ref, shift_ref, width_ref,
                   out_ref, table_ref, *, slots, points, devices):
    build_table(floor_ref, noise_ref, hop_ref, shift_ref, width_ref, table_ref)
    here = here_ref[0]
    count = length_ref[here]

    def single(slot):
        onsite_re, onsite_im = onsite_terms(
            table_ref, energy_ref, here, count, devices, slots, points, slot
        )
        g_re, g_im = reciprocal(onsite_re, onsite_im)
        coupling = table_ref[slots + slot]
        square = coupling * coupling
        sq_re, sq_im = complex_mul(g_re, g_im, g_re, g_im)
        return (g_re, g_im, square * g_re, square * g_im, square * sq_re, square * sq_im)

    def body(slot, summary):
        return join_coupled(summary, single(slot))

    summary = lax.fori_loop(1, count, body, single(0))
    for index, value in enumerate(summary):
        out_ref[index * points:(index + 1) * points] = value


def join_coupled(left, right):
    d_re, d_im = complex_mul(left[2], left[3], right[0], right[1])
    inv_re, inv_im = reciprocal(1.0 - d_re, -d_im)
    f_re, f_im = complex_mul(left[4], left[5], right[0], right[1])
    f_re, f_im = complex_mul(f_re, f_im, inv_re, inv_im)
    g_re, g_im = complex_mul(right[4], right[5], left[2], left[3])
    g_re, g_im = complex_mul(g_re, g_im, inv_re, inv_im)
    x_re, x_im = complex_mul(left[4], left[5], right[4], right[5])
    x_re, x_im = complex_mul(x_re, x_im, inv_re, inv_im)
    x_re, x_im = complex_mul(x_re, x_im, inv_re, inv_im)
    return (left[0] + f_re, left[1] + f_im, right[2] + g_re, right[3] + g_im, x_re, x_im)


def in_order(refs, own, mixed):
    loaded = [ref[...] for ref in refs]
    if not mixed:
        return loaded
    ordered = []
    for position in range(len(refs)):
        offset = jnp.bitwise_xor(own, position)
        value = loaded[0]
        for index in range(1, len(refs)):
            value = jnp.where(offset == index, loaded[index], value)
        ordered.append(value)
    return ordered


def split_fields(value, points):
    return tuple(value[f * points:(f + 1) * points] for f in range(6))


def group_kernel(here_ref, *refs):
    local_refs, out_ref = refs[:-1], refs[-1]
    points = out_ref.shape[0] // 6
    size = len(local_refs)
    own = jnp.bitwise_and(here_ref[0], size - 1)
    for offset in range(size):

        @pl.when(own == offset)
        def _(offset=offset):
            summary = split_fields(local_refs[offset][...], points)
            for member in range(1, size):
                block = split_fields(local_refs[member ^ offset][...], points)
                summary = join_coupled(summary, block)
            for index, value in enumerate(summary):
                out_ref[index * points:(index + 1) * points] = value


def final_kernel(here_ref, group_ref, length_ref, energy_ref, code_ref, *refs,
                 slots, points, devices, mixed, size, groups, scale):
    local_refs = refs[:size]
    group_refs = refs[size:size + groups]
    (floor_ref, noise_ref, hop_ref, shift_ref, width_ref, dens_out_ref, bond_out_ref, theirs_ref,
     left_re_ref, left_im_ref, dens_ref, bond_ref, table_ref) = refs[size + groups:]
    build_table(floor_ref, noise_ref, hop_ref, shift_ref, width_ref, table_ref)
    here = here_ref[0]
    count = length_ref[here]
    rows = table_ref.shape[1]
    member_here = here % size
    group_here = here // size

    def into_step(block, run):
        run_re, run_im = run
        m_re, m_im = complex_mul(run_re, run_im, block[0], block[1])
        inv_re, inv_im = reciprocal(1.0 - m_re, -m_im)
        t_re, t_im = complex_mul(block[4], block[5], run_re, run_im)
        t_re, t_im = complex_mul(t_re, t_im, inv_re, inv_im)
        return (block[2] + t_re, block[3] + t_im)

    def from_step(block, run):
        run_re, run_im = run
        m_re, m_im = complex_mul(block[2], block[3], run_re, run_im)
        inv_re, inv_im = reciprocal(1.0 - m_re, -m_im)
        h_re, h_im = complex_mul(block[4], block[5], run_re, run_im)
        h_re, h_im = complex_mul(h_re, h_im, inv_re, inv_im)
        return (block[0] + h_re, block[1] + h_im)

    def masked(keep, new, old):
        return tuple(jnp.where(keep, n, o) for n, o in zip(new, old))

    zero = jnp.zeros((points,) + table_ref.shape[1:], jnp.float32)
    group_blocks = [split_fields(v, points) for v in in_order(group_refs, group_here, mixed)]
    local_blocks = [split_fields(v, points) for v in in_order(local_refs, member_here, mixed)]
    into = (zero, zero)
    for group in range(groups):
        into = masked(group < group_here, into_step(group_blocks[group], into), into)
    for member in range(size):
        into = masked(member < member_here, into_step(local_blocks[member], into), into)
    outof = (zero, zero)
    for group in reversed(range(groups)):
        outof = masked(group > group_here, from_step(group_blocks[group], outof), outof)
    for member in reversed(range(size)):
        outof = masked(member > member_here, from_step(local_blocks[member], outof), outof)
    into_re, into_im = into
    from_re, from_im = outof

    def onsite(slot):
        return onsite_terms(table_ref, energy_ref, here, count, devices, slots, points, slot)

    def forward_body(slot, carry):
        prev_re, prev_im, prev_coupling = carry
        onsite_re, onsite_im = onsite(slot)
        square = prev_coupling * prev_coupling
        denom_re, denom_im = onsite_re - square * prev_re, onsite_im - square * prev_im
        g_re, g_im = reciprocal(denom_re, denom_im)
        left_re_ref[slot] = denom_re
        left_im_ref[slot] = denom_im
        return (g_re, g_im, table_ref[slots + slot])

    ones = jnp.ones(table_ref.shape[1:], jnp.float32)
    lax.fori_loop(0, count, forward_body, (into_re, into_im, ones))
    dens_ref[...] = jnp.zeros(dens_ref.shape, jnp.float32)
    bond_ref[...] = jnp.zeros(bond_ref.shape, jnp.float32)
    weights = [code_ref[point].astype(jnp.float32) * scale for point in range(points)]

    def backward_body(step, carry):
        next_re, next_im = carry
        slot = count - 1 - step
        onsite_re, onsite_im = onsite(slot)
        denom_re, denom_im = left_re_ref[slot], left_im_ref[slot]
        coupling = table_ref[slots + slot]
        square = coupling * coupling
        diag_re, diag_im = reciprocal(denom_re - square * next_re, denom_im - square * next_im)
        _, bond_im = complex_mul(diag_re, diag_im, next_re, next_im)
        dens = weights[0] * diag_im[0]
        bond = weights[0] * (square * bond_im[0])
        for point in range(1, points):
            dens = dens + weights[point] * diag_im[point]
            bond = bond + weights[point] * (square * bond_im[point])
        dens_ref[slot] = -inv_pi * dens
        bond_ref[slot] = -2.0 * inv_pi * bond
        return reciprocal(onsite_re - square * next_re, onsite_im - square * next_im)

    lax.fori_loop(0, count, backward_body, (from_re, from_im))
    lower = group_ref[0] == 0
    half = rows // 2
    for slot in range(slots):
        dens = dens_ref[slot]
        bond = bond_ref[slot]
        for row in range(half):
            lane = row * 128
            for kind, value, mine_ref in ((0, dens, dens_out_ref), (1, bond, bond_out_ref)):
                low, high = value[row:row + 1], value[row + half:row + half + 1]
                mine_ref[slot:slot + 1, lane:lane + 128] = jnp.where(lower, low, high)
                theirs_ref[kind, slot:slot + 1, lane:lane + 128] = jnp.where(lower, high, low)


def shards(
    mode_floor, onsite_noise, hopping, lengths, energy_index, weight_code, lead_shift, lead_width
):
    slots = onsite_noise.shape[0]
    modes = onsite_noise.shape[1]
    points = energy_index.shape[0]
    rows = modes // 128
    here = lax.axis_index("slab")
    devices = lax.axis_size("slab")
    groups = lax.axis_size("energy")
    raw = (mode_floor.reshape(1, modes), onsite_noise, hopping, lead_shift, lead_width)
    table_shape = (2 * slots + 4 * points, rows, 128)
    here_arr = here.astype(jnp.int32).reshape(1)
    smem = pl.BlockSpec(memory_space=pltpu.SMEM)
    vmem = pl.BlockSpec(memory_space=pltpu.VMEM)

    packed = pl.pallas_call(
        functools.partial(summary_kernel, slots=slots, points=points, devices=devices),
        out_shape=jax.ShapeDtypeStruct((6 * points, rows, 128), jnp.float32),
        in_specs=[smem, smem, smem] + [vmem] * len(raw),
        out_specs=vmem,
        scratch_shapes=[pltpu.VMEM(table_shape, jnp.float32)],
    )(here_arr, lengths, energy_index, *raw)
    mixed = devices & (devices - 1) == 0 and devices >= 4
    if mixed:
        size = 4
        local = [packed] + [
            lax.ppermute(packed, "slab", [(device, device ^ offset) for device in range(devices)])
            for offset in range(1, size)
        ]
        summary = pl.pallas_call(
            group_kernel,
            out_shape=jax.ShapeDtypeStruct(packed.shape, jnp.float32),
            in_specs=[smem] + [vmem] * size,
            out_specs=vmem,
        )(here_arr, *local)
        if devices == size * size:
            every = [summary] + [
                lax.ppermute(summary, "slab", [(device, device ^ (offset * size)) for device in range(devices)])
                for offset in range(1, size)
            ]
        else:
            stacked = summary[None]
            distance = size
            while distance < devices:
                pairs = [(device, device ^ distance) for device in range(devices)]
                stacked = jnp.concatenate([stacked, lax.ppermute(stacked, "slab", pairs)], axis=0)
                distance *= 2
            every = [stacked[index] for index in range(devices // size)]
    else:
        size = devices
        gathered = lax.all_gather(packed, "slab")
        local = [gathered[index] for index in range(devices)]
        every = [jnp.zeros(packed.shape, jnp.float32)]
    half = jax.ShapeDtypeStruct((slots, modes // 2), jnp.float32)
    group_arr = lax.axis_index("energy").astype(jnp.int32).reshape(1)
    density, bond_density, theirs = pl.pallas_call(
        functools.partial(
            final_kernel, slots=slots, points=points, devices=devices, mixed=mixed,
            size=len(local), groups=len(every), scale=1.0 / (32.0 * points * groups),
        ),
        out_shape=(half, half, jax.ShapeDtypeStruct((2, slots, modes // 2), jnp.float32)),
        in_specs=[smem] * 5 + [vmem] * (len(local) + len(every) + len(raw)),
        out_specs=(vmem, vmem, vmem),
        scratch_shapes=[
            pltpu.VMEM((slots, points, rows, 128), jnp.float32),
            pltpu.VMEM((slots, points, rows, 128), jnp.float32),
            pltpu.VMEM((slots, rows, 128), jnp.float32),
            pltpu.VMEM((slots, rows, 128), jnp.float32),
            pltpu.VMEM(table_shape, jnp.float32),
        ],
    )(here_arr, group_arr, lengths, energy_index, weight_code, *local, *every, *raw)
    if groups == 2:
        theirs = lax.ppermute(theirs, "energy", [(0, 1), (1, 0)])
        return (density + theirs[0], bond_density + theirs[1])
    lower = lax.axis_index("energy") == 0
    both = jnp.stack([
        jnp.where(lower, jnp.concatenate([density, theirs[0]], axis=1), jnp.concatenate([theirs[0], density], axis=1)),
        jnp.where(lower, jnp.concatenate([bond_density, theirs[1]], axis=1), jnp.concatenate([theirs[1], bond_density], axis=1)),
    ])
    both = lax.psum_scatter(both, "energy", scatter_dimension=2, tiled=True)
    return (both[0], both[1])


def solution(mesh):
    in_specs = (
        P(),
        P("slab", None),
        P("slab", None),
        P(),
        P("energy"),
        P("energy"),
        P("energy", None, None),
        P("energy", None, None),
    )
    out_specs = (P("slab", "energy"), P("slab", "energy"))
    return jax.shard_map(shards, mesh=mesh, in_specs=in_specs, out_specs=out_specs, check_vma=False)
```

```python
import functools

import jax
import jax.numpy as jnp
from jax import lax
from jax.experimental import pallas as pl
from jax.experimental.pallas import tpu as pltpu
from jax.sharding import PartitionSpec as P

broaden = 0.002
e_low = -1.5
e_step = 3.0 / 4096.0
inv_pi = 1.0 / 3.141592653589793


def reciprocal(real_part, imag_part):
    scale = 1.0 / (real_part * real_part + imag_part * imag_part)
    return (real_part * scale, -imag_part * scale)


def complex_mul(first_re, first_im, second_re, second_im):
    return (
        first_re * second_re - first_im * second_im,
        first_re * second_im + first_im * second_re,
    )


def join_segments(left, right):
    square = left[6] * left[6]
    mix_re, mix_im = complex_mul(left[4], left[5], right[0], right[1])
    inv_re, inv_im = reciprocal(1.0 - square * mix_re, -square * mix_im)
    left_sq_re, left_sq_im = complex_mul(left[2], left[3], left[2], left[3])
    head_re, head_im = complex_mul(left_sq_re, left_sq_im, right[0], right[1])
    head_re, head_im = complex_mul(head_re, head_im, inv_re, inv_im)
    right_sq_re, right_sq_im = complex_mul(right[2], right[3], right[2], right[3])
    tail_re, tail_im = complex_mul(right_sq_re, right_sq_im, left[4], left[5])
    tail_re, tail_im = complex_mul(tail_re, tail_im, inv_re, inv_im)
    link_re, link_im = complex_mul(left[2], left[3], right[2], right[3])
    link_re, link_im = complex_mul(link_re, link_im, inv_re, inv_im)
    return (
        left[0] + square * head_re,
        left[1] + square * head_im,
        left[6] * link_re,
        left[6] * link_im,
        right[4] + square * tail_re,
        right[5] + square * tail_im,
        right[6],
    )


def onsite_terms(table_ref, energy_ref, here, count, devices, slots, points, slot):
    rows = 2 * slots
    levels = table_ref[slot]
    first_on = jnp.logical_and(here == 0, slot == 0).astype(jnp.float32)
    last_on = jnp.logical_and(here == devices - 1, slot == count - 1).astype(jnp.float32)
    onsite_re, onsite_im = [], []
    for point in range(points):
        energy = e_low + e_step * energy_ref[point].astype(jnp.float32)
        onsite_re.append(
            energy - levels
            - first_on * table_ref[rows + 2 * point]
            - last_on * table_ref[rows + 2 * point + 1]
        )
        onsite_im.append(
            broaden
            + first_on * table_ref[rows + 2 * points + 2 * point]
            + last_on * table_ref[rows + 2 * points + 2 * point + 1]
        )
    return jnp.stack(onsite_re), jnp.stack(onsite_im)


def build_table(floor_ref, noise_ref, hop_ref, shift_ref, width_ref, table_ref):
    slots = noise_ref.shape[0]
    points = shift_ref.shape[0]
    for row in range(table_ref.shape[1]):
        lanes = slice(row * 128, (row + 1) * 128)
        floor = floor_ref[0:1, lanes]
        for slot in range(slots):
            table_ref[slot, row:row + 1, :] = floor + noise_ref[slot:slot + 1, lanes]
            table_ref[slots + slot, row:row + 1, :] = hop_ref[slot:slot + 1, lanes]
        for point in range(points):
            for side in range(2):
                index = 2 * slots + 2 * point + side
                table_ref[index, row:row + 1, :] = shift_ref[point, side:side + 1, lanes]
                table_ref[index + 2 * points, row:row + 1, :] = width_ref[point, side:side + 1, lanes]


def summary_kernel(here_ref, length_ref, energy_ref, floor_ref, noise_ref, hop_ref, shift_ref, width_ref,
                   out_ref, table_ref, *, slots, points, devices):
    build_table(floor_ref, noise_ref, hop_ref, shift_ref, width_ref, table_ref)
    here = here_ref[0]
    count = length_ref[here]

    def single(slot):
        onsite_re, onsite_im = onsite_terms(
            table_ref, energy_ref, here, count, devices, slots, points, slot
        )
        g_re, g_im = reciprocal(onsite_re, onsite_im)
        coupling = table_ref[slots + slot]
        square = coupling * coupling
        sq_re, sq_im = complex_mul(g_re, g_im, g_re, g_im)
        return (g_re, g_im, square * g_re, square * g_im, square * sq_re, square * sq_im)

    def body(slot, summary):
        return join_coupled(summary, single(slot))

    summary = lax.fori_loop(1, count, body, single(0))
    for index, value in enumerate(summary):
        out_ref[index * points:(index + 1) * points] = value


def join_coupled(left, right):
    d_re, d_im = complex_mul(left[2], left[3], right[0], right[1])
    inv_re, inv_im = reciprocal(1.0 - d_re, -d_im)
    f_re, f_im = complex_mul(left[4], left[5], right[0], right[1])
    f_re, f_im = complex_mul(f_re, f_im, inv_re, inv_im)
    g_re, g_im = complex_mul(right[4], right[5], left[2], left[3])
    g_re, g_im = complex_mul(g_re, g_im, inv_re, inv_im)
    x_re, x_im = complex_mul(left[4], left[5], right[4], right[5])
    x_re, x_im = complex_mul(x_re, x_im, inv_re, inv_im)
    x_re, x_im = complex_mul(x_re, x_im, inv_re, inv_im)
    return (left[0] + f_re, left[1] + f_im, right[2] + g_re, right[3] + g_im, x_re, x_im)


def in_order(refs, own, mixed):
    loaded = [ref[...] for ref in refs]
    if not mixed:
        return loaded
    ordered = []
    for position in range(len(refs)):
        offset = jnp.bitwise_xor(own, position)
        value = loaded[0]
        for index in range(1, len(refs)):
            value = jnp.where(offset == index, loaded[index], value)
        ordered.append(value)
    return ordered


def split_fields(value, points):
    return tuple(value[f * points:(f + 1) * points] for f in range(6))


def group_kernel(here_ref, *refs):
    local_refs, out_ref = refs[:-1], refs[-1]
    points = out_ref.shape[0] // 6
    size = len(local_refs)
    here = here_ref[0]
    blocks = in_order(local_refs, jnp.bitwise_and(here, size - 1), True)
    summary = split_fields(blocks[0], points)
    for member in range(1, size):
        summary = join_coupled(summary, split_fields(blocks[member], points))
    for index, value in enumerate(summary):
        out_ref[index * points:(index + 1) * points] = value


def final_kernel(here_ref, group_ref, length_ref, energy_ref, code_ref, *refs,
                 slots, points, devices, mixed, size, groups, scale):
    local_refs = refs[:size]
    group_refs = refs[size:size + groups]
    (floor_ref, noise_ref, hop_ref, shift_ref, width_ref, dens_out_ref, bond_out_ref, theirs_ref,
     left_re_ref, left_im_ref, dens_ref, bond_ref, table_ref) = refs[size + groups:]
    build_table(floor_ref, noise_ref, hop_ref, shift_ref, width_ref, table_ref)
    here = here_ref[0]
    count = length_ref[here]
    rows = table_ref.shape[1]
    member_here = here % size
    group_here = here // size

    def into_step(block, run):
        run_re, run_im = run
        m_re, m_im = complex_mul(run_re, run_im, block[0], block[1])
        inv_re, inv_im = reciprocal(1.0 - m_re, -m_im)
        t_re, t_im = complex_mul(block[4], block[5], run_re, run_im)
        t_re, t_im = complex_mul(t_re, t_im, inv_re, inv_im)
        return (block[2] + t_re, block[3] + t_im)

    def from_step(block, run):
        run_re, run_im = run
        m_re, m_im = complex_mul(block[2], block[3], run_re, run_im)
        inv_re, inv_im = reciprocal(1.0 - m_re, -m_im)
        h_re, h_im = complex_mul(block[4], block[5], run_re, run_im)
        h_re, h_im = complex_mul(h_re, h_im, inv_re, inv_im)
        return (block[0] + h_re, block[1] + h_im)

    def masked(keep, new, old):
        return tuple(jnp.where(keep, n, o) for n, o in zip(new, old))

    zero = jnp.zeros((points,) + table_ref.shape[1:], jnp.float32)
    group_blocks = [split_fields(v, points) for v in in_order(group_refs, group_here, mixed)]
    local_blocks = [split_fields(v, points) for v in in_order(local_refs, member_here, mixed)]
    into = (zero, zero)
    for group in range(groups):
        into = masked(group < group_here, into_step(group_blocks[group], into), into)
    for member in range(size):
        into = masked(member < member_here, into_step(local_blocks[member], into), into)
    outof = (zero, zero)
    for group in reversed(range(groups)):
        outof = masked(group > group_here, from_step(group_blocks[group], outof), outof)
    for member in reversed(range(size)):
        outof = masked(member > member_here, from_step(local_blocks[member], outof), outof)
    into_re, into_im = into
    from_re, from_im = outof

    def onsite(slot):
        return onsite_terms(table_ref, energy_ref, here, count, devices, slots, points, slot)

    def forward_body(slot, carry):
        prev_re, prev_im, prev_coupling = carry
        onsite_re, onsite_im = onsite(slot)
        square = prev_coupling * prev_coupling
        denom_re, denom_im = onsite_re - square * prev_re, onsite_im - square * prev_im
        g_re, g_im = reciprocal(denom_re, denom_im)
        left_re_ref[slot] = denom_re
        left_im_ref[slot] = denom_im
        return (g_re, g_im, table_ref[slots + slot])

    ones = jnp.ones(table_ref.shape[1:], jnp.float32)
    lax.fori_loop(0, count, forward_body, (into_re, into_im, ones))
    dens_ref[...] = jnp.zeros(dens_ref.shape, jnp.float32)
    bond_ref[...] = jnp.zeros(bond_ref.shape, jnp.float32)
    weights = [code_ref[point].astype(jnp.float32) * scale for point in range(points)]

    def backward_body(step, carry):
        next_re, next_im = carry
        slot = count - 1 - step
        onsite_re, onsite_im = onsite(slot)
        denom_re, denom_im = left_re_ref[slot], left_im_ref[slot]
        coupling = table_ref[slots + slot]
        square = coupling * coupling
        diag_re, diag_im = reciprocal(denom_re - square * next_re, denom_im - square * next_im)
        _, bond_im = complex_mul(diag_re, diag_im, next_re, next_im)
        dens = weights[0] * diag_im[0]
        bond = weights[0] * (square * bond_im[0])
        for point in range(1, points):
            dens = dens + weights[point] * diag_im[point]
            bond = bond + weights[point] * (square * bond_im[point])
        dens_ref[slot] = -inv_pi * dens
        bond_ref[slot] = -2.0 * inv_pi * bond
        return reciprocal(onsite_re - square * next_re, onsite_im - square * next_im)

    lax.fori_loop(0, count, backward_body, (from_re, from_im))
    lower = group_ref[0] == 0
    half = rows // 2
    for slot in range(slots):
        dens = dens_ref[slot]
        bond = bond_ref[slot]
        for row in range(half):
            lane = row * 128
            for kind, value, mine_ref in ((0, dens, dens_out_ref), (1, bond, bond_out_ref)):
                low, high = value[row:row + 1], value[row + half:row + half + 1]
                mine_ref[slot:slot + 1, lane:lane + 128] = jnp.where(lower, low, high)
                theirs_ref[kind, slot:slot + 1, lane:lane + 128] = jnp.where(lower, high, low)


def shards(
    mode_floor, onsite_noise, hopping, lengths, energy_index, weight_code, lead_shift, lead_width
):
    slots = onsite_noise.shape[0]
    modes = onsite_noise.shape[1]
    points = energy_index.shape[0]
    rows = modes // 128
    here = lax.axis_index("slab")
    devices = lax.axis_size("slab")
    groups = lax.axis_size("energy")
    raw = (mode_floor.reshape(1, modes), onsite_noise, hopping, lead_shift, lead_width)
    table_shape = (2 * slots + 4 * points, rows, 128)
    here_arr = here.astype(jnp.int32).reshape(1)
    smem = pl.BlockSpec(memory_space=pltpu.SMEM)
    vmem = pl.BlockSpec(memory_space=pltpu.VMEM)

    packed = pl.pallas_call(
        functools.partial(summary_kernel, slots=slots, points=points, devices=devices),
        out_shape=jax.ShapeDtypeStruct((6 * points, rows, 128), jnp.float32),
        in_specs=[smem, smem, smem] + [vmem] * len(raw),
        out_specs=vmem,
        scratch_shapes=[pltpu.VMEM(table_shape, jnp.float32)],
    )(here_arr, lengths, energy_index, *raw)
    mixed = devices & (devices - 1) == 0 and devices >= 4
    if mixed:
        size = 4
        def swap(value, offset):
            return lax.ppermute(value, "slab", [(device, device ^ offset) for device in range(devices)])

        across = swap(packed, 2)
        local = [packed, swap(packed, 1), across, swap(across, 1)]
        summary = pl.pallas_call(
            group_kernel,
            out_shape=jax.ShapeDtypeStruct(packed.shape, jnp.float32),
            in_specs=[smem] + [vmem] * size,
            out_specs=vmem,
        )(here_arr, *local)
        if devices == size * size:
            every = [summary] + [
                lax.ppermute(summary, "slab", [(device, device ^ (offset * size)) for device in range(devices)])
                for offset in range(1, size)
            ]
        else:
            stacked = summary[None]
            distance = size
            while distance < devices:
                pairs = [(device, device ^ distance) for device in range(devices)]
                stacked = jnp.concatenate([stacked, lax.ppermute(stacked, "slab", pairs)], axis=0)
                distance *= 2
            every = [stacked[index] for index in range(devices // size)]
    else:
        size = devices
        gathered = lax.all_gather(packed, "slab")
        local = [gathered[index] for index in range(devices)]
        every = [jnp.zeros(packed.shape, jnp.float32)]
    half = jax.ShapeDtypeStruct((slots, modes // 2), jnp.float32)
    group_arr = lax.axis_index("energy").astype(jnp.int32).reshape(1)
    density, bond_density, theirs = pl.pallas_call(
        functools.partial(
            final_kernel, slots=slots, points=points, devices=devices, mixed=mixed,
            size=len(local), groups=len(every), scale=1.0 / (32.0 * points * groups),
        ),
        out_shape=(half, half, jax.ShapeDtypeStruct((2, slots, modes // 2), jnp.float32)),
        in_specs=[smem] * 5 + [vmem] * (len(local) + len(every) + len(raw)),
        out_specs=(vmem, vmem, vmem),
        scratch_shapes=[
            pltpu.VMEM((slots, points, rows, 128), jnp.float32),
            pltpu.VMEM((slots, points, rows, 128), jnp.float32),
            pltpu.VMEM((slots, rows, 128), jnp.float32),
            pltpu.VMEM((slots, rows, 128), jnp.float32),
            pltpu.VMEM(table_shape, jnp.float32),
        ],
    )(here_arr, group_arr, lengths, energy_index, weight_code, *local, *every, *raw)
    if groups == 2:
        theirs = lax.ppermute(theirs, "energy", [(0, 1), (1, 0)])
        return (density + theirs[0], bond_density + theirs[1])
    lower = lax.axis_index("energy") == 0
    both = jnp.stack([
        jnp.where(lower, jnp.concatenate([density, theirs[0]], axis=1), jnp.concatenate([theirs[0], density], axis=1)),
        jnp.where(lower, jnp.concatenate([bond_density, theirs[1]], axis=1), jnp.concatenate([theirs[1], bond_density], axis=1)),
    ])
    both = lax.psum_scatter(both, "energy", scatter_dimension=2, tiled=True)
    return (both[0], both[1])


def solution(mesh):
    in_specs = (
        P(),
        P("slab", None),
        P("slab", None),
        P(),
        P("energy"),
        P("energy"),
        P("energy", None, None),
        P("energy", None, None),
    )
    out_specs = (P("slab", "energy"), P("slab", "energy"))
    return jax.shard_map(shards, mesh=mesh, in_specs=in_specs, out_specs=out_specs, check_vma=False)
```

```python
import functools

import jax
import jax.numpy as jnp
from jax import lax
from jax.experimental import pallas as pl
from jax.experimental.pallas import tpu as pltpu
from jax.sharding import PartitionSpec as P

broaden = 0.002
e_low = -1.5
e_step = 3.0 / 4096.0
inv_pi = 1.0 / 3.141592653589793


def reciprocal(real_part, imag_part):
    scale = 1.0 / (real_part * real_part + imag_part * imag_part)
    return (real_part * scale, -imag_part * scale)


def complex_mul(first_re, first_im, second_re, second_im):
    return (
        first_re * second_re - first_im * second_im,
        first_re * second_im + first_im * second_re,
    )


def join_segments(left, right):
    square = left[6] * left[6]
    mix_re, mix_im = complex_mul(left[4], left[5], right[0], right[1])
    inv_re, inv_im = reciprocal(1.0 - square * mix_re, -square * mix_im)
    left_sq_re, left_sq_im = complex_mul(left[2], left[3], left[2], left[3])
    head_re, head_im = complex_mul(left_sq_re, left_sq_im, right[0], right[1])
    head_re, head_im = complex_mul(head_re, head_im, inv_re, inv_im)
    right_sq_re, right_sq_im = complex_mul(right[2], right[3], right[2], right[3])
    tail_re, tail_im = complex_mul(right_sq_re, right_sq_im, left[4], left[5])
    tail_re, tail_im = complex_mul(tail_re, tail_im, inv_re, inv_im)
    link_re, link_im = complex_mul(left[2], left[3], right[2], right[3])
    link_re, link_im = complex_mul(link_re, link_im, inv_re, inv_im)
    return (
        left[0] + square * head_re,
        left[1] + square * head_im,
        left[6] * link_re,
        left[6] * link_im,
        right[4] + square * tail_re,
        right[5] + square * tail_im,
        right[6],
    )


def onsite_terms(table_ref, energy_ref, here, count, devices, slots, points, slot):
    rows = 2 * slots
    levels = table_ref[slot]
    first_on = jnp.logical_and(here == 0, slot == 0).astype(jnp.float32)
    last_on = jnp.logical_and(here == devices - 1, slot == count - 1).astype(jnp.float32)
    onsite_re, onsite_im = [], []
    for point in range(points):
        energy = e_low + e_step * energy_ref[point].astype(jnp.float32)
        onsite_re.append(
            energy - levels
            - first_on * table_ref[rows + 2 * point]
            - last_on * table_ref[rows + 2 * point + 1]
        )
        onsite_im.append(
            broaden
            + first_on * table_ref[rows + 2 * points + 2 * point]
            + last_on * table_ref[rows + 2 * points + 2 * point + 1]
        )
    return jnp.stack(onsite_re), jnp.stack(onsite_im)


def build_table(floor_ref, noise_ref, hop_ref, shift_ref, width_ref, table_ref):
    slots = noise_ref.shape[0]
    points = shift_ref.shape[0]
    for row in range(table_ref.shape[1]):
        lanes = slice(row * 128, (row + 1) * 128)
        floor = floor_ref[0:1, lanes]
        for slot in range(slots):
            table_ref[slot, row:row + 1, :] = floor + noise_ref[slot:slot + 1, lanes]
            table_ref[slots + slot, row:row + 1, :] = hop_ref[slot:slot + 1, lanes]
        for point in range(points):
            for side in range(2):
                index = 2 * slots + 2 * point + side
                table_ref[index, row:row + 1, :] = shift_ref[point, side:side + 1, lanes]
                table_ref[index + 2 * points, row:row + 1, :] = width_ref[point, side:side + 1, lanes]


def summary_kernel(here_ref, length_ref, energy_ref, floor_ref, noise_ref, hop_ref, shift_ref, width_ref,
                   out_ref, table_ref, *, slots, points, devices):
    build_table(floor_ref, noise_ref, hop_ref, shift_ref, width_ref, table_ref)
    here = here_ref[0]
    count = length_ref[here]

    def single(slot):
        onsite_re, onsite_im = onsite_terms(
            table_ref, energy_ref, here, count, devices, slots, points, slot
        )
        g_re, g_im = reciprocal(onsite_re, onsite_im)
        coupling = table_ref[slots + slot]
        square = coupling * coupling
        sq_re, sq_im = complex_mul(g_re, g_im, g_re, g_im)
        return (g_re, g_im, square * g_re, square * g_im, square * sq_re, square * sq_im)

    def body(slot, summary):
        return join_coupled(summary, single(slot))

    summary = lax.fori_loop(1, count, body, single(0))
    for index, value in enumerate(summary):
        out_ref[index * points:(index + 1) * points] = value


def join_coupled(left, right):
    d_re, d_im = complex_mul(left[2], left[3], right[0], right[1])
    inv_re, inv_im = reciprocal(1.0 - d_re, -d_im)
    f_re, f_im = complex_mul(left[4], left[5], right[0], right[1])
    f_re, f_im = complex_mul(f_re, f_im, inv_re, inv_im)
    g_re, g_im = complex_mul(right[4], right[5], left[2], left[3])
    g_re, g_im = complex_mul(g_re, g_im, inv_re, inv_im)
    x_re, x_im = complex_mul(left[4], left[5], right[4], right[5])
    x_re, x_im = complex_mul(x_re, x_im, inv_re, inv_im)
    x_re, x_im = complex_mul(x_re, x_im, inv_re, inv_im)
    return (left[0] + f_re, left[1] + f_im, right[2] + g_re, right[3] + g_im, x_re, x_im)


def in_order(refs, own, mixed, loaded=None):
    if loaded is None:
        loaded = [ref[...] for ref in refs]
    if not mixed:
        return loaded
    ordered = []
    for position in range(len(loaded)):
        offset = jnp.bitwise_xor(own, position)
        value = loaded[0]
        for index in range(1, len(loaded)):
            value = jnp.where(offset == index, loaded[index], value)
        ordered.append(value)
    return ordered


def split_fields(value, points):
    return tuple(value[f * points:(f + 1) * points] for f in range(6))


def group_kernel(here_ref, *refs):
    local_refs, out_ref = refs[:-1], refs[-1]
    points = out_ref.shape[0] // 6
    size = len(local_refs)
    here = here_ref[0]
    blocks = in_order(local_refs, jnp.bitwise_and(here, size - 1), True)
    summary = split_fields(blocks[0], points)
    for member in range(1, size):
        summary = join_coupled(summary, split_fields(blocks[member], points))
    for index, value in enumerate(summary):
        out_ref[index * points:(index + 1) * points] = value


def final_kernel(here_ref, group_ref, length_ref, energy_ref, code_ref, *refs,
                 slots, points, devices, mixed, size, groups, scale, relay):
    local_refs = refs[:size]
    group_refs = refs[size:size + groups + 2 * relay]
    (floor_ref, noise_ref, hop_ref, shift_ref, width_ref, dens_out_ref, bond_out_ref, theirs_ref,
     left_re_ref, left_im_ref, dens_ref, bond_ref, table_ref) = refs[size + groups + 2 * relay:]
    build_table(floor_ref, noise_ref, hop_ref, shift_ref, width_ref, table_ref)
    here = here_ref[0]
    count = length_ref[here]
    rows = table_ref.shape[1]
    member_here = here % size
    group_here = here // size

    def into_step(block, run):
        run_re, run_im = run
        m_re, m_im = complex_mul(run_re, run_im, block[0], block[1])
        inv_re, inv_im = reciprocal(1.0 - m_re, -m_im)
        t_re, t_im = complex_mul(block[4], block[5], run_re, run_im)
        t_re, t_im = complex_mul(t_re, t_im, inv_re, inv_im)
        return (block[2] + t_re, block[3] + t_im)

    def from_step(block, run):
        run_re, run_im = run
        m_re, m_im = complex_mul(block[2], block[3], run_re, run_im)
        inv_re, inv_im = reciprocal(1.0 - m_re, -m_im)
        h_re, h_im = complex_mul(block[4], block[5], run_re, run_im)
        h_re, h_im = complex_mul(h_re, h_im, inv_re, inv_im)
        return (block[0] + h_re, block[1] + h_im)

    def masked(keep, new, old):
        return tuple(jnp.where(keep, n, o) for n, o in zip(new, old))

    zero = jnp.zeros((points,) + table_ref.shape[1:], jnp.float32)
    group_values = None
    if relay:
        own_g, near, far, back, swapped, swapped_far = [ref[...] for ref in group_refs]
        first_core = jnp.bitwise_and(here, 1) == 0
        group_values = [
            own_g,
            jnp.where(first_core, near, swapped),
            jnp.where(first_core, far, swapped_far),
            jnp.where(first_core, swapped, back),
        ]
    group_blocks = [
        split_fields(v, points) for v in in_order(group_refs, group_here, mixed, group_values)
    ]
    local_blocks = [split_fields(v, points) for v in in_order(local_refs, member_here, mixed)]
    into = (zero, zero)
    for group in range(groups):
        into = masked(group < group_here, into_step(group_blocks[group], into), into)
    for member in range(size):
        into = masked(member < member_here, into_step(local_blocks[member], into), into)
    outof = (zero, zero)
    for group in reversed(range(groups)):
        outof = masked(group > group_here, from_step(group_blocks[group], outof), outof)
    for member in reversed(range(size)):
        outof = masked(member > member_here, from_step(local_blocks[member], outof), outof)
    into_re, into_im = into
    from_re, from_im = outof

    def onsite(slot):
        return onsite_terms(table_ref, energy_ref, here, count, devices, slots, points, slot)

    def forward_body(slot, carry):
        prev_re, prev_im, prev_coupling = carry
        onsite_re, onsite_im = onsite(slot)
        square = prev_coupling * prev_coupling
        denom_re, denom_im = onsite_re - square * prev_re, onsite_im - square * prev_im
        g_re, g_im = reciprocal(denom_re, denom_im)
        left_re_ref[slot] = denom_re
        left_im_ref[slot] = denom_im
        return (g_re, g_im, table_ref[slots + slot])

    ones = jnp.ones(table_ref.shape[1:], jnp.float32)
    lax.fori_loop(0, count, forward_body, (into_re, into_im, ones))
    dens_ref[...] = jnp.zeros(dens_ref.shape, jnp.float32)
    bond_ref[...] = jnp.zeros(bond_ref.shape, jnp.float32)
    weights = [code_ref[point].astype(jnp.float32) * scale for point in range(points)]

    def backward_body(step, carry):
        next_re, next_im = carry
        slot = count - 1 - step
        onsite_re, onsite_im = onsite(slot)
        denom_re, denom_im = left_re_ref[slot], left_im_ref[slot]
        coupling = table_ref[slots + slot]
        square = coupling * coupling
        diag_re, diag_im = reciprocal(denom_re - square * next_re, denom_im - square * next_im)
        _, bond_im = complex_mul(diag_re, diag_im, next_re, next_im)
        dens = weights[0] * diag_im[0]
        bond = weights[0] * (square * bond_im[0])
        for point in range(1, points):
            dens = dens + weights[point] * diag_im[point]
            bond = bond + weights[point] * (square * bond_im[point])
        dens_ref[slot] = -inv_pi * dens
        bond_ref[slot] = -2.0 * inv_pi * bond
        return reciprocal(onsite_re - square * next_re, onsite_im - square * next_im)

    lax.fori_loop(0, count, backward_body, (from_re, from_im))
    lower = group_ref[0] == 0
    half = rows // 2
    for slot in range(slots):
        dens = dens_ref[slot]
        bond = bond_ref[slot]
        for row in range(half):
            lane = row * 128
            for kind, value, mine_ref in ((0, dens, dens_out_ref), (1, bond, bond_out_ref)):
                low, high = value[row:row + 1], value[row + half:row + half + 1]
                mine_ref[slot:slot + 1, lane:lane + 128] = jnp.where(lower, low, high)
                theirs_ref[kind, slot:slot + 1, lane:lane + 128] = jnp.where(lower, high, low)


def shards(
    mode_floor, onsite_noise, hopping, lengths, energy_index, weight_code, lead_shift, lead_width
):
    slots = onsite_noise.shape[0]
    modes = onsite_noise.shape[1]
    points = energy_index.shape[0]
    rows = modes // 128
    here = lax.axis_index("slab")
    devices = lax.axis_size("slab")
    groups = lax.axis_size("energy")
    raw = (mode_floor.reshape(1, modes), onsite_noise, hopping, lead_shift, lead_width)
    table_shape = (2 * slots + 4 * points, rows, 128)
    here_arr = here.astype(jnp.int32).reshape(1)
    smem = pl.BlockSpec(memory_space=pltpu.SMEM)
    vmem = pl.BlockSpec(memory_space=pltpu.VMEM)

    packed = pl.pallas_call(
        functools.partial(summary_kernel, slots=slots, points=points, devices=devices),
        out_shape=jax.ShapeDtypeStruct((6 * points, rows, 128), jnp.float32),
        in_specs=[smem, smem, smem] + [vmem] * len(raw),
        out_specs=vmem,
        scratch_shapes=[pltpu.VMEM(table_shape, jnp.float32)],
    )(here_arr, lengths, energy_index, *raw)
    mixed = devices & (devices - 1) == 0 and devices >= 4
    relay = False
    if mixed:
        size = 4
        def swap(value, offset):
            return lax.ppermute(value, "slab", [(device, device ^ offset) for device in range(devices)])

        across = swap(packed, 2)
        local = [packed, swap(packed, 1), across, swap(across, 1)]
        summary = pl.pallas_call(
            group_kernel,
            out_shape=jax.ShapeDtypeStruct(packed.shape, jnp.float32),
            in_specs=[smem] + [vmem] * size,
            out_specs=vmem,
        )(here_arr, *local)
        if devices == size * size:
            def fetch(offset, core):
                pairs = [(device, device ^ offset) for device in range(devices) if device % 2 == core]
                return lax.ppermute(summary, "slab", pairs)

            near, far, back = fetch(size, 0), fetch(2 * size, 0), fetch(3 * size, 1)
            swapped = swap(near + back, 1)
            swapped_far = swap(far, 1)
            every = [summary, near, far, back, swapped, swapped_far]
            relay = True
        else:
            stacked = summary[None]
            distance = size
            while distance < devices:
                pairs = [(device, device ^ distance) for device in range(devices)]
                stacked = jnp.concatenate([stacked, lax.ppermute(stacked, "slab", pairs)], axis=0)
                distance *= 2
            every = [stacked[index] for index in range(devices // size)]
    else:
        size = devices
        gathered = lax.all_gather(packed, "slab")
        local = [gathered[index] for index in range(devices)]
        every = [jnp.zeros(packed.shape, jnp.float32)]
    half = jax.ShapeDtypeStruct((slots, modes // 2), jnp.float32)
    group_arr = lax.axis_index("energy").astype(jnp.int32).reshape(1)
    density, bond_density, theirs = pl.pallas_call(
        functools.partial(
            final_kernel, slots=slots, points=points, devices=devices, mixed=mixed,
            size=len(local), groups=len(every) - 2 * relay, relay=relay,
            scale=1.0 / (32.0 * points * groups),
        ),
        out_shape=(half, half, jax.ShapeDtypeStruct((2, slots, modes // 2), jnp.float32)),
        in_specs=[smem] * 5 + [vmem] * (len(local) + len(every) + len(raw)),
        out_specs=(vmem, vmem, vmem),
        scratch_shapes=[
            pltpu.VMEM((slots, points, rows, 128), jnp.float32),
            pltpu.VMEM((slots, points, rows, 128), jnp.float32),
            pltpu.VMEM((slots, rows, 128), jnp.float32),
            pltpu.VMEM((slots, rows, 128), jnp.float32),
            pltpu.VMEM(table_shape, jnp.float32),
        ],
    )(here_arr, group_arr, lengths, energy_index, weight_code, *local, *every, *raw)
    if groups == 2:
        theirs = lax.ppermute(theirs, "energy", [(0, 1), (1, 0)])
        return (density + theirs[0], bond_density + theirs[1])
    lower = lax.axis_index("energy") == 0
    both = jnp.stack([
        jnp.where(lower, jnp.concatenate([density, theirs[0]], axis=1), jnp.concatenate([theirs[0], density], axis=1)),
        jnp.where(lower, jnp.concatenate([bond_density, theirs[1]], axis=1), jnp.concatenate([theirs[1], bond_density], axis=1)),
    ])
    both = lax.psum_scatter(both, "energy", scatter_dimension=2, tiled=True)
    return (both[0], both[1])


def solution(mesh):
    in_specs = (
        P(),
        P("slab", None),
        P("slab", None),
        P(),
        P("energy"),
        P("energy"),
        P("energy", None, None),
        P("energy", None, None),
    )
    out_specs = (P("slab", "energy"), P("slab", "energy"))
    return jax.shard_map(shards, mesh=mesh, in_specs=in_specs, out_specs=out_specs, check_vma=False)
```
